32 devices in a mesh: hx: 4 (over z), hy: 4 (over y, x), torso: 2 (over core).
Axes of the slice: x: 2, y: 2, z: 4, core: 2. Of those that a mesh axis runs over, the one named last changes fastest.
Arguments:
- potential: float32 [8, 52, 1024], P('torso', 'hx', 'hy'), may hold values from -4 to 4, as said below
- gating: float32 [40, 8, 52, 1024], P(None, 'torso', 'hx', 'hy'), may hold values from 0 to 1, as said below
- cell_type: int32 [8, 52, 1024], P('torso', 'hx', 'hy'), may hold values from 0 to 2, as said below
- drug_class: int32 [8, 52, 1024], P('torso', 'hx', 'hy'), may hold values from 0 to 3, as said below
- half_point: float32 [3, 40], replicated, may hold values from -3 to 3
- gate_slope: float32 [3, 40], replicated, may hold values from 1 to 4
- time_const: float32 [3, 40], replicated, may hold values from 0.003 to 0.06
- max_conduct: float32 [3, 40], replicated, may hold values from 1 to 16
- reversal: float32 [40], replicated, may hold values from -4 to 4
- drug_block: float32 [4, 40], replicated, may hold values from 0.2 to 1
- heart_cond: float32 [2, 16, 340], P('torso', 'hx', 'hy'), may hold values from 0.5 to 1.5
- torso_cond: float32 [2, 16, 340], P('torso', 'hx', 'hy'), may hold values from 0.5 to 2
- epi_target: int32 [52, 1024], P('hx', 'hy'), may hold values from 0 to 50028, as said below
Outputs:
- new_potential: float32 [8, 52, 1024], P('torso', 'hx', 'hy')
- new_gating: float32 [40, 8, 52, 1024], P(None, 'torso', 'hx', 'hy')
- torso_field: float32 [8, 52, 1024], P('torso', 'hx', 'hy')
The draws below stay inside these ranges and needn't reach their ends.
Inputs may be any that keep to these rules, and one draw needn't show every extreme that they name: `potential`: copies of a shared node hold equal values. `gating`: copies of a shared node hold equal values. `cell_type`: copies of a shared node hold equal values. `drug_class`: copies of a shared node hold equal values. `epi_target`: the node p * 1021 + q that feeds the torso surface copy at distinct coordinates (a, b) has p within 2 of a and q within 2 of b; copies of a shared node hold equal values.
All inputs are finite; a program needn't handle non-finite values.
Results may differ from the reference program's by a relative error of at most 0.0001.
Values sent between devices are 32-bit elements; how exact they have to be, the bound alone decides.
No kernel may reach another device: no remote copies, remote signals or barrier semaphores. Data moves between devices by JAX's collectives and lax.ppermute only.
A program may use at most 64 MiB of HBM per device.

```python
import math
import jax
import jax.numpy as jnp
import numpy as np
from jax import lax

STATES = 40
TYPES = 3
CLASSES = 4
STEPS = 2
ITERS = 4
REACH = 2
NDL = 4
NXL = 13
NYL = 256
TDL = 4
NDH = 8
NXH = 52
NYH = 1024
TDH = 8
EDH = 2
TEDH = 2
EXH = 16
EYH = 340
UD = 7
UX = 49
UY = 1021


def copy_index_drawn(length_all, length_local):
    position = jnp.arange(length_all)
    return position // length_local * (length_local - 1) + position % length_local


def spread_copies(distinct):
    spread = jnp.take(distinct, copy_index_drawn(NDH, NDL), axis=-3)
    spread = jnp.take(spread, copy_index_drawn(NXH, NXL), axis=-2)
    return jnp.take(spread, copy_index_drawn(NYH, NYL), axis=-1)


def draw_potential(key, part):
    distinct = jnp.clip(jax.random.normal(key, (UD, UX, UY), jnp.float32), -4.0, 4.0)
    return spread_copies(distinct)


def draw_gating(key, part):
    distinct = jax.random.uniform(key, (STATES, UD, UX, UY), jnp.float32, 0.05, 0.95)
    return spread_copies(distinct)


def draw_cell_type(key, part):
    distinct = jax.random.randint(key, (UD, UX, UY), 0, TYPES)
    return spread_copies(distinct).astype(jnp.int32)


def draw_drug_class(key, part):
    distinct = jax.random.randint(key, (UD, UX, UY), 0, CLASSES)
    return spread_copies(distinct).astype(jnp.int32)


def draw_epi_target(key, part):
    key_first, key_second = jax.random.split(key)
    row_index = jnp.arange(UX, dtype=jnp.int32)[:, None]
    col_index = jnp.arange(UY, dtype=jnp.int32)[None, :]
    move_first = jax.random.randint(key_first, (UX, UY), -REACH, REACH + 1)
    move_second = jax.random.randint(key_second, (UX, UY), -REACH, REACH + 1)
    marker = (row_index * 7 + col_index) % 61
    move_first = jnp.where(marker == 3, REACH, jnp.where(marker == 5, -REACH, move_first))
    move_second = jnp.where(marker == 3, -REACH, jnp.where(marker == 5, REACH, move_second))
    target_first = jnp.clip(row_index + move_first, 0, UX - 1)
    target_second = jnp.clip(col_index + move_second, 0, UY - 1)
    target = target_first * UY + target_second
    target = jnp.where((row_index == 0) & (col_index == 0), 0, target)
    target = jnp.where((row_index == UX - 1) & (col_index == UY - 1), UX * UY - 1, target)
    target = jnp.take(target, copy_index_drawn(NXH, NXL), axis=0)
    return jnp.take(target, copy_index_drawn(NYH, NYL), axis=1).astype(jnp.int32)


def steps_of(key, shape, cuts, smallest, top_value):
    level, own = 1.0, jax.random.fold_in(key, 6)
    for axis_at, shards_of in cuts:
        draws = jnp.exp(jax.random.uniform(jax.random.fold_in(own, axis_at), (shards_of,), jnp.float32, smallest / len(cuts), top_value / len(cuts)))
        level = level * jnp.repeat(draws, shape[axis_at] // shards_of).reshape([-1 if axis == axis_at else 1 for axis in range(len(shape))])
    return level


def normal_values(rng, shape, deviation, limit, held_as=jnp.bfloat16):
    values = jax.random.normal(rng, shape, jnp.float32) * deviation
    return jnp.minimum(jnp.maximum(values, -limit), limit).astype(held_as)


def setup_inputs(seed: int = 0) -> dict:
    splits = jax.random.split(jax.random.key(seed), 14)
    potential = draw_potential(jax.random.fold_in(splits[13], 71), 0)
    gating = draw_gating(jax.random.fold_in(splits[13], 71), 0)
    cell_type = draw_cell_type(jax.random.fold_in(splits[13], 71), 0)
    drug_class = draw_drug_class(jax.random.fold_in(splits[13], 71), 0)
    half_point = normal_values(splits[4], (TYPES, STATES), 1.0, 3.0, jnp.float32)
    gate_slope = jnp.clip(jnp.exp(jax.random.uniform(splits[5], (TYPES, STATES), jnp.float32, math.log(1.0), math.log(4.0))), 1.0, 4.0)
    time_const = jnp.clip(jnp.exp(jax.random.uniform(splits[6], (TYPES, STATES), jnp.float32, math.log(0.003), math.log(0.06))), 0.003, 0.06)
    max_conduct = jnp.clip(jnp.exp(jax.random.uniform(splits[7], (TYPES, STATES), jnp.float32, math.log(1.0), math.log(16.0))), 1.0, 16.0)
    reversal = normal_values(splits[8], (STATES,), 1.5, 4.0, jnp.float32)
    drug_block = jnp.clip(jax.random.uniform(splits[9], (CLASSES, STATES), jnp.float32, 0.2, 1.0), 0.2, 1.0)
    heart_cond = jnp.clip(jnp.exp(math.log(1.5) - 1.0986123 * jax.random.uniform(splits[10], (EDH, EXH, EYH), jnp.float32) ** steps_of(splits[10], (EDH, EXH, EYH), ((0, 2), (1, 4), (2, 4)), -0.2, 0.2)), 0.5, 1.5)
    torso_cond = jnp.clip(jnp.exp(math.log(2.0) - 1.3862944 * jax.random.uniform(splits[11], (TEDH, EXH, EYH), jnp.float32) ** steps_of(splits[11], (TEDH, EXH, EYH), ((0, 2), (1, 4), (2, 4)), -0.2, 0.2)), 0.5, 2.0)
    epi_target = draw_epi_target(jax.random.fold_in(splits[13], 71), 0)
    return dict(potential=potential, gating=gating, cell_type=cell_type, drug_class=drug_class, half_point=half_point, gate_slope=gate_slope, time_const=time_const, max_conduct=max_conduct, reversal=reversal, drug_block=drug_block, heart_cond=heart_cond, torso_cond=torso_cond, epi_target=epi_target)


STIFF_LINE = np.array([[148.0, -189.0, 54.0, -13.0], [-189.0, 432.0, -297.0, 54.0], [54.0, -297.0, 432.0, -189.0], [-13.0, 54.0, -189.0, 148.0]]) / 40.0
MASS_LINE = np.array([[128.0, 99.0, -36.0, 19.0], [99.0, 648.0, -81.0, -36.0], [-36.0, -81.0, 648.0, 99.0], [19.0, -36.0, 99.0, 128.0]]) / 1680.0
ELEMENT_MATRIX = (np.kron(np.kron(STIFF_LINE, MASS_LINE), MASS_LINE) + np.kron(np.kron(MASS_LINE, STIFF_LINE), MASS_LINE) + np.kron(np.kron(MASS_LINE, MASS_LINE), STIFF_LINE))
time_step = 0.002
torso_shift = 0.02


def pick_nodes(values, axis_place, length):
    return jnp.stack([lax.slice_in_dim(values, offset, offset + 3 * length - 2, 3, axis_place) for offset in range(4)], 0)


def place_nodes(stacked, axis_place):
    result = None
    for offset in range(4):
        slab_part = stacked[offset]
        config = [(0, 0, 0)] * slab_part.ndim
        config[axis_place] = (offset, 3 - offset, 2)
        placed = lax.pad(slab_part, jnp.zeros((), slab_part.dtype), config)
        result = placed if result is None else result + placed
    return result


def element_products(values, conduct):
    counts = conduct.shape
    picked = pick_nodes(values, 0, counts[0])
    picked = pick_nodes(picked, 2, counts[1])
    picked = pick_nodes(picked, 4, counts[2])
    matrix = jnp.asarray(ELEMENT_MATRIX, values.dtype)
    product = jnp.dot(matrix, picked.reshape(64, -1), precision=lax.Precision.HIGHEST)
    product = (product * conduct.reshape(1, -1)).reshape(picked.shape)
    spread = place_nodes(product, 4)
    spread = place_nodes(spread, 2)
    return place_nodes(spread, 0)


def to_blocks(values, blocks):
    shape = values.shape
    lengths = [shape[axis_id] // blocks[axis_id] for axis_id in range(3)]
    split = values.reshape(blocks[0], lengths[0], blocks[1], lengths[1], blocks[2], lengths[2])
    return split.transpose(0, 2, 4, 1, 3, 5).reshape(-1, lengths[0], lengths[1], lengths[2])


def from_blocks(stacked, blocks):
    lengths = stacked.shape[1:]
    split = stacked.reshape(blocks[0], blocks[1], blocks[2], lengths[0], lengths[1], lengths[2])
    return split.transpose(0, 3, 1, 4, 2, 5).reshape(blocks[0] * lengths[0], blocks[1] * lengths[1], blocks[2] * lengths[2])


def add_faces(stacked, blocks):
    grid = stacked.reshape(tuple(blocks) + stacked.shape[1:])
    for axis_id in range(3):
        moved = jnp.moveaxis(grid, (axis_id, 3 + axis_id), (0, 1))
        start_plane = moved[:, 0]
        end_plane = moved[:, -1]
        from_lower = jnp.concatenate([jnp.zeros_like(end_plane[:1]), end_plane[:-1]], 0)
        from_upper = jnp.concatenate([start_plane[1:], jnp.zeros_like(start_plane[:1])], 0)
        moved = moved.at[:, 0].add(from_lower).at[:, -1].add(from_upper)
        grid = jnp.moveaxis(moved, (0, 1), (axis_id, 3 + axis_id))
    return grid.reshape(stacked.shape)


def apply_stiffness(values, conduct, blocks):
    products = jax.vmap(element_products)(to_blocks(values, blocks), to_blocks(conduct, blocks))
    return from_blocks(add_faces(products, blocks), blocks)


def line_factors(length_all, length_local):
    position = jnp.arange(length_all)
    local_pos = position % length_local
    block_id = position // length_local
    block_count = length_all // length_local
    at_start = (local_pos == 0) & (block_id == 0)
    at_end = (local_pos == length_local - 1) & (block_id == block_count - 1)
    mass_line = jnp.where(local_pos % 3 == 0, jnp.where(at_start | at_end, 0.125, 0.25), 0.375)
    shared = ((local_pos == 0) & (block_id > 0)) | ((local_pos == length_local - 1) & (block_id < block_count - 1))
    weight = jnp.where(shared, 0.5, 1.0)
    return mass_line.astype(jnp.float32), weight.astype(jnp.float32)


def factor_grid(depth_line, first_line, second_line):
    return depth_line[:, None, None] * first_line[None, :, None] * second_line[None, None, :]


def copy_index(distinct_pos, length_local, block_count):
    block_id = jnp.minimum(distinct_pos // (length_local - 1), block_count - 1)
    return (block_id * length_local + distinct_pos - block_id * (length_local - 1)).astype(jnp.int32)


def reference(potential, gating, cell_type, drug_class, half_point, gate_slope, time_const, max_conduct, reversal, drug_block, heart_cond, torso_cond, epi_target):
    heart_blocks = (NDH // NDL, NXH // NXL, NYH // NYL)
    torso_blocks = (TDH // TDL, NXH // NXL, NYH // NYL)
    heart_depth, unused_depth = line_factors(NDH, NDL)
    first_mass, first_weight = line_factors(NXH, NXL)
    second_mass, second_weight = line_factors(NYH, NYL)
    torso_depth, torso_depth_weight = line_factors(TDH, TDL)
    heart_mass = factor_grid(heart_depth, first_mass, second_mass)
    torso_mass = factor_grid(torso_depth, first_mass, second_mass)
    torso_weight = factor_grid(torso_depth_weight, first_weight, second_weight)

    for repeat in range(STEPS):
        volts = potential

        def one_state(current, slices):
            gate_now, half_row, slope_row, tau_row, conduct_row, block_row, reversal_value = slices
            half_nodes = jnp.take(half_row, cell_type)
            slope_nodes = jnp.take(slope_row, cell_type)
            tau_nodes = jnp.take(tau_row, cell_type)
            cond_nodes = jnp.take(conduct_row, cell_type) * jnp.take(block_row, drug_class)
            inf_value = jax.nn.sigmoid((volts - half_nodes) * slope_nodes)
            gate_next = inf_value + (gate_now - inf_value) * jnp.exp(-time_step / tau_nodes)
            current = current + cond_nodes * gate_next * (volts - reversal_value)
            return current, gate_next

        current, gating = lax.scan(one_state, jnp.zeros_like(volts), (gating, half_point.T, gate_slope.T, time_const.T, max_conduct.T, drug_block.T, reversal))
        diffusion = apply_stiffness(volts, heart_cond, heart_blocks)
        potential = volts - time_step * (diffusion / heart_mass + current)

    target_first = epi_target // UY
    target_second = epi_target % UY
    copy_first = copy_index(target_first, NXL, NXH // NXL)
    copy_second = copy_index(target_second, NYL, NYH // NYL)
    surface_values = potential[0][copy_first, copy_second]
    rhs = jnp.zeros((TDH, NXH, NYH), jnp.float32).at[0].set(surface_values)

    def torso_apply(values):
        return apply_stiffness(values, torso_cond, torso_blocks) + torso_shift * torso_mass * values

    solution = jnp.zeros_like(rhs)
    residual = rhs
    direction = rhs
    norm_now = jnp.sum(torso_weight * residual * residual)
    for iteration in range(ITERS):
        image = torso_apply(direction)
        step_size = norm_now / jnp.sum(torso_weight * direction * image)
        solution = solution + step_size * direction
        residual = residual - step_size * image
        norm_next = jnp.sum(torso_weight * residual * residual)
        direction = residual + (norm_next / norm_now) * direction
        norm_now = norm_next
    return potential, gating, solution
```

```python
import jax
import jax.numpy as jnp
import numpy as np
from jax import lax
from jax.sharding import PartitionSpec as P

TYPES = 3
CLASSES = 4
STEPS = 2
ITERS = 4
REACH = 2


STIFF_LINE = (
    np.array(
        [
            [148.0, -189.0, 54.0, -13.0],
            [-189.0, 432.0, -297.0, 54.0],
            [54.0, -297.0, 432.0, -189.0],
            [-13.0, 54.0, -189.0, 148.0],
        ]
    )
    / 40.0
)
MASS_LINE = (
    np.array(
        [
            [128.0, 99.0, -36.0, 19.0],
            [99.0, 648.0, -81.0, -36.0],
            [-36.0, -81.0, 648.0, 99.0],
            [19.0, -36.0, 99.0, 128.0],
        ]
    )
    / 1680.0
)
ELEMENT_MATRIX = (
    np.kron(np.kron(STIFF_LINE, MASS_LINE), MASS_LINE)
    + np.kron(np.kron(MASS_LINE, STIFF_LINE), MASS_LINE)
    + np.kron(np.kron(MASS_LINE, MASS_LINE), STIFF_LINE)
)
time_step = 0.002
torso_shift = 0.02


def extended_2(cells, sides, width):
    for axis, dim in sides:
        count = lax.axis_size(axis)
        ends = count - 1
        head = lax.slice_in_dim(cells, 0, width, axis=dim)
        tail = lax.slice_in_dim(cells, cells.shape[dim] - width, cells.shape[dim], axis=dim)
        cells = jnp.concatenate(
            [
                lax.ppermute(tail, axis, [(i, (i + 1) % count) for i in range(ends)]),
                cells,
                lax.ppermute(head, axis, [((i + 1) % count, i) for i in range(ends)]),
            ],
            axis=dim,
        )
    return cells


def all_sum(value):
    axes = ("hx", "hy", "torso")
    count = 1
    for axis in axes:
        count *= lax.axis_size(axis)
    parts = lax.all_to_all(jnp.broadcast_to(value, (count, 1)), axes, 0, 0, tiled=True)
    return jnp.sum(parts)


def pick_nodes(values, axis_place, length):
    return jnp.stack(
        [
            lax.slice_in_dim(values, offset, offset + 3 * length - 2, 3, axis_place)
            for offset in range(4)
        ],
        0,
    )


def place_nodes(stacked, axis_place):
    result = None
    for offset in range(4):
        slab_part = stacked[offset]
        config = [(0, 0, 0)] * slab_part.ndim
        config[axis_place] = (offset, 3 - offset, 2)
        placed = lax.pad(slab_part, jnp.zeros((), slab_part.dtype), config)
        result = placed if result is None else result + placed
    return result


def element_products(values, conduct):
    counts = conduct.shape
    picked = pick_nodes(values, 0, counts[0])
    picked = pick_nodes(picked, 2, counts[1])
    picked = pick_nodes(picked, 4, counts[2])
    matrix = jnp.asarray(ELEMENT_MATRIX, values.dtype)
    product = jnp.dot(matrix, picked.reshape(64, -1), precision=lax.Precision.HIGHEST)
    product = (product * conduct.reshape(1, -1)).reshape(picked.shape)
    spread = place_nodes(product, 4)
    spread = place_nodes(spread, 2)
    return place_nodes(spread, 0)


def add_faces(local_sums):
    extended = extended_2(local_sums, (("hx", 1), ("hy", 2), ("torso", 0)), 1)
    summed = extended[1:-1].at[0].add(extended[0]).at[-1].add(extended[-1])
    summed = summed[:, 1:-1].at[:, 0].add(summed[:, 0]).at[:, -1].add(summed[:, -1])
    summed = summed[:, :, 1:-1].at[:, :, 0].add(summed[:, :, 0]).at[:, :, -1].add(summed[:, :, -1])
    return summed


def line_factors(length, block_id, block_count):
    position = jnp.arange(length)
    at_start = (position == 0) & (block_id == 0)
    at_end = (position == length - 1) & (block_id == block_count - 1)
    mass_line = jnp.where(position % 3 == 0, jnp.where(at_start | at_end, 0.125, 0.25), 0.375)
    shared = (position == 0) & (block_id > 0) | (position == length - 1) & (
        block_id < block_count - 1
    )
    weight = jnp.where(shared, 0.5, 1.0)
    return (mass_line.astype(jnp.float32), weight.astype(jnp.float32))


def factor_grid(depth_line, first_line, second_line):
    return depth_line[:, None, None] * first_line[None, :, None] * second_line[None, None, :]


def node_table(matrix, labels, kind_count):
    onehot = (
        labels.reshape(1, -1) == jnp.arange(kind_count, dtype=jnp.int32).reshape(-1, 1)
    ).astype(jnp.float32)
    return jnp.dot(matrix.T, onehot, precision=lax.Precision.HIGHEST)


def ext_index(target, anchor, length_local, rim_width):
    relative = target - anchor
    return jnp.where(
        relative < 0,
        rim_width - 1 + relative,
        jnp.where(relative > length_local - 1, rim_width + relative + 1, rim_width + relative),
    )


def per_device(
    potential,
    gating,
    cell_type,
    drug_class,
    half_point,
    gate_slope,
    time_const,
    max_conduct,
    reversal,
    drug_block,
    heart_cond,
    torso_cond,
    epi_target,
):
    depth_len, first_len, second_len = potential.shape
    torso_len = 3 * torso_cond.shape[0] + 1
    index_torso = lax.axis_index("torso")
    index_first = lax.axis_index("hx")
    index_second = lax.axis_index("hy")
    heart_depth, unused_depth = line_factors(depth_len, index_torso, lax.axis_size("torso"))
    first_mass, first_weight = line_factors(first_len, index_first, lax.axis_size("hx"))
    second_mass, second_weight = line_factors(second_len, index_second, lax.axis_size("hy"))
    torso_depth, torso_depth_weight = line_factors(torso_len, index_torso, lax.axis_size("torso"))
    heart_mass = factor_grid(heart_depth, first_mass, second_mass)
    torso_mass = factor_grid(torso_depth, first_mass, second_mass)
    torso_weight = factor_grid(torso_depth_weight, first_weight, second_weight)
    type_flat = cell_type.reshape(-1)
    half_nodes = node_table(half_point, type_flat, TYPES)
    slope_nodes = node_table(gate_slope, type_flat, TYPES)
    decay_nodes = jnp.exp(-time_step / node_table(time_const, type_flat, TYPES))
    cond_nodes = node_table(max_conduct, type_flat, TYPES) * node_table(
        drug_block, drug_class.reshape(-1), CLASSES
    )
    gate_flat = gating.reshape(gating.shape[0], -1)
    for repeat in range(STEPS):
        volts = potential.reshape(1, -1)
        inf_value = jax.nn.sigmoid((volts - half_nodes) * slope_nodes)
        gate_flat = inf_value + (gate_flat - inf_value) * decay_nodes
        current = jnp.sum(cond_nodes * gate_flat * (volts - reversal[:, None]), 0)
        diffusion = add_faces(element_products(potential, heart_cond))
        potential = potential - time_step * (
            diffusion / heart_mass + current.reshape(potential.shape)
        )
    new_gating = gate_flat.reshape(gating.shape)
    rim_width = REACH + 1
    extended = extended_2(potential[0], (("hx", 0), ("hy", 1)), rim_width)
    distinct_second = lax.axis_size("hy") * (second_len - 1) + 1
    target_first = epi_target // distinct_second
    target_second = epi_target % distinct_second
    place_first = ext_index(target_first, index_first * (first_len - 1), first_len, rim_width)
    place_second = ext_index(target_second, index_second * (second_len - 1), second_len, rim_width)
    flat_place = (place_first * (second_len + 2 * rim_width) + place_second).reshape(-1)
    picked_values = jnp.take(extended.reshape(-1), flat_place).reshape(first_len, second_len)
    plane = jnp.where(index_torso == 0, picked_values, 0.0)
    rhs = jnp.concatenate(
        [plane[None], jnp.zeros((torso_len - 1, first_len, second_len), jnp.float32)], 0
    )

    def torso_apply(values):
        return add_faces(element_products(values, torso_cond)) + torso_shift * torso_mass * values

    def squares(vector):
        return all_sum(jnp.sum(torso_weight * vector * vector))

    def standard_turn(turn_index, state_tuple):
        solution, residual, direction, norm_now = state_tuple
        image = torso_apply(direction)
        curvature = all_sum(jnp.sum(torso_weight * direction * image))
        step_size = norm_now / curvature
        solution = solution + step_size * direction
        residual = residual - step_size * image
        norm_next = squares(residual)
        direction = residual + norm_next / norm_now * direction
        return (solution, residual, direction, norm_next)

    start_state = (jnp.zeros_like(rhs), rhs, rhs, squares(rhs))
    solution = lax.fori_loop(0, ITERS, standard_turn, start_state)[0]
    return (potential, new_gating, solution)


def solution(mesh):
    placed = (
        P("torso", "hx", "hy"),
        P(None, "torso", "hx", "hy"),
        P("torso", "hx", "hy"),
        P("torso", "hx", "hy"),
        P(),
        P(),
        P(),
        P(),
        P(),
        P(),
        P("torso", "hx", "hy"),
        P("torso", "hx", "hy"),
        P("hx", "hy"),
    )
    return jax.shard_map(
        per_device,
        mesh=mesh,
        in_specs=placed,
        out_specs=(P("torso", "hx", "hy"), P(None, "torso", "hx", "hy"), P("torso", "hx", "hy")),
        check_vma=False,
    )
```

```python
import jax
import jax.numpy as jnp
import numpy as np
from jax import lax
from jax.sharding import PartitionSpec as P

TYPES = 3
CLASSES = 4
STEPS = 2
ITERS = 4
REACH = 2


STIFF_LINE = (
    np.array(
        [
            [148.0, -189.0, 54.0, -13.0],
            [-189.0, 432.0, -297.0, 54.0],
            [54.0, -297.0, 432.0, -189.0],
            [-13.0, 54.0, -189.0, 148.0],
        ]
    )
    / 40.0
)
MASS_LINE = (
    np.array(
        [
            [128.0, 99.0, -36.0, 19.0],
            [99.0, 648.0, -81.0, -36.0],
            [-36.0, -81.0, 648.0, 99.0],
            [19.0, -36.0, 99.0, 128.0],
        ]
    )
    / 1680.0
)
time_step = 0.002
torso_shift = 0.02
HIGH = lax.Precision.HIGHEST


def gather_matrix(length, line):
    elements = (length - 1) // 3
    out = np.zeros((length, 4, elements))
    for e in range(elements):
        for a in range(4):
            out[3 * e : 3 * e + 4, a, e] = line[a, :]
    return out.reshape(length, 4 * elements)


def local_products(values, conduct):
    depth, first, second = values.shape
    first_el, second_el = conduct.shape[1], conduct.shape[2]
    mass_d = [[float(MASS_LINE[i, j]) for j in range(4)] for i in range(4)]
    stiff_d = [[float(STIFF_LINE[i, j]) for j in range(4)] for i in range(4)]
    rows = [values[j] for j in range(depth)]
    v_mass = jnp.stack([sum(mass_d[i][j] * rows[j] for j in range(4)) for i in range(4)])
    v_stiff = jnp.stack([sum(stiff_d[i][j] * rows[j] for j in range(4)) for i in range(4)])
    pick_mass = jnp.asarray(gather_matrix(first, MASS_LINE).T, jnp.float32)
    pick_stiff = jnp.asarray(gather_matrix(first, STIFF_LINE).T, jnp.float32)
    along_first_m = jnp.einsum("kx,dxy->dky", pick_mass, v_mass, precision=HIGH)
    along_first_k = jnp.einsum("kx,dxy->dky", pick_stiff, v_mass, precision=HIGH) + jnp.einsum(
        "kx,dxy->dky", pick_mass, v_stiff, precision=HIGH
    )
    lanes_m = jnp.asarray(gather_matrix(second, MASS_LINE), jnp.float32)
    lanes_k = jnp.asarray(gather_matrix(second, STIFF_LINE), jnp.float32)
    flat_m = along_first_m.reshape(-1, second)
    flat_k = along_first_k.reshape(-1, second)
    element = jnp.dot(flat_m, lanes_k, precision=HIGH) + jnp.dot(flat_k, lanes_m, precision=HIGH)
    element = element.reshape(depth, 4, first_el, 4, second_el) * conduct.reshape(
        1, 1, first_el, 1, second_el
    )
    scatter_second = jnp.asarray(gather_matrix(second, np.eye(4)).T, jnp.float32)
    spread = jnp.dot(element.reshape(-1, 4 * second_el), scatter_second, precision=HIGH)
    spread = spread.reshape(depth, 4 * first_el, second)
    scatter_first = jnp.asarray(gather_matrix(first, np.eye(4)), jnp.float32)
    return jnp.einsum("xk,dky->dxy", scatter_first, spread, precision=HIGH)


def torso_stage(values, scalars):
    count = lax.axis_size("torso")
    if count == 1:
        return values, scalars
    if count != 2:
        raise NotImplementedError("torso size")
    me = lax.axis_index("torso")
    face = jnp.where(me == 0, values[-1], values[0])
    extra = None
    if scalars is not None:
        extra = jnp.zeros((1, values.shape[2]), values.dtype).at[0, : scalars.shape[0]].set(scalars)
        face = jnp.concatenate([face, extra], 0)
    got = lax.ppermute(face, "torso", [(0, 1), (1, 0)])
    rows = values.shape[1]
    got_face = got[:rows]
    values = values.at[-1].add(jnp.where(me == 0, got_face, 0.0))
    values = values.at[0].add(jnp.where(me == 1, got_face, 0.0))
    if scalars is not None:
        scalars = scalars + got[rows, : scalars.shape[0]]
    return values, scalars


def plane_exchange(pieces, width, scalars):
    count_x, count_y = lax.axis_size("hx"), lax.axis_size("hy")
    me_x, me_y = lax.axis_index("hx"), lax.axis_index("hy")
    rows = []
    for code in range(9):
        offset = (code // 3 - 1, code % 3 - 1)
        piece = pieces.get(offset)
        row = jnp.zeros((width,), jnp.float32) if piece is None else jnp.pad(piece, (0, width - piece.shape[0]))
        if scalars is not None:
            row = jnp.concatenate([row, scalars])
        rows.append(row)
    table = jnp.stack(rows)
    peers = jnp.arange(count_x * count_y, dtype=jnp.int32)
    off_x = peers // count_y - me_x
    off_y = peers % count_y - me_y
    near = (jnp.abs(off_x) <= 1) & (jnp.abs(off_y) <= 1)
    code_of = jnp.where(near, (off_x + 1) * 3 + (off_y + 1), 4)
    send = jnp.take(table, code_of, axis=0)
    got = lax.all_to_all(send, ("hx", "hy"), 0, 0, tiled=True)
    received = {}
    for offset in pieces:
        src_x, src_y = me_x + offset[0], me_y + offset[1]
        valid = (src_x >= 0) & (src_x < count_x) & (src_y >= 0) & (src_y < count_y)
        src = jnp.clip(src_x, 0, count_x - 1) * count_y + jnp.clip(src_y, 0, count_y - 1)
        row = lax.dynamic_index_in_dim(got, src, 0, keepdims=False)
        received[offset] = jnp.where(valid, row[: pieces[offset].shape[0]], 0.0)
    total = None
    if scalars is not None:
        total = jnp.sum(got[:, width:], axis=0)
    return received, total


def face_sums(values, scalars=None):
    values, scalars = torso_stage(values, scalars)
    depth, first, second = values.shape
    pieces = {
        (1, 0): values[:, -1, :].reshape(-1),
        (-1, 0): values[:, 0, :].reshape(-1),
        (0, 1): values[:, :, -1].reshape(-1),
        (0, -1): values[:, :, 0].reshape(-1),
        (1, 1): values[:, -1, -1],
        (1, -1): values[:, -1, 0],
        (-1, 1): values[:, 0, -1],
        (-1, -1): values[:, 0, 0],
    }
    got, total = plane_exchange(pieces, depth * second, scalars)
    low_second = got[(0, -1)].reshape(depth, first)
    low_second = low_second.at[:, 0].add(got[(-1, -1)]).at[:, -1].add(got[(1, -1)])
    high_second = got[(0, 1)].reshape(depth, first)
    high_second = high_second.at[:, 0].add(got[(-1, 1)]).at[:, -1].add(got[(1, 1)])
    values = values.at[:, 0, :].add(got[(-1, 0)].reshape(depth, second))
    values = values.at[:, -1, :].add(got[(1, 0)].reshape(depth, second))
    values = values.at[:, :, 0].add(low_second).at[:, :, -1].add(high_second)
    return values, total


def rim_plane(plane, rim):
    first, second = plane.shape
    pieces = {
        (1, 0): plane[-rim:, :].reshape(-1),
        (-1, 0): plane[:rim, :].reshape(-1),
        (0, 1): plane[:, -rim:].reshape(-1),
        (0, -1): plane[:, :rim].reshape(-1),
        (1, 1): plane[-rim:, -rim:].reshape(-1),
        (1, -1): plane[-rim:, :rim].reshape(-1),
        (-1, 1): plane[:rim, -rim:].reshape(-1),
        (-1, -1): plane[:rim, :rim].reshape(-1),
    }
    got, _ = plane_exchange(pieces, rim * second, None)
    top = jnp.concatenate(
        [got[(-1, -1)].reshape(rim, rim), got[(-1, 0)].reshape(rim, second), got[(-1, 1)].reshape(rim, rim)], 1
    )
    middle = jnp.concatenate(
        [got[(0, -1)].reshape(first, rim), plane, got[(0, 1)].reshape(first, rim)], 1
    )
    bottom = jnp.concatenate(
        [got[(1, -1)].reshape(rim, rim), got[(1, 0)].reshape(rim, second), got[(1, 1)].reshape(rim, rim)], 1
    )
    return jnp.concatenate([top, middle, bottom], 0)


def line_factors(length, block_id, block_count):
    position = jnp.arange(length)
    at_start = (position == 0) & (block_id == 0)
    at_end = (position == length - 1) & (block_id == block_count - 1)
    mass_line = jnp.where(position % 3 == 0, jnp.where(at_start | at_end, 0.125, 0.25), 0.375)
    shared = (position == 0) & (block_id > 0) | (position == length - 1) & (
        block_id < block_count - 1
    )
    weight = jnp.where(shared, 0.5, 1.0)
    return (mass_line.astype(jnp.float32), weight.astype(jnp.float32))


def factor_grid(depth_line, first_line, second_line):
    return depth_line[:, None, None] * first_line[None, :, None] * second_line[None, None, :]


def node_table(matrix, labels, kind_count):
    onehot = (
        labels.reshape(1, -1) == jnp.arange(kind_count, dtype=jnp.int32).reshape(-1, 1)
    ).astype(jnp.float32)
    return jnp.dot(matrix.T, onehot, precision=HIGH)


def ext_index(target, anchor, length_local, rim_width):
    relative = target - anchor
    return jnp.where(
        relative < 0,
        rim_width - 1 + relative,
        jnp.where(relative > length_local - 1, rim_width + relative + 1, rim_width + relative),
    )


def per_device(
    potential,
    gating,
    cell_type,
    drug_class,
    half_point,
    gate_slope,
    time_const,
    max_conduct,
    reversal,
    drug_block,
    heart_cond,
    torso_cond,
    epi_target,
):
    depth_len, first_len, second_len = potential.shape
    torso_len = 3 * torso_cond.shape[0] + 1
    index_torso = lax.axis_index("torso")
    index_first = lax.axis_index("hx")
    index_second = lax.axis_index("hy")
    heart_depth, unused_depth = line_factors(depth_len, index_torso, lax.axis_size("torso"))
    first_mass, first_weight = line_factors(first_len, index_first, lax.axis_size("hx"))
    second_mass, second_weight = line_factors(second_len, index_second, lax.axis_size("hy"))
    torso_depth, torso_depth_weight = line_factors(torso_len, index_torso, lax.axis_size("torso"))
    heart_mass = factor_grid(heart_depth, first_mass, second_mass)
    torso_mass = factor_grid(torso_depth, first_mass, second_mass)
    torso_weight = factor_grid(torso_depth_weight, first_weight, second_weight)
    type_flat = cell_type.reshape(-1)
    half_nodes = node_table(half_point, type_flat, TYPES)
    slope_nodes = node_table(gate_slope, type_flat, TYPES)
    decay_nodes = jnp.exp(-time_step / node_table(time_const, type_flat, TYPES))
    cond_nodes = node_table(max_conduct, type_flat, TYPES) * node_table(
        drug_block, drug_class.reshape(-1), CLASSES
    )
    gate_flat = gating.reshape(gating.shape[0], -1)
    for repeat in range(STEPS):
        volts = potential.reshape(1, -1)
        inf_value = jax.nn.sigmoid((volts - half_nodes) * slope_nodes)
        gate_flat = inf_value + (gate_flat - inf_value) * decay_nodes
        current = jnp.sum(cond_nodes * gate_flat * (volts - reversal[:, None]), 0)
        diffusion, _ = face_sums(local_products(potential, heart_cond))
        potential = potential - time_step * (
            diffusion / heart_mass + current.reshape(potential.shape)
        )
    new_gating = gate_flat.reshape(gating.shape)

    rim_width = REACH + 1
    extended = rim_plane(potential[0], rim_width)
    distinct_second = lax.axis_size("hy") * (second_len - 1) + 1
    target_first = epi_target // distinct_second
    target_second = epi_target % distinct_second
    place_first = ext_index(target_first, index_first * (first_len - 1), first_len, rim_width)
    place_second = ext_index(target_second, index_second * (second_len - 1), second_len, rim_width)
    shift_first = place_first - rim_width - jnp.arange(first_len)[:, None]
    shift_second = place_second - rim_width - jnp.arange(second_len)[None, :]
    picked_values = jnp.zeros((first_len, second_len), jnp.float32)
    for step_first in range(-rim_width, rim_width + 1):
        rows = extended[rim_width + step_first : rim_width + step_first + first_len]
        along = jnp.zeros((first_len, second_len), jnp.float32)
        for step_second in range(-rim_width, rim_width + 1):
            window = rows[:, rim_width + step_second : rim_width + step_second + second_len]
            along = jnp.where(shift_second == step_second, window, along)
        picked_values = jnp.where(shift_first == step_first, along, picked_values)
    plane = jnp.where(index_torso == 0, picked_values, 0.0)
    rhs = jnp.concatenate(
        [plane[None], jnp.zeros((torso_len - 1, first_len, second_len), jnp.float32)], 0
    )

    mass_shift = torso_shift * torso_mass
    weighted_mass = torso_weight * mass_shift

    def exchange(residual, extra):
        local = local_products(residual, torso_cond)
        partial = jnp.stack(
            [
                jnp.sum(torso_weight * residual * residual),
                jnp.sum(residual * local) + jnp.sum(weighted_mass * residual * residual),
            ]
            + extra(local)
        )
        summed, sums = face_sums(local, partial)
        return summed + mass_shift * residual, sums

    image, sums = exchange(rhs, lambda local: [])
    norm_now = sums[0]
    curvature = sums[1]
    step_size = norm_now / curvature
    solution = step_size * rhs
    direction = rhs
    residual = rhs - step_size * image

    def later_turn(turn_index, state_tuple):
        solution, residual, direction, image, norm_now, curvature = state_tuple
        s_image, sums = exchange(
            residual,
            lambda local: [
                jnp.sum(torso_weight * residual * image),
                jnp.sum(direction * local) + jnp.sum(weighted_mass * direction * residual),
            ],
        )
        norm_next = sums[0]
        ratio = norm_next / norm_now
        curvature = sums[1] + ratio * (sums[2] + sums[3]) + ratio * ratio * curvature
        direction = residual + ratio * direction
        image = s_image + ratio * image
        step_size = norm_next / curvature
        solution = solution + step_size * direction
        residual = residual - step_size * image
        return (solution, residual, direction, image, norm_next, curvature)

    state = (solution, residual, direction, image, norm_now, curvature)
    solution = lax.fori_loop(1, ITERS, later_turn, state)[0]
    return (potential, new_gating, solution)


def solution(mesh):
    placed = (
        P("torso", "hx", "hy"),
        P(None, "torso", "hx", "hy"),
        P("torso", "hx", "hy"),
        P("torso", "hx", "hy"),
        P(),
        P(),
        P(),
        P(),
        P(),
        P(),
        P("torso", "hx", "hy"),
        P("torso", "hx", "hy"),
        P("hx", "hy"),
    )
    return jax.shard_map(
        per_device,
        mesh=mesh,
        in_specs=placed,
        out_specs=(P("torso", "hx", "hy"), P(None, "torso", "hx", "hy"), P("torso", "hx", "hy")),
        check_vma=False,
    )
```

```python
import jax
import jax.numpy as jnp
import numpy as np
from jax import lax
from jax.sharding import PartitionSpec as P

TYPES = 3
CLASSES = 4
STEPS = 2
ITERS = 4
REACH = 2


STIFF_LINE = (
    np.array(
        [
            [148.0, -189.0, 54.0, -13.0],
            [-189.0, 432.0, -297.0, 54.0],
            [54.0, -297.0, 432.0, -189.0],
            [-13.0, 54.0, -189.0, 148.0],
        ]
    )
    / 40.0
)
MASS_LINE = (
    np.array(
        [
            [128.0, 99.0, -36.0, 19.0],
            [99.0, 648.0, -81.0, -36.0],
            [-36.0, -81.0, 648.0, 99.0],
            [19.0, -36.0, 99.0, 128.0],
        ]
    )
    / 1680.0
)
time_step = 0.002
torso_shift = 0.02
HIGH = lax.Precision.HIGHEST


def gather_matrix(length, line):
    elements = (length - 1) // 3
    shape = (length, 4, elements)
    node = lax.broadcasted_iota(jnp.int32, shape, 0)
    offset = lax.broadcasted_iota(jnp.int32, shape, 1)
    local = node - 3 * lax.broadcasted_iota(jnp.int32, shape, 2)
    out = jnp.zeros(shape, jnp.float32)
    for a in range(4):
        for j in range(4):
            if line[a, j] != 0.0:
                out = jnp.where((offset == a) & (local == j), jnp.float32(line[a, j]), out)
    return out.reshape(length, 4 * elements)


def local_products(values, conduct):
    depth, first, second = values.shape
    first_el, second_el = conduct.shape[1], conduct.shape[2]
    mass_d = [[float(MASS_LINE[i, j]) for j in range(4)] for i in range(4)]
    stiff_d = [[float(STIFF_LINE[i, j]) for j in range(4)] for i in range(4)]
    rows = [values[j] for j in range(depth)]
    v_mass = jnp.stack([sum(mass_d[i][j] * rows[j] for j in range(4)) for i in range(4)])
    v_stiff = jnp.stack([sum(stiff_d[i][j] * rows[j] for j in range(4)) for i in range(4)])
    pick_mass = gather_matrix(first, MASS_LINE).T
    pick_stiff = gather_matrix(first, STIFF_LINE).T
    along_first_m = jnp.einsum("kx,dxy->dky", pick_mass, v_mass, precision=HIGH)
    along_first_k = jnp.einsum("kx,dxy->dky", pick_stiff, v_mass, precision=HIGH) + jnp.einsum(
        "kx,dxy->dky", pick_mass, v_stiff, precision=HIGH
    )
    lanes_m = gather_matrix(second, MASS_LINE)
    lanes_k = gather_matrix(second, STIFF_LINE)
    flat_m = along_first_m.reshape(-1, second)
    flat_k = along_first_k.reshape(-1, second)
    element = jnp.dot(flat_m, lanes_k, precision=HIGH) + jnp.dot(flat_k, lanes_m, precision=HIGH)
    element = element.reshape(depth, 4, first_el, 4, second_el) * conduct.reshape(
        1, 1, first_el, 1, second_el
    )
    scatter_second = gather_matrix(second, np.eye(4)).T
    spread = jnp.dot(element.reshape(-1, 4 * second_el), scatter_second, precision=HIGH)
    spread = spread.reshape(depth, 4 * first_el, second)
    scatter_first = gather_matrix(first, np.eye(4))
    return jnp.einsum("xk,dky->dxy", scatter_first, spread, precision=HIGH)


def torso_stage(values, scalars):
    count = lax.axis_size("torso")
    if count == 1:
        return values, scalars
    if count != 2:
        raise NotImplementedError("torso size")
    me = lax.axis_index("torso")
    face = jnp.where(me == 0, values[-1], values[0])
    extra = None
    if scalars is not None:
        extra = jnp.zeros((1, values.shape[2]), values.dtype).at[0, : scalars.shape[0]].set(scalars)
        face = jnp.concatenate([face, extra], 0)
    got = lax.ppermute(face, "torso", [(0, 1), (1, 0)])
    rows = values.shape[1]
    got_face = got[:rows]
    values = values.at[-1].add(jnp.where(me == 0, got_face, 0.0))
    values = values.at[0].add(jnp.where(me == 1, got_face, 0.0))
    if scalars is not None:
        scalars = scalars + got[rows, : scalars.shape[0]]
    return values, scalars


def plane_exchange(pieces, width, scalars):
    count_x, count_y = lax.axis_size("hx"), lax.axis_size("hy")
    me_x, me_y = lax.axis_index("hx"), lax.axis_index("hy")
    rows = []
    for code in range(9):
        offset = (code // 3 - 1, code % 3 - 1)
        piece = pieces.get(offset)
        row = jnp.zeros((width,), jnp.float32) if piece is None else jnp.pad(piece, (0, width - piece.shape[0]))
        if scalars is not None:
            row = jnp.concatenate([row, scalars])
        rows.append(row)
    table = jnp.stack(rows)
    peers = jnp.arange(count_x * count_y, dtype=jnp.int32)
    off_x = peers // count_y - me_x
    off_y = peers % count_y - me_y
    near = (jnp.abs(off_x) <= 1) & (jnp.abs(off_y) <= 1)
    code_of = jnp.where(near, (off_x + 1) * 3 + (off_y + 1), 4)
    send = jnp.take(table, code_of, axis=0)
    got = lax.all_to_all(send, ("hx", "hy"), 0, 0, tiled=True)
    received = {}
    for offset in pieces:
        src_x, src_y = me_x + offset[0], me_y + offset[1]
        valid = (src_x >= 0) & (src_x < count_x) & (src_y >= 0) & (src_y < count_y)
        src = jnp.clip(src_x, 0, count_x - 1) * count_y + jnp.clip(src_y, 0, count_y - 1)
        row = lax.dynamic_index_in_dim(got, src, 0, keepdims=False)
        received[offset] = jnp.where(valid, row[: pieces[offset].shape[0]], 0.0)
    total = None
    if scalars is not None:
        total = jnp.sum(got[:, width:], axis=0)
    return received, total


def face_sums(values, scalars=None):
    values, scalars = torso_stage(values, scalars)
    depth, first, second = values.shape
    pieces = {
        (1, 0): values[:, -1, :].reshape(-1),
        (-1, 0): values[:, 0, :].reshape(-1),
        (0, 1): values[:, :, -1].reshape(-1),
        (0, -1): values[:, :, 0].reshape(-1),
        (1, 1): values[:, -1, -1],
        (1, -1): values[:, -1, 0],
        (-1, 1): values[:, 0, -1],
        (-1, -1): values[:, 0, 0],
    }
    got, total = plane_exchange(pieces, depth * second, scalars)
    low_second = got[(0, -1)].reshape(depth, first)
    low_second = low_second.at[:, 0].add(got[(-1, -1)]).at[:, -1].add(got[(1, -1)])
    high_second = got[(0, 1)].reshape(depth, first)
    high_second = high_second.at[:, 0].add(got[(-1, 1)]).at[:, -1].add(got[(1, 1)])
    values = values.at[:, 0, :].add(got[(-1, 0)].reshape(depth, second))
    values = values.at[:, -1, :].add(got[(1, 0)].reshape(depth, second))
    values = values.at[:, :, 0].add(low_second).at[:, :, -1].add(high_second)
    return values, total


def rim_plane(plane, rim):
    first, second = plane.shape
    pieces = {
        (1, 0): plane[-rim:, :].reshape(-1),
        (-1, 0): plane[:rim, :].reshape(-1),
        (0, 1): plane[:, -rim:].reshape(-1),
        (0, -1): plane[:, :rim].reshape(-1),
        (1, 1): plane[-rim:, -rim:].reshape(-1),
        (1, -1): plane[-rim:, :rim].reshape(-1),
        (-1, 1): plane[:rim, -rim:].reshape(-1),
        (-1, -1): plane[:rim, :rim].reshape(-1),
    }
    got, _ = plane_exchange(pieces, rim * second, None)
    top = jnp.concatenate(
        [got[(-1, -1)].reshape(rim, rim), got[(-1, 0)].reshape(rim, second), got[(-1, 1)].reshape(rim, rim)], 1
    )
    middle = jnp.concatenate(
        [got[(0, -1)].reshape(first, rim), plane, got[(0, 1)].reshape(first, rim)], 1
    )
    bottom = jnp.concatenate(
        [got[(1, -1)].reshape(rim, rim), got[(1, 0)].reshape(rim, second), got[(1, 1)].reshape(rim, rim)], 1
    )
    return jnp.concatenate([top, middle, bottom], 0)


def line_factors(length, block_id, block_count):
    position = jnp.arange(length)
    at_start = (position == 0) & (block_id == 0)
    at_end = (position == length - 1) & (block_id == block_count - 1)
    mass_line = jnp.where(position % 3 == 0, jnp.where(at_start | at_end, 0.125, 0.25), 0.375)
    shared = (position == 0) & (block_id > 0) | (position == length - 1) & (
        block_id < block_count - 1
    )
    weight = jnp.where(shared, 0.5, 1.0)
    return (mass_line.astype(jnp.float32), weight.astype(jnp.float32))


def factor_grid(depth_line, first_line, second_line):
    return depth_line[:, None, None] * first_line[None, :, None] * second_line[None, None, :]


def node_table(matrix, labels, kind_count):
    out = matrix[kind_count - 1][:, None]
    for kind in range(kind_count - 2, -1, -1):
        out = jnp.where(labels == kind, matrix[kind][:, None], out)
    return out


def ext_index(target, anchor, length_local, rim_width):
    relative = target - anchor
    return jnp.where(
        relative < 0,
        rim_width - 1 + relative,
        jnp.where(relative > length_local - 1, rim_width + relative + 1, rim_width + relative),
    )


def per_device(
    potential,
    gating,
    cell_type,
    drug_class,
    half_point,
    gate_slope,
    time_const,
    max_conduct,
    reversal,
    drug_block,
    heart_cond,
    torso_cond,
    epi_target,
):
    depth_len, first_len, second_len = potential.shape
    torso_len = 3 * torso_cond.shape[0] + 1
    index_torso = lax.axis_index("torso")
    index_first = lax.axis_index("hx")
    index_second = lax.axis_index("hy")
    heart_depth, unused_depth = line_factors(depth_len, index_torso, lax.axis_size("torso"))
    first_mass, first_weight = line_factors(first_len, index_first, lax.axis_size("hx"))
    second_mass, second_weight = line_factors(second_len, index_second, lax.axis_size("hy"))
    torso_depth, torso_depth_weight = line_factors(torso_len, index_torso, lax.axis_size("torso"))
    heart_mass = factor_grid(heart_depth, first_mass, second_mass)
    torso_mass = factor_grid(torso_depth, first_mass, second_mass)
    torso_weight = factor_grid(torso_depth_weight, first_weight, second_weight)
    type_flat = cell_type.reshape(1, -1)
    class_flat = drug_class.reshape(1, -1)
    half_nodes = node_table(half_point, type_flat, TYPES)
    slope_nodes = node_table(gate_slope, type_flat, TYPES)
    decay_nodes = node_table(jnp.exp(-time_step / time_const), type_flat, TYPES)
    cond_nodes = node_table(max_conduct, type_flat, TYPES) * node_table(
        drug_block, class_flat, CLASSES
    )
    gate_flat = gating.reshape(gating.shape[0], -1)
    for repeat in range(STEPS):
        volts = potential.reshape(1, -1)
        inf_value = jax.nn.sigmoid((volts - half_nodes) * slope_nodes)
        gate_flat = inf_value + (gate_flat - inf_value) * decay_nodes
        current = jnp.sum(cond_nodes * gate_flat * (volts - reversal[:, None]), 0)
        diffusion, _ = face_sums(local_products(potential, heart_cond))
        potential = potential - time_step * (
            diffusion / heart_mass + current.reshape(potential.shape)
        )
    new_gating = gate_flat.reshape(gating.shape)

    rim_width = REACH + 1
    extended = rim_plane(potential[0], rim_width)
    distinct_second = lax.axis_size("hy") * (second_len - 1) + 1
    target_first = epi_target // distinct_second
    target_second = epi_target % distinct_second
    place_first = ext_index(target_first, index_first * (first_len - 1), first_len, rim_width)
    place_second = ext_index(target_second, index_second * (second_len - 1), second_len, rim_width)
    shift_first = place_first - rim_width - jnp.arange(first_len)[:, None]
    shift_second = place_second - rim_width - jnp.arange(second_len)[None, :]
    picked_values = jnp.zeros((first_len, second_len), jnp.float32)
    for step_first in range(-rim_width, rim_width + 1):
        rows = extended[rim_width + step_first : rim_width + step_first + first_len]
        along = jnp.zeros((first_len, second_len), jnp.float32)
        for step_second in range(-rim_width, rim_width + 1):
            window = rows[:, rim_width + step_second : rim_width + step_second + second_len]
            along = jnp.where(shift_second == step_second, window, along)
        picked_values = jnp.where(shift_first == step_first, along, picked_values)
    plane = jnp.where(index_torso == 0, picked_values, 0.0)
    rhs = jnp.concatenate(
        [plane[None], jnp.zeros((torso_len - 1, first_len, second_len), jnp.float32)], 0
    )

    mass_shift = torso_shift * torso_mass
    weighted_mass = torso_weight * mass_shift

    def exchange(residual, extra):
        local = local_products(residual, torso_cond)
        partial = jnp.stack(
            [
                jnp.sum(torso_weight * residual * residual),
                jnp.sum(residual * local) + jnp.sum(weighted_mass * residual * residual),
            ]
            + extra(local)
        )
        summed, sums = face_sums(local, partial)
        return summed + mass_shift * residual, sums

    image, sums = exchange(rhs, lambda local: [])
    norm_now = sums[0]
    curvature = sums[1]
    step_size = norm_now / curvature
    solution = step_size * rhs
    direction = rhs
    residual = rhs - step_size * image

    def later_turn(turn_index, state_tuple):
        solution, residual, direction, image, norm_now, curvature = state_tuple
        s_image, sums = exchange(
            residual,
            lambda local: [
                jnp.sum(torso_weight * residual * image),
                jnp.sum(direction * local) + jnp.sum(weighted_mass * direction * residual),
            ],
        )
        norm_next = sums[0]
        ratio = norm_next / norm_now
        curvature = sums[1] + ratio * (sums[2] + sums[3]) + ratio * ratio * curvature
        direction = residual + ratio * direction
        image = s_image + ratio * image
        step_size = norm_next / curvature
        solution = solution + step_size * direction
        residual = residual - step_size * image
        return (solution, residual, direction, image, norm_next, curvature)

    state = (solution, residual, direction, image, norm_now, curvature)
    solution = lax.fori_loop(1, ITERS, later_turn, state)[0]
    return (potential, new_gating, solution)


def solution(mesh):
    placed = (
        P("torso", "hx", "hy"),
        P(None, "torso", "hx", "hy"),
        P("torso", "hx", "hy"),
        P("torso", "hx", "hy"),
        P(),
        P(),
        P(),
        P(),
        P(),
        P(),
        P("torso", "hx", "hy"),
        P("torso", "hx", "hy"),
        P("hx", "hy"),
    )
    return jax.shard_map(
        per_device,
        mesh=mesh,
        in_specs=placed,
        out_specs=(P("torso", "hx", "hy"), P(None, "torso", "hx", "hy"), P("torso", "hx", "hy")),
        check_vma=False,
    )
```

```python
import jax
import jax.numpy as jnp
import numpy as np
from jax import lax
from jax.sharding import PartitionSpec as P

TYPES = 3
CLASSES = 4
STEPS = 2
ITERS = 4
REACH = 2


STIFF_LINE = (
    np.array(
        [
            [148.0, -189.0, 54.0, -13.0],
            [-189.0, 432.0, -297.0, 54.0],
            [54.0, -297.0, 432.0, -189.0],
            [-13.0, 54.0, -189.0, 148.0],
        ]
    )
    / 40.0
)
MASS_LINE = (
    np.array(
        [
            [128.0, 99.0, -36.0, 19.0],
            [99.0, 648.0, -81.0, -36.0],
            [-36.0, -81.0, 648.0, 99.0],
            [19.0, -36.0, 99.0, 128.0],
        ]
    )
    / 1680.0
)
time_step = 0.002
torso_shift = 0.02
HIGH = lax.Precision.HIGHEST


def gather_matrix(length, line):
    elements = (length - 1) // 3
    shape = (length, 4, elements)
    node = lax.broadcasted_iota(jnp.int32, shape, 0)
    offset = lax.broadcasted_iota(jnp.int32, shape, 1)
    local = node - 3 * lax.broadcasted_iota(jnp.int32, shape, 2)
    out = jnp.zeros(shape, jnp.float32)
    for a in range(4):
        for j in range(4):
            if line[a, j] != 0.0:
                out = jnp.where((offset == a) & (local == j), jnp.float32(line[a, j]), out)
    return out.reshape(length, 4 * elements)


def element_matrices(first, second):
    return dict(
        pick_mass=gather_matrix(first, MASS_LINE).T,
        pick_stiff=gather_matrix(first, STIFF_LINE).T,
        lanes_m=gather_matrix(second, MASS_LINE),
        lanes_k=gather_matrix(second, STIFF_LINE),
        scatter_second=gather_matrix(second, np.eye(4)).T,
        scatter_first=gather_matrix(first, np.eye(4)),
    )


def local_products(values, conduct, mats):
    depth, first, second = values.shape
    first_el, second_el = conduct.shape[1], conduct.shape[2]
    mass_d = [[float(MASS_LINE[i, j]) for j in range(4)] for i in range(4)]
    stiff_d = [[float(STIFF_LINE[i, j]) for j in range(4)] for i in range(4)]
    rows = [values[j] for j in range(depth)]
    v_mass = jnp.stack([sum(mass_d[i][j] * rows[j] for j in range(4)) for i in range(4)])
    v_stiff = jnp.stack([sum(stiff_d[i][j] * rows[j] for j in range(4)) for i in range(4)])
    pick_mass = mats["pick_mass"]
    pick_stiff = mats["pick_stiff"]
    along_first_m = jnp.einsum("kx,dxy->dky", pick_mass, v_mass, precision=HIGH)
    along_first_k = jnp.einsum("kx,dxy->dky", pick_stiff, v_mass, precision=HIGH) + jnp.einsum(
        "kx,dxy->dky", pick_mass, v_stiff, precision=HIGH
    )
    lanes_m = mats["lanes_m"]
    lanes_k = mats["lanes_k"]
    flat_m = along_first_m.reshape(-1, second)
    flat_k = along_first_k.reshape(-1, second)
    element = jnp.dot(flat_m, lanes_k, precision=HIGH) + jnp.dot(flat_k, lanes_m, precision=HIGH)
    element = element.reshape(depth, 4, first_el, 4, second_el) * conduct.reshape(
        1, 1, first_el, 1, second_el
    )
    scatter_second = mats["scatter_second"]
    spread = jnp.dot(element.reshape(-1, 4 * second_el), scatter_second, precision=HIGH)
    spread = spread.reshape(depth, 4 * first_el, second)
    scatter_first = mats["scatter_first"]
    return jnp.einsum("xk,dky->dxy", scatter_first, spread, precision=HIGH)


def torso_stage(values, scalars):
    count = lax.axis_size("torso")
    if count == 1:
        return values, scalars
    if count != 2:
        raise NotImplementedError("torso size")
    me = lax.axis_index("torso")
    face = jnp.where(me == 0, values[-1], values[0])
    extra = None
    if scalars is not None:
        extra = jnp.pad(scalars, (0, values.shape[2] - scalars.shape[0]))[None, :]
        face = jnp.concatenate([face, extra], 0)
    got = lax.ppermute(face, "torso", [(0, 1), (1, 0)])
    rows = values.shape[1]
    got_face = got[:rows]
    values = values.at[-1].add(jnp.where(me == 0, got_face, 0.0))
    values = values.at[0].add(jnp.where(me == 1, got_face, 0.0))
    if scalars is not None:
        scalars = scalars + got[rows, : scalars.shape[0]]
    return values, scalars


def plane_exchange(pieces, width, scalars):
    count_x, count_y = lax.axis_size("hx"), lax.axis_size("hy")
    me_x, me_y = lax.axis_index("hx"), lax.axis_index("hy")
    rows = []
    for code in range(9):
        offset = (code // 3 - 1, code % 3 - 1)
        piece = pieces.get(offset)
        row = jnp.zeros((width,), jnp.float32) if piece is None else jnp.pad(piece, (0, width - piece.shape[0]))
        if scalars is not None:
            row = jnp.concatenate([row, scalars])
        rows.append(row)
    table = jnp.stack(rows)
    peers = jnp.arange(count_x * count_y, dtype=jnp.int32)
    off_x = peers // count_y - me_x
    off_y = peers % count_y - me_y
    near = (jnp.abs(off_x) <= 1) & (jnp.abs(off_y) <= 1)
    code_of = jnp.where(near, (off_x + 1) * 3 + (off_y + 1), 4)
    send = jnp.take(table, code_of, axis=0)
    got = lax.all_to_all(send, ("hx", "hy"), 0, 0, tiled=True)
    received = {}
    for offset in pieces:
        src_x, src_y = me_x + offset[0], me_y + offset[1]
        valid = (src_x >= 0) & (src_x < count_x) & (src_y >= 0) & (src_y < count_y)
        src = jnp.clip(src_x, 0, count_x - 1) * count_y + jnp.clip(src_y, 0, count_y - 1)
        row = lax.dynamic_index_in_dim(got, src, 0, keepdims=False)
        received[offset] = jnp.where(valid, row[: pieces[offset].shape[0]], 0.0)
    total = None
    if scalars is not None:
        total = jnp.sum(got[:, width:], axis=0)
    return received, total


def face_sums(values, scalars=None):
    values, scalars = torso_stage(values, scalars)
    depth, first, second = values.shape
    pieces = {
        (1, 0): values[:, -1, :].reshape(-1),
        (-1, 0): values[:, 0, :].reshape(-1),
        (0, 1): values[:, :, -1].reshape(-1),
        (0, -1): values[:, :, 0].reshape(-1),
        (1, 1): values[:, -1, -1],
        (1, -1): values[:, -1, 0],
        (-1, 1): values[:, 0, -1],
        (-1, -1): values[:, 0, 0],
    }
    got, total = plane_exchange(pieces, depth * second, scalars)
    low_second = got[(0, -1)].reshape(depth, first)
    low_second = low_second.at[:, 0].add(got[(-1, -1)]).at[:, -1].add(got[(1, -1)])
    high_second = got[(0, 1)].reshape(depth, first)
    high_second = high_second.at[:, 0].add(got[(-1, 1)]).at[:, -1].add(got[(1, 1)])
    values = values.at[:, 0, :].add(got[(-1, 0)].reshape(depth, second))
    values = values.at[:, -1, :].add(got[(1, 0)].reshape(depth, second))
    values = values.at[:, :, 0].add(low_second).at[:, :, -1].add(high_second)
    return values, total


def rim_plane(plane, rim):
    first, second = plane.shape
    pieces = {
        (1, 0): plane[-rim:, :].reshape(-1),
        (-1, 0): plane[:rim, :].reshape(-1),
        (0, 1): plane[:, -rim:].reshape(-1),
        (0, -1): plane[:, :rim].reshape(-1),
        (1, 1): plane[-rim:, -rim:].reshape(-1),
        (1, -1): plane[-rim:, :rim].reshape(-1),
        (-1, 1): plane[:rim, -rim:].reshape(-1),
        (-1, -1): plane[:rim, :rim].reshape(-1),
    }
    got, _ = plane_exchange(pieces, rim * second, None)
    top = jnp.concatenate(
        [got[(-1, -1)].reshape(rim, rim), got[(-1, 0)].reshape(rim, second), got[(-1, 1)].reshape(rim, rim)], 1
    )
    middle = jnp.concatenate(
        [got[(0, -1)].reshape(first, rim), plane, got[(0, 1)].reshape(first, rim)], 1
    )
    bottom = jnp.concatenate(
        [got[(1, -1)].reshape(rim, rim), got[(1, 0)].reshape(rim, second), got[(1, 1)].reshape(rim, rim)], 1
    )
    return jnp.concatenate([top, middle, bottom], 0)


def line_factors(length, block_id, block_count):
    position = jnp.arange(length)
    at_start = (position == 0) & (block_id == 0)
    at_end = (position == length - 1) & (block_id == block_count - 1)
    mass_line = jnp.where(position % 3 == 0, jnp.where(at_start | at_end, 0.125, 0.25), 0.375)
    shared = (position == 0) & (block_id > 0) | (position == length - 1) & (
        block_id < block_count - 1
    )
    weight = jnp.where(shared, 0.5, 1.0)
    return (mass_line.astype(jnp.float32), weight.astype(jnp.float32))


def factor_grid(depth_line, first_line, second_line):
    return depth_line[:, None, None] * first_line[None, :, None] * second_line[None, None, :]


def node_table(matrix, labels, kind_count):
    out = matrix[kind_count - 1][:, None]
    for kind in range(kind_count - 2, -1, -1):
        out = jnp.where(labels == kind, matrix[kind][:, None], out)
    return out


def ext_index(target, anchor, length_local, rim_width):
    relative = target - anchor
    return jnp.where(
        relative < 0,
        rim_width - 1 + relative,
        jnp.where(relative > length_local - 1, rim_width + relative + 1, rim_width + relative),
    )


def per_device(
    potential,
    gating,
    cell_type,
    drug_class,
    half_point,
    gate_slope,
    time_const,
    max_conduct,
    reversal,
    drug_block,
    heart_cond,
    torso_cond,
    epi_target,
):
    depth_len, first_len, second_len = potential.shape
    torso_len = 3 * torso_cond.shape[0] + 1
    index_torso = lax.axis_index("torso")
    index_first = lax.axis_index("hx")
    index_second = lax.axis_index("hy")
    heart_depth, unused_depth = line_factors(depth_len, index_torso, lax.axis_size("torso"))
    first_mass, first_weight = line_factors(first_len, index_first, lax.axis_size("hx"))
    second_mass, second_weight = line_factors(second_len, index_second, lax.axis_size("hy"))
    torso_depth, torso_depth_weight = line_factors(torso_len, index_torso, lax.axis_size("torso"))
    heart_mass = factor_grid(heart_depth, first_mass, second_mass)
    torso_mass = factor_grid(torso_depth, first_mass, second_mass)
    torso_weight = factor_grid(torso_depth_weight, first_weight, second_weight)
    type_flat = cell_type.reshape(1, -1)
    class_flat = drug_class.reshape(1, -1)
    half_nodes = node_table(half_point, type_flat, TYPES)
    slope_nodes = node_table(gate_slope, type_flat, TYPES)
    decay_nodes = node_table(jnp.exp(-time_step / time_const), type_flat, TYPES)
    cond_nodes = node_table(max_conduct, type_flat, TYPES) * node_table(
        drug_block, class_flat, CLASSES
    )
    gate_flat = gating.reshape(gating.shape[0], -1)
    mats = element_matrices(first_len, second_len)
    for repeat in range(STEPS):
        volts = potential.reshape(1, -1)
        inf_value = jax.nn.sigmoid((volts - half_nodes) * slope_nodes)
        gate_flat = inf_value + (gate_flat - inf_value) * decay_nodes
        current = jnp.sum(cond_nodes * gate_flat * (volts - reversal[:, None]), 0)
        diffusion, _ = face_sums(local_products(potential, heart_cond, mats))
        potential = potential - time_step * (
            diffusion / heart_mass + current.reshape(potential.shape)
        )
    new_gating = gate_flat.reshape(gating.shape)

    rim_width = REACH + 1
    extended = rim_plane(potential[0], rim_width)
    distinct_second = lax.axis_size("hy") * (second_len - 1) + 1
    target_first = epi_target // distinct_second
    target_second = epi_target % distinct_second
    place_first = ext_index(target_first, index_first * (first_len - 1), first_len, rim_width)
    place_second = ext_index(target_second, index_second * (second_len - 1), second_len, rim_width)
    shift_first = place_first - rim_width - jnp.arange(first_len)[:, None]
    shift_second = place_second - rim_width - jnp.arange(second_len)[None, :]
    picked_values = jnp.zeros((first_len, second_len), jnp.float32)
    for step_first in range(-rim_width, rim_width + 1):
        rows = extended[rim_width + step_first : rim_width + step_first + first_len]
        along = jnp.zeros((first_len, second_len), jnp.float32)
        for step_second in range(-rim_width, rim_width + 1):
            window = rows[:, rim_width + step_second : rim_width + step_second + second_len]
            along = jnp.where(shift_second == step_second, window, along)
        picked_values = jnp.where(shift_first == step_first, along, picked_values)
    plane = jnp.where(index_torso == 0, picked_values, 0.0)
    rhs = jnp.concatenate(
        [plane[None], jnp.zeros((torso_len - 1, first_len, second_len), jnp.float32)], 0
    )

    mass_shift = torso_shift * torso_mass
    weighted_mass = torso_weight * mass_shift
    zero_lanes = 0.0 * torso_weight[0, 0]

    def exchange(residual, extra):
        local = local_products(residual, torso_cond, mats)
        terms = [
            torso_weight * residual * residual,
            residual * local + weighted_mass * residual * residual,
        ] + extra(local)
        partial = jnp.sum(jnp.sum(jnp.stack(terms), axis=(1, 2)), axis=1)
        summed, sums = face_sums(local, partial)
        return summed + mass_shift * residual, sums[:, None] + zero_lanes[None, :]

    image, sums = exchange(rhs, lambda local: [])
    norm_now = sums[0]
    curvature = sums[1]
    step_size = norm_now / curvature
    solution = step_size * rhs
    direction = rhs
    residual = rhs - step_size * image

    def later_turn(turn_index, state_tuple):
        solution, residual, direction, image, norm_now, curvature = state_tuple
        s_image, sums = exchange(
            residual,
            lambda local: [
                torso_weight * residual * image,
                direction * local + weighted_mass * direction * residual,
            ],
        )
        norm_next = sums[0]
        ratio = norm_next / norm_now
        curvature = sums[1] + ratio * (sums[2] + sums[3]) + ratio * ratio * curvature
        direction = residual + ratio * direction
        image = s_image + ratio * image
        step_size = norm_next / curvature
        solution = solution + step_size * direction
        residual = residual - step_size * image
        return (solution, residual, direction, image, norm_next, curvature)

    state = (solution, residual, direction, image, norm_now, curvature)
    solution = lax.fori_loop(1, ITERS, later_turn, state)[0]
    return (potential, new_gating, solution)


def solution(mesh):
    placed = (
        P("torso", "hx", "hy"),
        P(None, "torso", "hx", "hy"),
        P("torso", "hx", "hy"),
        P("torso", "hx", "hy"),
        P(),
        P(),
        P(),
        P(),
        P(),
        P(),
        P("torso", "hx", "hy"),
        P("torso", "hx", "hy"),
        P("hx", "hy"),
    )
    return jax.shard_map(
        per_device,
        mesh=mesh,
        in_specs=placed,
        out_specs=(P("torso", "hx", "hy"), P(None, "torso", "hx", "hy"), P("torso", "hx", "hy")),
        check_vma=False,
    )
```

```python
import jax
import jax.numpy as jnp
import numpy as np
from jax import lax
from jax.sharding import PartitionSpec as P

TYPES = 3
CLASSES = 4
STEPS = 2
ITERS = 4
REACH = 2


STIFF_LINE = (
    np.array(
        [
            [148.0, -189.0, 54.0, -13.0],
            [-189.0, 432.0, -297.0, 54.0],
            [54.0, -297.0, 432.0, -189.0],
            [-13.0, 54.0, -189.0, 148.0],
        ]
    )
    / 40.0
)
MASS_LINE = (
    np.array(
        [
            [128.0, 99.0, -36.0, 19.0],
            [99.0, 648.0, -81.0, -36.0],
            [-36.0, -81.0, 648.0, 99.0],
            [19.0, -36.0, 99.0, 128.0],
        ]
    )
    / 1680.0
)
time_step = 0.002
torso_shift = 0.02
HIGH = lax.Precision.HIGHEST


def gather_matrix(length, line):
    elements = (length - 1) // 3
    shape = (length, 4, elements)
    node = lax.broadcasted_iota(jnp.int32, shape, 0)
    offset = lax.broadcasted_iota(jnp.int32, shape, 1)
    local = node - 3 * lax.broadcasted_iota(jnp.int32, shape, 2)
    out = jnp.zeros(shape, jnp.float32)
    for a in range(4):
        for j in range(4):
            if line[a, j] != 0.0:
                out = jnp.where((offset == a) & (local == j), jnp.float32(line[a, j]), out)
    return out.reshape(length, 4 * elements)


def element_matrices(first, second):
    return dict(
        pick_mass=gather_matrix(first, MASS_LINE).T,
        pick_stiff=gather_matrix(first, STIFF_LINE).T,
        lanes_m=gather_matrix(second, MASS_LINE),
        lanes_k=gather_matrix(second, STIFF_LINE),
        scatter_second=gather_matrix(second, np.eye(4)).T,
        scatter_first=gather_matrix(first, np.eye(4)),
    )


def local_products(values, conduct, mats):
    depth, first, second = values.shape
    first_el, second_el = conduct.shape[1], conduct.shape[2]
    mass_d = [[float(MASS_LINE[i, j]) for j in range(4)] for i in range(4)]
    stiff_d = [[float(STIFF_LINE[i, j]) for j in range(4)] for i in range(4)]
    rows = [values[j] for j in range(depth)]
    v_mass = jnp.stack([sum(mass_d[i][j] * rows[j] for j in range(4)) for i in range(4)])
    v_stiff = jnp.stack([sum(stiff_d[i][j] * rows[j] for j in range(4)) for i in range(4)])
    pick_mass = mats["pick_mass"]
    pick_stiff = mats["pick_stiff"]
    along_first_m = jnp.einsum("kx,dxy->dky", pick_mass, v_mass, precision=HIGH)
    along_first_k = jnp.einsum("kx,dxy->dky", pick_stiff, v_mass, precision=HIGH) + jnp.einsum(
        "kx,dxy->dky", pick_mass, v_stiff, precision=HIGH
    )
    lanes_m = mats["lanes_m"]
    lanes_k = mats["lanes_k"]
    flat_m = along_first_m.reshape(-1, second)
    flat_k = along_first_k.reshape(-1, second)
    element = jnp.dot(flat_m, lanes_k, precision=HIGH) + jnp.dot(flat_k, lanes_m, precision=HIGH)
    element = element.reshape(depth, 4, first_el, 4, second_el) * conduct.reshape(
        1, 1, first_el, 1, second_el
    )
    scatter_second = mats["scatter_second"]
    spread = jnp.dot(element.reshape(-1, 4 * second_el), scatter_second, precision=HIGH)
    spread = spread.reshape(depth, 4 * first_el, second)
    scatter_first = mats["scatter_first"]
    return jnp.einsum("xk,dky->dxy", scatter_first, spread, precision=HIGH)


def torso_stage(values, scalars):
    count = lax.axis_size("torso")
    if count == 1:
        return values, scalars
    if count != 2:
        raise NotImplementedError("torso size")
    me = lax.axis_index("torso")
    face = jnp.where(me == 0, values[-1], values[0])
    extra = None
    if scalars is not None:
        extra = jnp.pad(scalars, (0, values.shape[2] - scalars.shape[0]))[None, :]
        face = jnp.concatenate([face, extra], 0)
    got = lax.ppermute(face, "torso", [(0, 1), (1, 0)])
    rows = values.shape[1]
    got_face = got[:rows]
    values = values.at[-1].add(jnp.where(me == 0, got_face, 0.0))
    values = values.at[0].add(jnp.where(me == 1, got_face, 0.0))
    if scalars is not None:
        scalars = scalars + got[rows, : scalars.shape[0]]
    return values, scalars


def plane_exchange(pieces, width, scalars):
    count_x, count_y = lax.axis_size("hx"), lax.axis_size("hy")
    me_x, me_y = lax.axis_index("hx"), lax.axis_index("hy")
    rows = []
    for code in range(9):
        offset = (code // 3 - 1, code % 3 - 1)
        piece = pieces.get(offset)
        row = jnp.zeros((width,), jnp.float32) if piece is None else jnp.pad(piece, (0, width - piece.shape[0]))
        if scalars is not None:
            row = jnp.concatenate([row, scalars])
        rows.append(row)
    table = jnp.stack(rows)
    peers = jnp.arange(count_x * count_y, dtype=jnp.int32)
    off_x = peers // count_y - me_x
    off_y = peers % count_y - me_y
    near = (jnp.abs(off_x) <= 1) & (jnp.abs(off_y) <= 1)
    code_of = jnp.where(near, (off_x + 1) * 3 + (off_y + 1), 4)
    send = jnp.broadcast_to(table[4][None, :], (count_x * count_y, table.shape[1]))
    for code in range(9):
        if code != 4:
            send = jnp.where(code_of[:, None] == code, table[code][None, :], send)
    got = lax.all_to_all(send, ("hx", "hy"), 0, 0, tiled=True)
    received = {}
    for offset in pieces:
        src_x, src_y = me_x + offset[0], me_y + offset[1]
        valid = (src_x >= 0) & (src_x < count_x) & (src_y >= 0) & (src_y < count_y)
        src = jnp.clip(src_x, 0, count_x - 1) * count_y + jnp.clip(src_y, 0, count_y - 1)
        row = lax.dynamic_index_in_dim(got, src, 0, keepdims=False)
        received[offset] = jnp.where(valid, row[: pieces[offset].shape[0]], 0.0)
    total = None
    if scalars is not None:
        total = jnp.sum(got[:, width:], axis=0)
    return received, total


def face_sums(values, scalars=None):
    values, scalars = torso_stage(values, scalars)
    depth, first, second = values.shape
    pieces = {
        (1, 0): values[:, -1, :].reshape(-1),
        (-1, 0): values[:, 0, :].reshape(-1),
        (0, 1): values[:, :, -1].reshape(-1),
        (0, -1): values[:, :, 0].reshape(-1),
        (1, 1): values[:, -1, -1],
        (1, -1): values[:, -1, 0],
        (-1, 1): values[:, 0, -1],
        (-1, -1): values[:, 0, 0],
    }
    got, total = plane_exchange(pieces, depth * second, scalars)
    row = lax.broadcasted_iota(jnp.int32, (1, first, 1), 1)
    col = lax.broadcasted_iota(jnp.int32, (1, 1, second), 2)
    row_2d = row[:, :, 0]
    low_second = got[(0, -1)].reshape(depth, first)
    low_second = low_second + jnp.where(row_2d == 0, got[(-1, -1)][:, None], 0.0)
    low_second = low_second + jnp.where(row_2d == first - 1, got[(1, -1)][:, None], 0.0)
    high_second = got[(0, 1)].reshape(depth, first)
    high_second = high_second + jnp.where(row_2d == 0, got[(-1, 1)][:, None], 0.0)
    high_second = high_second + jnp.where(row_2d == first - 1, got[(1, 1)][:, None], 0.0)
    along_first = jnp.where(
        row == 0,
        got[(-1, 0)].reshape(depth, 1, second),
        jnp.where(row == first - 1, got[(1, 0)].reshape(depth, 1, second), 0.0),
    )
    along_second = jnp.where(
        col == 0,
        low_second[:, :, None],
        jnp.where(col == second - 1, high_second[:, :, None], 0.0),
    )
    return values + along_first + along_second, total


def rim_plane(plane, rim):
    first, second = plane.shape
    pieces = {
        (1, 0): plane[-rim:, :].reshape(-1),
        (-1, 0): plane[:rim, :].reshape(-1),
        (0, 1): plane[:, -rim:].reshape(-1),
        (0, -1): plane[:, :rim].reshape(-1),
        (1, 1): plane[-rim:, -rim:].reshape(-1),
        (1, -1): plane[-rim:, :rim].reshape(-1),
        (-1, 1): plane[:rim, -rim:].reshape(-1),
        (-1, -1): plane[:rim, :rim].reshape(-1),
    }
    got, _ = plane_exchange(pieces, rim * second, None)
    top = jnp.concatenate(
        [got[(-1, -1)].reshape(rim, rim), got[(-1, 0)].reshape(rim, second), got[(-1, 1)].reshape(rim, rim)], 1
    )
    middle = jnp.concatenate(
        [got[(0, -1)].reshape(first, rim), plane, got[(0, 1)].reshape(first, rim)], 1
    )
    bottom = jnp.concatenate(
        [got[(1, -1)].reshape(rim, rim), got[(1, 0)].reshape(rim, second), got[(1, 1)].reshape(rim, rim)], 1
    )
    return jnp.concatenate([top, middle, bottom], 0)


def line_factors(length, block_id, block_count):
    position = jnp.arange(length)
    at_start = (position == 0) & (block_id == 0)
    at_end = (position == length - 1) & (block_id == block_count - 1)
    mass_line = jnp.where(position % 3 == 0, jnp.where(at_start | at_end, 0.125, 0.25), 0.375)
    shared = (position == 0) & (block_id > 0) | (position == length - 1) & (
        block_id < block_count - 1
    )
    weight = jnp.where(shared, 0.5, 1.0)
    return (mass_line.astype(jnp.float32), weight.astype(jnp.float32))


def factor_grid(depth_line, first_line, second_line):
    return depth_line[:, None, None] * first_line[None, :, None] * second_line[None, None, :]


def node_table(matrix, labels, kind_count):
    out = matrix[kind_count - 1][:, None]
    for kind in range(kind_count - 2, -1, -1):
        out = jnp.where(labels == kind, matrix[kind][:, None], out)
    return out


def ext_index(target, anchor, length_local, rim_width):
    relative = target - anchor
    return jnp.where(
        relative < 0,
        rim_width - 1 + relative,
        jnp.where(relative > length_local - 1, rim_width + relative + 1, rim_width + relative),
    )


def per_device(
    potential,
    gating,
    cell_type,
    drug_class,
    half_point,
    gate_slope,
    time_const,
    max_conduct,
    reversal,
    drug_block,
    heart_cond,
    torso_cond,
    epi_target,
):
    depth_len, first_len, second_len = potential.shape
    torso_len = 3 * torso_cond.shape[0] + 1
    index_torso = lax.axis_index("torso")
    index_first = lax.axis_index("hx")
    index_second = lax.axis_index("hy")
    heart_depth, unused_depth = line_factors(depth_len, index_torso, lax.axis_size("torso"))
    first_mass, first_weight = line_factors(first_len, index_first, lax.axis_size("hx"))
    second_mass, second_weight = line_factors(second_len, index_second, lax.axis_size("hy"))
    torso_depth, torso_depth_weight = line_factors(torso_len, index_torso, lax.axis_size("torso"))
    heart_mass = factor_grid(heart_depth, first_mass, second_mass)
    torso_mass = factor_grid(torso_depth, first_mass, second_mass)
    torso_weight = factor_grid(torso_depth_weight, first_weight, second_weight)
    type_flat = cell_type.reshape(1, -1)
    class_flat = drug_class.reshape(1, -1)
    half_nodes = node_table(half_point, type_flat, TYPES)
    slope_nodes = node_table(gate_slope, type_flat, TYPES)
    decay_nodes = node_table(jnp.exp(-time_step / time_const), type_flat, TYPES)
    cond_nodes = node_table(max_conduct, type_flat, TYPES) * node_table(
        drug_block, class_flat, CLASSES
    )
    gate_flat = gating.reshape(gating.shape[0], -1)
    mats = element_matrices(first_len, second_len)
    for repeat in range(STEPS):
        volts = potential.reshape(1, -1)
        inf_value = jax.nn.sigmoid((volts - half_nodes) * slope_nodes)
        gate_flat = inf_value + (gate_flat - inf_value) * decay_nodes
        current = jnp.sum(cond_nodes * gate_flat * (volts - reversal[:, None]), 0)
        diffusion, _ = face_sums(local_products(potential, heart_cond, mats))
        potential = potential - time_step * (
            diffusion / heart_mass + current.reshape(potential.shape)
        )
    new_gating = gate_flat.reshape(gating.shape)

    rim_width = REACH + 1
    extended = rim_plane(potential[0], rim_width)
    distinct_second = lax.axis_size("hy") * (second_len - 1) + 1
    target_first = epi_target // distinct_second
    target_second = epi_target % distinct_second
    place_first = ext_index(target_first, index_first * (first_len - 1), first_len, rim_width)
    place_second = ext_index(target_second, index_second * (second_len - 1), second_len, rim_width)
    shift_first = place_first - rim_width - jnp.arange(first_len)[:, None]
    shift_second = place_second - rim_width - jnp.arange(second_len)[None, :]
    picked_values = jnp.zeros((first_len, second_len), jnp.float32)
    for step_first in range(-rim_width, rim_width + 1):
        rows = extended[rim_width + step_first : rim_width + step_first + first_len]
        along = jnp.zeros((first_len, second_len), jnp.float32)
        for step_second in range(-rim_width, rim_width + 1):
            window = rows[:, rim_width + step_second : rim_width + step_second + second_len]
            along = jnp.where(shift_second == step_second, window, along)
        picked_values = jnp.where(shift_first == step_first, along, picked_values)
    plane = jnp.where(index_torso == 0, picked_values, 0.0)
    rhs = jnp.concatenate(
        [plane[None], jnp.zeros((torso_len - 1, first_len, second_len), jnp.float32)], 0
    )

    mass_shift = torso_shift * torso_mass
    weighted_mass = torso_weight * mass_shift
    zero_lanes = 0.0 * torso_weight[0, 0]

    def exchange(residual, extra):
        local = local_products(residual, torso_cond, mats)
        terms = [
            torso_weight * residual * residual,
            residual * local + weighted_mass * residual * residual,
        ] + extra(local)
        partial = jnp.sum(jnp.sum(jnp.stack(terms), axis=(1, 2)), axis=1)
        summed, sums = face_sums(local, partial)
        return summed + mass_shift * residual, sums[:, None] + zero_lanes[None, :]

    image, sums = exchange(rhs, lambda local: [])
    norm_now = sums[0]
    curvature = sums[1]
    step_size = norm_now / curvature
    solution = step_size * rhs
    direction = rhs
    residual = rhs - step_size * image

    def later_turn(turn_index, state_tuple):
        solution, residual, direction, image, norm_now, curvature = state_tuple
        s_image, sums = exchange(
            residual,
            lambda local: [
                torso_weight * residual * image,
                direction * local + weighted_mass * direction * residual,
            ],
        )
        norm_next = sums[0]
        ratio = norm_next / norm_now
        curvature = sums[1] + ratio * (sums[2] + sums[3]) + ratio * ratio * curvature
        direction = residual + ratio * direction
        image = s_image + ratio * image
        step_size = norm_next / curvature
        solution = solution + step_size * direction
        residual = residual - step_size * image
        return (solution, residual, direction, image, norm_next, curvature)

    state = (solution, residual, direction, image, norm_now, curvature)
    solution = lax.fori_loop(1, ITERS, later_turn, state)[0]
    return (potential, new_gating, solution)


def solution(mesh):
    placed = (
        P("torso", "hx", "hy"),
        P(None, "torso", "hx", "hy"),
        P("torso", "hx", "hy"),
        P("torso", "hx", "hy"),
        P(),
        P(),
        P(),
        P(),
        P(),
        P(),
        P("torso", "hx", "hy"),
        P("torso", "hx", "hy"),
        P("hx", "hy"),
    )
    return jax.shard_map(
        per_device,
        mesh=mesh,
        in_specs=placed,
        out_specs=(P("torso", "hx", "hy"), P(None, "torso", "hx", "hy"), P("torso", "hx", "hy")),
        check_vma=False,
    )
```

```python
import jax
import jax.numpy as jnp
import numpy as np
from jax import lax
from jax.sharding import PartitionSpec as P

TYPES = 3
CLASSES = 4
STEPS = 2
ITERS = 4
REACH = 2


STIFF_LINE = (
    np.array(
        [
            [148.0, -189.0, 54.0, -13.0],
            [-189.0, 432.0, -297.0, 54.0],
            [54.0, -297.0, 432.0, -189.0],
            [-13.0, 54.0, -189.0, 148.0],
        ]
    )
    / 40.0
)
MASS_LINE = (
    np.array(
        [
            [128.0, 99.0, -36.0, 19.0],
            [99.0, 648.0, -81.0, -36.0],
            [-36.0, -81.0, 648.0, 99.0],
            [19.0, -36.0, 99.0, 128.0],
        ]
    )
    / 1680.0
)
time_step = 0.002
torso_shift = 0.02
HIGH = lax.Precision.HIGHEST


def gather_matrix(length, line):
    elements = (length - 1) // 3
    shape = (length, 4, elements)
    node = lax.broadcasted_iota(jnp.int32, shape, 0)
    offset = lax.broadcasted_iota(jnp.int32, shape, 1)
    local = node - 3 * lax.broadcasted_iota(jnp.int32, shape, 2)
    out = jnp.zeros(shape, jnp.float32)
    for a in range(4):
        for j in range(4):
            if line[a, j] != 0.0:
                out = jnp.where((offset == a) & (local == j), jnp.float32(line[a, j]), out)
    return out.reshape(length, 4 * elements)


def element_matrices(first, second):
    return dict(
        pick_mass=gather_matrix(first, MASS_LINE).T,
        pick_stiff=gather_matrix(first, STIFF_LINE).T,
        lanes_m=gather_matrix(second, MASS_LINE),
        lanes_k=gather_matrix(second, STIFF_LINE),
        scatter_second=gather_matrix(second, np.eye(4)).T,
        scatter_first=gather_matrix(first, np.eye(4)),
    )


def local_products(values, conduct, mats):
    depth, first, second = values.shape
    first_el, second_el = conduct.shape[1], conduct.shape[2]
    mass_d = [[float(MASS_LINE[i, j]) for j in range(4)] for i in range(4)]
    stiff_d = [[float(STIFF_LINE[i, j]) for j in range(4)] for i in range(4)]
    rows = [values[j] for j in range(depth)]
    v_mass = jnp.stack([sum(mass_d[i][j] * rows[j] for j in range(4)) for i in range(4)])
    v_stiff = jnp.stack([sum(stiff_d[i][j] * rows[j] for j in range(4)) for i in range(4)])
    pick_mass = mats["pick_mass"]
    pick_stiff = mats["pick_stiff"]
    along_first_m = jnp.einsum("kx,dxy->dky", pick_mass, v_mass, precision=HIGH)
    along_first_k = jnp.einsum("kx,dxy->dky", pick_stiff, v_mass, precision=HIGH) + jnp.einsum(
        "kx,dxy->dky", pick_mass, v_stiff, precision=HIGH
    )
    lanes_m = mats["lanes_m"]
    lanes_k = mats["lanes_k"]
    flat_m = along_first_m.reshape(-1, second)
    flat_k = along_first_k.reshape(-1, second)
    element = jnp.dot(flat_m, lanes_k, precision=HIGH) + jnp.dot(flat_k, lanes_m, precision=HIGH)
    element = element.reshape(depth, 4, first_el, 4, second_el) * conduct.reshape(
        1, 1, first_el, 1, second_el
    )
    scatter_second = mats["scatter_second"]
    spread = jnp.dot(element.reshape(-1, 4 * second_el), scatter_second, precision=HIGH)
    spread = spread.reshape(depth, 4 * first_el, second)
    scatter_first = mats["scatter_first"]
    return jnp.einsum("xk,dky->dxy", scatter_first, spread, precision=HIGH)


def torso_stage(values, scalars):
    count = lax.axis_size("torso")
    if count == 1:
        return values, scalars
    if count != 2:
        raise NotImplementedError("torso size")
    me = lax.axis_index("torso")
    face = jnp.where(me == 0, values[-1], values[0])
    extra = None
    if scalars is not None:
        extra = jnp.pad(scalars, (0, values.shape[2] - scalars.shape[0]))[None, :]
        face = jnp.concatenate([face, extra], 0)
    got = lax.ppermute(face, "torso", [(0, 1), (1, 0)])
    rows = values.shape[1]
    got_face = got[:rows]
    values = values.at[-1].add(jnp.where(me == 0, got_face, 0.0))
    values = values.at[0].add(jnp.where(me == 1, got_face, 0.0))
    if scalars is not None:
        scalars = scalars + got[rows, : scalars.shape[0]]
    return values, scalars


def plane_exchange(pieces, width, scalars, tie=None):
    count_x, count_y = lax.axis_size("hx"), lax.axis_size("hy")
    me_x, me_y = lax.axis_index("hx"), lax.axis_index("hy")
    rows = []
    for code in range(9):
        offset = (code // 3 - 1, code % 3 - 1)
        piece = pieces.get(offset)
        row = jnp.zeros((width,), jnp.float32) if piece is None else jnp.pad(piece, (0, width - piece.shape[0]))
        if scalars is not None:
            row = jnp.concatenate([row, scalars])
        rows.append(row)
    table = jnp.stack(rows)
    peers = jnp.arange(count_x * count_y, dtype=jnp.int32)
    off_x = peers // count_y - me_x
    off_y = peers % count_y - me_y
    near = (jnp.abs(off_x) <= 1) & (jnp.abs(off_y) <= 1)
    code_of = jnp.where(near, (off_x + 1) * 3 + (off_y + 1), 4)
    send = jnp.broadcast_to(table[4][None, :], (count_x * count_y, table.shape[1]))
    for code in range(9):
        if code != 4:
            send = jnp.where(code_of[:, None] == code, table[code][None, :], send)
    if tie is not None:
        send, tie = lax.optimization_barrier((send, tie))
    got = lax.all_to_all(send, ("hx", "hy"), 0, 0, tiled=True)
    received = {}
    for offset in pieces:
        src_x, src_y = me_x + offset[0], me_y + offset[1]
        valid = (src_x >= 0) & (src_x < count_x) & (src_y >= 0) & (src_y < count_y)
        src = jnp.clip(src_x, 0, count_x - 1) * count_y + jnp.clip(src_y, 0, count_y - 1)
        row = lax.dynamic_index_in_dim(got, src, 0, keepdims=False)
        received[offset] = jnp.where(valid, row[: pieces[offset].shape[0]], 0.0)
    total = None
    if scalars is not None:
        total = jnp.sum(got[:, width:], axis=0)
    return received, total, tie


def face_sums(values, scalars=None, tie=None):
    values, scalars = torso_stage(values, scalars)
    depth, first, second = values.shape
    pieces = {
        (1, 0): values[:, -1, :].reshape(-1),
        (-1, 0): values[:, 0, :].reshape(-1),
        (0, 1): values[:, :, -1].reshape(-1),
        (0, -1): values[:, :, 0].reshape(-1),
        (1, 1): values[:, -1, -1],
        (1, -1): values[:, -1, 0],
        (-1, 1): values[:, 0, -1],
        (-1, -1): values[:, 0, 0],
    }
    got, total, tie = plane_exchange(pieces, depth * second, scalars, tie)
    at_low = ((0, 0), (0, first - 1))
    at_high = ((0, 0), (first - 1, 0))
    low_second = got[(0, -1)].reshape(depth, first)
    low_second = low_second + jnp.pad(got[(-1, -1)][:, None], at_low)
    low_second = low_second + jnp.pad(got[(1, -1)][:, None], at_high)
    high_second = got[(0, 1)].reshape(depth, first)
    high_second = high_second + jnp.pad(got[(-1, 1)][:, None], at_low)
    high_second = high_second + jnp.pad(got[(1, 1)][:, None], at_high)
    along_first = jnp.pad(got[(-1, 0)].reshape(depth, 1, second), ((0, 0), (0, first - 1), (0, 0)))
    along_first = along_first + jnp.pad(
        got[(1, 0)].reshape(depth, 1, second), ((0, 0), (first - 1, 0), (0, 0))
    )
    along_second = jnp.pad(low_second[:, :, None], ((0, 0), (0, 0), (0, second - 1)))
    along_second = along_second + jnp.pad(
        high_second[:, :, None], ((0, 0), (0, 0), (second - 1, 0))
    )
    summed = values + along_first + along_second
    if tie is None:
        return summed, total
    return summed, total, tie


def rim_plane(plane, rim):
    first, second = plane.shape
    pieces = {
        (1, 0): plane[-rim:, :].reshape(-1),
        (-1, 0): plane[:rim, :].reshape(-1),
        (0, 1): plane[:, -rim:].reshape(-1),
        (0, -1): plane[:, :rim].reshape(-1),
        (1, 1): plane[-rim:, -rim:].reshape(-1),
        (1, -1): plane[-rim:, :rim].reshape(-1),
        (-1, 1): plane[:rim, -rim:].reshape(-1),
        (-1, -1): plane[:rim, :rim].reshape(-1),
    }
    got, _, _ = plane_exchange(pieces, rim * second, None)
    top = jnp.concatenate(
        [got[(-1, -1)].reshape(rim, rim), got[(-1, 0)].reshape(rim, second), got[(-1, 1)].reshape(rim, rim)], 1
    )
    middle = jnp.concatenate(
        [got[(0, -1)].reshape(first, rim), plane, got[(0, 1)].reshape(first, rim)], 1
    )
    bottom = jnp.concatenate(
        [got[(1, -1)].reshape(rim, rim), got[(1, 0)].reshape(rim, second), got[(1, 1)].reshape(rim, rim)], 1
    )
    return jnp.concatenate([top, middle, bottom], 0)


def line_factors(length, block_id, block_count):
    position = jnp.arange(length)
    at_start = (position == 0) & (block_id == 0)
    at_end = (position == length - 1) & (block_id == block_count - 1)
    mass_line = jnp.where(position % 3 == 0, jnp.where(at_start | at_end, 0.125, 0.25), 0.375)
    shared = (position == 0) & (block_id > 0) | (position == length - 1) & (
        block_id < block_count - 1
    )
    weight = jnp.where(shared, 0.5, 1.0)
    return (mass_line.astype(jnp.float32), weight.astype(jnp.float32))


def factor_grid(depth_line, first_line, second_line):
    return depth_line[:, None, None] * first_line[None, :, None] * second_line[None, None, :]


def node_table(matrix, labels, kind_count):
    out = matrix[kind_count - 1][:, None]
    for kind in range(kind_count - 2, -1, -1):
        out = jnp.where(labels == kind, matrix[kind][:, None], out)
    return out


def ext_index(target, anchor, length_local, rim_width):
    relative = target - anchor
    return jnp.where(
        relative < 0,
        rim_width - 1 + relative,
        jnp.where(relative > length_local - 1, rim_width + relative + 1, rim_width + relative),
    )


def per_device(
    potential,
    gating,
    cell_type,
    drug_class,
    half_point,
    gate_slope,
    time_const,
    max_conduct,
    reversal,
    drug_block,
    heart_cond,
    torso_cond,
    epi_target,
):
    depth_len, first_len, second_len = potential.shape
    torso_len = 3 * torso_cond.shape[0] + 1
    index_torso = lax.axis_index("torso")
    index_first = lax.axis_index("hx")
    index_second = lax.axis_index("hy")
    heart_depth, unused_depth = line_factors(depth_len, index_torso, lax.axis_size("torso"))
    first_mass, first_weight = line_factors(first_len, index_first, lax.axis_size("hx"))
    second_mass, second_weight = line_factors(second_len, index_second, lax.axis_size("hy"))
    torso_depth, torso_depth_weight = line_factors(torso_len, index_torso, lax.axis_size("torso"))
    heart_mass = factor_grid(heart_depth, first_mass, second_mass)
    torso_mass = factor_grid(torso_depth, first_mass, second_mass)
    torso_weight = factor_grid(torso_depth_weight, first_weight, second_weight)
    type_flat = cell_type.reshape(1, -1)
    class_flat = drug_class.reshape(1, -1)
    half_nodes = node_table(half_point, type_flat, TYPES)
    slope_nodes = node_table(gate_slope, type_flat, TYPES)
    decay_nodes = node_table(jnp.exp(-time_step / time_const), type_flat, TYPES)
    cond_nodes = node_table(max_conduct, type_flat, TYPES) * node_table(
        drug_block, class_flat, CLASSES
    )
    gate_flat = gating.reshape(gating.shape[0], -1)
    mats = element_matrices(first_len, second_len)
    for repeat in range(STEPS):
        diffusion, _, tied = face_sums(local_products(potential, heart_cond, mats), tie=potential)
        volts = tied.reshape(1, -1)
        inf_value = jax.nn.sigmoid((volts - half_nodes) * slope_nodes)
        gate_flat = inf_value + (gate_flat - inf_value) * decay_nodes
        current = jnp.sum(cond_nodes * gate_flat * (volts - reversal[:, None]), 0)
        potential = potential - time_step * (
            diffusion / heart_mass + current.reshape(potential.shape)
        )
    new_gating = gate_flat.reshape(gating.shape)

    rim_width = REACH + 1
    extended = rim_plane(potential[0], rim_width)
    distinct_second = lax.axis_size("hy") * (second_len - 1) + 1
    target_first = epi_target // distinct_second
    target_second = epi_target % distinct_second
    place_first = ext_index(target_first, index_first * (first_len - 1), first_len, rim_width)
    place_second = ext_index(target_second, index_second * (second_len - 1), second_len, rim_width)
    shift_first = place_first - rim_width - jnp.arange(first_len)[:, None]
    shift_second = place_second - rim_width - jnp.arange(second_len)[None, :]
    picked_values = jnp.zeros((first_len, second_len), jnp.float32)
    for step_first in range(-rim_width, rim_width + 1):
        rows = extended[rim_width + step_first : rim_width + step_first + first_len]
        along = jnp.zeros((first_len, second_len), jnp.float32)
        for step_second in range(-rim_width, rim_width + 1):
            window = rows[:, rim_width + step_second : rim_width + step_second + second_len]
            along = jnp.where(shift_second == step_second, window, along)
        picked_values = jnp.where(shift_first == step_first, along, picked_values)
    plane = jnp.where(index_torso == 0, picked_values, 0.0)
    rhs = jnp.concatenate(
        [plane[None], jnp.zeros((torso_len - 1, first_len, second_len), jnp.float32)], 0
    )

    mass_shift = torso_shift * torso_mass
    weighted_mass = torso_weight * mass_shift
    zero_lanes = 0.0 * torso_weight[0, 0]

    def exchange(residual, extra):
        local = local_products(residual, torso_cond, mats)
        terms = [
            torso_weight * residual * residual,
            residual * local + weighted_mass * residual * residual,
        ] + extra(local)
        partial = jnp.sum(jnp.sum(jnp.stack(terms), axis=(1, 2)), axis=1)
        summed, sums = face_sums(local, partial)
        return summed + mass_shift * residual, sums[:, None] + zero_lanes[None, :]

    image, sums = exchange(rhs, lambda local: [])
    norm_now = sums[0]
    curvature = sums[1]
    step_size = norm_now / curvature
    solution = step_size * rhs
    direction = rhs
    residual = rhs - step_size * image

    def later_turn(turn_index, state_tuple):
        solution, residual, direction, image, norm_now, curvature = state_tuple
        s_image, sums = exchange(
            residual,
            lambda local: [
                torso_weight * residual * image,
                direction * local + weighted_mass * direction * residual,
            ],
        )
        norm_next = sums[0]
        ratio = norm_next / norm_now
        curvature = sums[1] + ratio * (sums[2] + sums[3]) + ratio * ratio * curvature
        direction = residual + ratio * direction
        image = s_image + ratio * image
        step_size = norm_next / curvature
        solution = solution + step_size * direction
        residual = residual - step_size * image
        return (solution, residual, direction, image, norm_next, curvature)

    state = (solution, residual, direction, image, norm_now, curvature)
    solution = lax.fori_loop(1, ITERS, later_turn, state)[0]
    return (potential, new_gating, solution)


def solution(mesh):
    placed = (
        P("torso", "hx", "hy"),
        P(None, "torso", "hx", "hy"),
        P("torso", "hx", "hy"),
        P("torso", "hx", "hy"),
        P(),
        P(),
        P(),
        P(),
        P(),
        P(),
        P("torso", "hx", "hy"),
        P("torso", "hx", "hy"),
        P("hx", "hy"),
    )
    return jax.shard_map(
        per_device,
        mesh=mesh,
        in_specs=placed,
        out_specs=(P("torso", "hx", "hy"), P(None, "torso", "hx", "hy"), P("torso", "hx", "hy")),
        check_vma=False,
    )
```

```python
import jax
import jax.numpy as jnp
import numpy as np
from jax import lax
from jax.sharding import PartitionSpec as P

TYPES = 3
CLASSES = 4
STEPS = 2
ITERS = 4
REACH = 2


STIFF_LINE = (
    np.array(
        [
            [148.0, -189.0, 54.0, -13.0],
            [-189.0, 432.0, -297.0, 54.0],
            [54.0, -297.0, 432.0, -189.0],
            [-13.0, 54.0, -189.0, 148.0],
        ]
    )
    / 40.0
)
MASS_LINE = (
    np.array(
        [
            [128.0, 99.0, -36.0, 19.0],
            [99.0, 648.0, -81.0, -36.0],
            [-36.0, -81.0, 648.0, 99.0],
            [19.0, -36.0, 99.0, 128.0],
        ]
    )
    / 1680.0
)
time_step = 0.002
torso_shift = 0.02
HIGH = lax.Precision.HIGHEST


def gather_matrix(length, line):
    elements = (length - 1) // 3
    shape = (length, 4, elements)
    node = lax.broadcasted_iota(jnp.int32, shape, 0)
    offset = lax.broadcasted_iota(jnp.int32, shape, 1)
    local = node - 3 * lax.broadcasted_iota(jnp.int32, shape, 2)
    out = jnp.zeros(shape, jnp.float32)
    for a in range(4):
        for j in range(4):
            if line[a, j] != 0.0:
                out = jnp.where((offset == a) & (local == j), jnp.float32(line[a, j]), out)
    return out.reshape(length, 4 * elements)


def element_matrices(first, second):
    return dict(
        pick_mass=gather_matrix(first, MASS_LINE).T,
        pick_stiff=gather_matrix(first, STIFF_LINE).T,
        lanes_m=gather_matrix(second, MASS_LINE),
        lanes_k=gather_matrix(second, STIFF_LINE),
        scatter_second=gather_matrix(second, np.eye(4)).T,
        scatter_first=gather_matrix(first, np.eye(4)),
    )


def local_products(values, conduct, mats):
    depth, first, second = values.shape
    first_el, second_el = conduct.shape[1], conduct.shape[2]
    mass_d = [[float(MASS_LINE[i, j]) for j in range(4)] for i in range(4)]
    stiff_d = [[float(STIFF_LINE[i, j]) for j in range(4)] for i in range(4)]
    rows = [values[j] for j in range(depth)]
    v_mass = jnp.stack([sum(mass_d[i][j] * rows[j] for j in range(4)) for i in range(4)])
    v_stiff = jnp.stack([sum(stiff_d[i][j] * rows[j] for j in range(4)) for i in range(4)])
    pick_mass = mats["pick_mass"]
    pick_stiff = mats["pick_stiff"]
    along_first_m = jnp.einsum("kx,dxy->dky", pick_mass, v_mass, precision=HIGH)
    along_first_k = jnp.einsum("kx,dxy->dky", pick_stiff, v_mass, precision=HIGH) + jnp.einsum(
        "kx,dxy->dky", pick_mass, v_stiff, precision=HIGH
    )
    lanes_m = mats["lanes_m"]
    lanes_k = mats["lanes_k"]
    flat_m = along_first_m.reshape(-1, second)
    flat_k = along_first_k.reshape(-1, second)
    element = jnp.dot(flat_m, lanes_k, precision=HIGH) + jnp.dot(flat_k, lanes_m, precision=HIGH)
    element = element.reshape(depth, 4, first_el, 4, second_el) * conduct.reshape(
        1, 1, first_el, 1, second_el
    )
    scatter_second = mats["scatter_second"]
    spread = jnp.dot(element.reshape(-1, 4 * second_el), scatter_second, precision=HIGH)
    spread = spread.reshape(depth, 4 * first_el, second)
    scatter_first = mats["scatter_first"]
    return jnp.einsum("xk,dky->dxy", scatter_first, spread, precision=HIGH)


def plane_exchange(pieces, width, scalars, tie=None):
    count_x, count_y = lax.axis_size("hx"), lax.axis_size("hy")
    me_x, me_y = lax.axis_index("hx"), lax.axis_index("hy")
    rows = []
    for code in range(9):
        offset = (code // 3 - 1, code % 3 - 1)
        piece = pieces.get(offset)
        row = jnp.zeros((width,), jnp.float32) if piece is None else jnp.pad(piece, (0, width - piece.shape[0]))
        if scalars is not None:
            row = jnp.concatenate([row, scalars])
        rows.append(row)
    table = jnp.stack(rows)
    peers = jnp.arange(count_x * count_y, dtype=jnp.int32)
    off_x = peers // count_y - me_x
    off_y = peers % count_y - me_y
    near = (jnp.abs(off_x) <= 1) & (jnp.abs(off_y) <= 1)
    code_of = jnp.where(near, (off_x + 1) * 3 + (off_y + 1), 4)
    send = jnp.broadcast_to(table[4][None, :], (count_x * count_y, table.shape[1]))
    for code in range(9):
        if code != 4:
            send = jnp.where(code_of[:, None] == code, table[code][None, :], send)
    if tie is not None:
        send, tie = lax.optimization_barrier((send, tie))
    got = lax.all_to_all(send, ("hx", "hy"), 0, 0, tiled=True)
    received = {}
    for offset in pieces:
        src_x, src_y = me_x + offset[0], me_y + offset[1]
        valid = (src_x >= 0) & (src_x < count_x) & (src_y >= 0) & (src_y < count_y)
        src = jnp.clip(src_x, 0, count_x - 1) * count_y + jnp.clip(src_y, 0, count_y - 1)
        row = lax.dynamic_index_in_dim(got, src, 0, keepdims=False)
        received[offset] = jnp.where(valid, row[: pieces[offset].shape[0]], 0.0)
    total = None
    if scalars is not None:
        total = jnp.sum(got[:, width:], axis=0)
    return received, total, tie


def edge_pieces(plane):
    return {
        (1, 0): plane[-1, :],
        (-1, 0): plane[0, :],
        (0, 1): plane[:, -1],
        (0, -1): plane[:, 0],
        (1, 1): plane[-1, -1][None],
        (1, -1): plane[-1, 0][None],
        (-1, 1): plane[0, -1][None],
        (-1, -1): plane[0, 0][None],
    }


def rim_sum(got, depth, first, second):
    at_low = ((0, 0), (0, first - 1))
    at_high = ((0, 0), (first - 1, 0))
    low_second = got[(0, -1)].reshape(depth, first)
    low_second = low_second + jnp.pad(got[(-1, -1)].reshape(depth, 1), at_low)
    low_second = low_second + jnp.pad(got[(1, -1)].reshape(depth, 1), at_high)
    high_second = got[(0, 1)].reshape(depth, first)
    high_second = high_second + jnp.pad(got[(-1, 1)].reshape(depth, 1), at_low)
    high_second = high_second + jnp.pad(got[(1, 1)].reshape(depth, 1), at_high)
    along_first = jnp.pad(got[(-1, 0)].reshape(depth, 1, second), ((0, 0), (0, first - 1), (0, 0)))
    along_first = along_first + jnp.pad(
        got[(1, 0)].reshape(depth, 1, second), ((0, 0), (first - 1, 0), (0, 0))
    )
    along_second = jnp.pad(low_second[:, :, None], ((0, 0), (0, 0), (0, second - 1)))
    along_second = along_second + jnp.pad(
        high_second[:, :, None], ((0, 0), (0, 0), (second - 1, 0))
    )
    return along_first + along_second


def face_sums(values, scalars=None, tie=None):
    depth, first, second = values.shape
    count_t, count_x, count_y = lax.axis_size("torso"), lax.axis_size("hx"), lax.axis_size("hy")
    if count_t != 2:
        raise NotImplementedError("torso size")
    me_t, me_x, me_y = lax.axis_index("torso"), lax.axis_index("hx"), lax.axis_index("hy")
    my_face = jnp.where(me_t == 0, values[-1], values[0])
    got_face = lax.ppermute(my_face, "torso", [(0, 1), (1, 0)])
    width = depth * second
    in_plane = {
        (1, 0): values[:, -1, :].reshape(-1),
        (-1, 0): values[:, 0, :].reshape(-1),
        (0, 1): values[:, :, -1].reshape(-1),
        (0, -1): values[:, :, 0].reshape(-1),
        (1, 1): values[:, -1, -1],
        (1, -1): values[:, -1, 0],
        (-1, 1): values[:, 0, -1],
        (-1, -1): values[:, 0, 0],
    }
    across = edge_pieces(my_face)
    rows = []
    for code in range(27):
        off_t, off_x, off_y = code // 9 - 1, code // 3 % 3 - 1, code % 3 - 1
        if off_t == 0:
            piece = in_plane.get((off_x, off_y))
        else:
            piece = across.get((off_x, off_y))
        row = jnp.zeros((width,), jnp.float32) if piece is None else jnp.pad(piece, (0, width - piece.shape[0]))
        if scalars is not None:
            row = jnp.concatenate([row, scalars])
        rows.append(row)
    peers = jnp.arange(count_t * count_x * count_y, dtype=jnp.int32)
    peer_t = peers % count_t
    peer_x = peers // (count_t * count_y)
    peer_y = peers // count_t % count_y
    off_t, off_x, off_y = peer_t - me_t, peer_x - me_x, peer_y - me_y
    near = (jnp.abs(off_x) <= 1) & (jnp.abs(off_y) <= 1)
    code_of = jnp.where(near, (off_t + 1) * 9 + (off_x + 1) * 3 + (off_y + 1), 13)
    send = jnp.broadcast_to(rows[13][None, :], (peers.shape[0], rows[13].shape[0]))
    for code in range(27):
        if code != 13:
            send = jnp.where(code_of[:, None] == code, rows[code][None, :], send)
    if tie is not None:
        send, tie = lax.optimization_barrier((send, tie))
    got = lax.all_to_all(send, ("hx", "hy", "torso"), 0, 0, tiled=True)

    def received(offset, length, torso_of):
        src_x, src_y = me_x + offset[0], me_y + offset[1]
        valid = (src_x >= 0) & (src_x < count_x) & (src_y >= 0) & (src_y < count_y)
        src = (jnp.clip(src_x, 0, count_x - 1) * count_y + jnp.clip(src_y, 0, count_y - 1)) * count_t + torso_of
        row = lax.dynamic_index_in_dim(got, src, 0, keepdims=False)
        return jnp.where(valid, row[:length], 0.0)

    got_in = {o: received(o, p.shape[0], me_t) for o, p in in_plane.items()}
    got_across = {o: received(o, p.shape[0], 1 - me_t) for o, p in across.items()}
    summed = values + rim_sum(got_in, depth, first, second)
    face_term = got_face + rim_sum(got_across, 1, first, second)[0]
    depth_index = lax.broadcasted_iota(jnp.int32, (depth, 1, 1), 0)
    face_at = jnp.where(me_t == 0, depth - 1, 0)
    summed = summed + jnp.where(depth_index == face_at, face_term[None], 0.0)
    total = None
    if scalars is not None:
        total = jnp.sum(got[:, width:], axis=0)
    if tie is None:
        return summed, total
    return summed, total, tie


def rim_plane(plane, rim):
    first, second = plane.shape
    pieces = {
        (1, 0): plane[-rim:, :].reshape(-1),
        (-1, 0): plane[:rim, :].reshape(-1),
        (0, 1): plane[:, -rim:].reshape(-1),
        (0, -1): plane[:, :rim].reshape(-1),
        (1, 1): plane[-rim:, -rim:].reshape(-1),
        (1, -1): plane[-rim:, :rim].reshape(-1),
        (-1, 1): plane[:rim, -rim:].reshape(-1),
        (-1, -1): plane[:rim, :rim].reshape(-1),
    }
    got, _, _ = plane_exchange(pieces, rim * second, None)
    top = jnp.concatenate(
        [got[(-1, -1)].reshape(rim, rim), got[(-1, 0)].reshape(rim, second), got[(-1, 1)].reshape(rim, rim)], 1
    )
    middle = jnp.concatenate(
        [got[(0, -1)].reshape(first, rim), plane, got[(0, 1)].reshape(first, rim)], 1
    )
    bottom = jnp.concatenate(
        [got[(1, -1)].reshape(rim, rim), got[(1, 0)].reshape(rim, second), got[(1, 1)].reshape(rim, rim)], 1
    )
    return jnp.concatenate([top, middle, bottom], 0)


def line_factors(length, block_id, block_count):
    position = jnp.arange(length)
    at_start = (position == 0) & (block_id == 0)
    at_end = (position == length - 1) & (block_id == block_count - 1)
    mass_line = jnp.where(position % 3 == 0, jnp.where(at_start | at_end, 0.125, 0.25), 0.375)
    shared = (position == 0) & (block_id > 0) | (position == length - 1) & (
        block_id < block_count - 1
    )
    weight = jnp.where(shared, 0.5, 1.0)
    return (mass_line.astype(jnp.float32), weight.astype(jnp.float32))


def factor_grid(depth_line, first_line, second_line):
    return depth_line[:, None, None] * first_line[None, :, None] * second_line[None, None, :]


def node_table(matrix, labels, kind_count):
    out = matrix[kind_count - 1][:, None]
    for kind in range(kind_count - 2, -1, -1):
        out = jnp.where(labels == kind, matrix[kind][:, None], out)
    return out


def ext_index(target, anchor, length_local, rim_width):
    relative = target - anchor
    return jnp.where(
        relative < 0,
        rim_width - 1 + relative,
        jnp.where(relative > length_local - 1, rim_width + relative + 1, rim_width + relative),
    )


def per_device(
    potential,
    gating,
    cell_type,
    drug_class,
    half_point,
    gate_slope,
    time_const,
    max_conduct,
    reversal,
    drug_block,
    heart_cond,
    torso_cond,
    epi_target,
):
    depth_len, first_len, second_len = potential.shape
    torso_len = 3 * torso_cond.shape[0] + 1
    index_torso = lax.axis_index("torso")
    index_first = lax.axis_index("hx")
    index_second = lax.axis_index("hy")
    heart_depth, unused_depth = line_factors(depth_len, index_torso, lax.axis_size("torso"))
    first_mass, first_weight = line_factors(first_len, index_first, lax.axis_size("hx"))
    second_mass, second_weight = line_factors(second_len, index_second, lax.axis_size("hy"))
    torso_depth, torso_depth_weight = line_factors(torso_len, index_torso, lax.axis_size("torso"))
    heart_mass = factor_grid(heart_depth, first_mass, second_mass)
    torso_mass = factor_grid(torso_depth, first_mass, second_mass)
    torso_weight = factor_grid(torso_depth_weight, first_weight, second_weight)
    type_flat = cell_type.reshape(1, -1)
    class_flat = drug_class.reshape(1, -1)
    half_nodes = node_table(half_point, type_flat, TYPES)
    slope_nodes = node_table(gate_slope, type_flat, TYPES)
    decay_nodes = node_table(jnp.exp(-time_step / time_const), type_flat, TYPES)
    cond_nodes = node_table(max_conduct, type_flat, TYPES) * node_table(
        drug_block, class_flat, CLASSES
    )
    gate_flat = gating.reshape(gating.shape[0], -1)
    mats = element_matrices(first_len, second_len)
    for repeat in range(STEPS):
        diffusion, _, tied = face_sums(local_products(potential, heart_cond, mats), tie=potential)
        volts = tied.reshape(1, -1)
        inf_value = jax.nn.sigmoid((volts - half_nodes) * slope_nodes)
        gate_flat = inf_value + (gate_flat - inf_value) * decay_nodes
        current = jnp.sum(cond_nodes * gate_flat * (volts - reversal[:, None]), 0)
        potential = potential - time_step * (
            diffusion / heart_mass + current.reshape(potential.shape)
        )
    new_gating = gate_flat.reshape(gating.shape)

    rim_width = REACH + 1
    extended = rim_plane(potential[0], rim_width)
    distinct_second = lax.axis_size("hy") * (second_len - 1) + 1
    target_first = epi_target // distinct_second
    target_second = epi_target % distinct_second
    place_first = ext_index(target_first, index_first * (first_len - 1), first_len, rim_width)
    place_second = ext_index(target_second, index_second * (second_len - 1), second_len, rim_width)
    shift_first = place_first - rim_width - jnp.arange(first_len)[:, None]
    shift_second = place_second - rim_width - jnp.arange(second_len)[None, :]
    picked_values = jnp.zeros((first_len, second_len), jnp.float32)
    for step_first in range(-rim_width, rim_width + 1):
        rows = extended[rim_width + step_first : rim_width + step_first + first_len]
        along = jnp.zeros((first_len, second_len), jnp.float32)
        for step_second in range(-rim_width, rim_width + 1):
            window = rows[:, rim_width + step_second : rim_width + step_second + second_len]
            along = jnp.where(shift_second == step_second, window, along)
        picked_values = jnp.where(shift_first == step_first, along, picked_values)
    plane = jnp.where(index_torso == 0, picked_values, 0.0)
    rhs = jnp.concatenate(
        [plane[None], jnp.zeros((torso_len - 1, first_len, second_len), jnp.float32)], 0
    )

    mass_shift = torso_shift * torso_mass
    weighted_mass = torso_weight * mass_shift
    zero_lanes = 0.0 * torso_weight[0, 0]

    def exchange(residual, extra):
        local = local_products(residual, torso_cond, mats)
        terms = [
            torso_weight * residual * residual,
            residual * local + weighted_mass * residual * residual,
        ] + extra(local)
        partial = jnp.sum(jnp.sum(jnp.stack(terms), axis=(1, 2)), axis=1)
        summed, sums = face_sums(local, partial)
        return summed + mass_shift * residual, sums[:, None] + zero_lanes[None, :]

    image, sums = exchange(rhs, lambda local: [])
    norm_now = sums[0]
    curvature = sums[1]
    step_size = norm_now / curvature
    solution = step_size * rhs
    direction = rhs
    residual = rhs - step_size * image

    def later_turn(turn_index, state_tuple):
        solution, residual, direction, image, norm_now, curvature = state_tuple
        s_image, sums = exchange(
            residual,
            lambda local: [
                torso_weight * residual * image,
                direction * local + weighted_mass * direction * residual,
            ],
        )
        norm_next = sums[0]
        ratio = norm_next / norm_now
        curvature = sums[1] + ratio * (sums[2] + sums[3]) + ratio * ratio * curvature
        direction = residual + ratio * direction
        image = s_image + ratio * image
        step_size = norm_next / curvature
        solution = solution + step_size * direction
        residual = residual - step_size * image
        return (solution, residual, direction, image, norm_next, curvature)

    state = (solution, residual, direction, image, norm_now, curvature)
    solution = lax.fori_loop(1, ITERS, later_turn, state)[0]
    return (potential, new_gating, solution)


def solution(mesh):
    placed = (
        P("torso", "hx", "hy"),
        P(None, "torso", "hx", "hy"),
        P("torso", "hx", "hy"),
        P("torso", "hx", "hy"),
        P(),
        P(),
        P(),
        P(),
        P(),
        P(),
        P("torso", "hx", "hy"),
        P("torso", "hx", "hy"),
        P("hx", "hy"),
    )
    return jax.shard_map(
        per_device,
        mesh=mesh,
        in_specs=placed,
        out_specs=(P("torso", "hx", "hy"), P(None, "torso", "hx", "hy"), P("torso", "hx", "hy")),
        check_vma=False,
    )
```

```python
import jax
import jax.numpy as jnp
import numpy as np
from jax import lax
from jax.sharding import PartitionSpec as P

TYPES = 3
CLASSES = 4
STEPS = 2
ITERS = 4
REACH = 2


STIFF_LINE = (
    np.array(
        [
            [148.0, -189.0, 54.0, -13.0],
            [-189.0, 432.0, -297.0, 54.0],
            [54.0, -297.0, 432.0, -189.0],
            [-13.0, 54.0, -189.0, 148.0],
        ]
    )
    / 40.0
)
MASS_LINE = (
    np.array(
        [
            [128.0, 99.0, -36.0, 19.0],
            [99.0, 648.0, -81.0, -36.0],
            [-36.0, -81.0, 648.0, 99.0],
            [19.0, -36.0, 99.0, 128.0],
        ]
    )
    / 1680.0
)
time_step = 0.002
torso_shift = 0.02
HIGH = lax.Precision.HIGHEST


def gather_matrix(length, line):
    elements = (length - 1) // 3
    shape = (length, 4, elements)
    node = lax.broadcasted_iota(jnp.int32, shape, 0)
    offset = lax.broadcasted_iota(jnp.int32, shape, 1)
    local = node - 3 * lax.broadcasted_iota(jnp.int32, shape, 2)
    out = jnp.zeros(shape, jnp.float32)
    for a in range(4):
        for j in range(4):
            if line[a, j] != 0.0:
                out = jnp.where((offset == a) & (local == j), jnp.float32(line[a, j]), out)
    return out.reshape(length, 4 * elements)


def element_matrices(first, second):
    return dict(
        pick_mass=gather_matrix(first, MASS_LINE).T,
        pick_stiff=gather_matrix(first, STIFF_LINE).T,
        lanes=jnp.concatenate([gather_matrix(second, STIFF_LINE), gather_matrix(second, MASS_LINE)], 0),
        scatter_second=gather_matrix(second, np.eye(4)).T,
        scatter_first=gather_matrix(first, np.eye(4)),
    )


def local_products(values, conduct, mats):
    depth, first, second = values.shape
    first_el, second_el = conduct.shape[1], conduct.shape[2]
    mass_d = [[float(MASS_LINE[i, j]) for j in range(4)] for i in range(4)]
    stiff_d = [[float(STIFF_LINE[i, j]) for j in range(4)] for i in range(4)]
    rows = [values[j] for j in range(depth)]
    v_mass = jnp.stack([sum(mass_d[i][j] * rows[j] for j in range(4)) for i in range(4)])
    v_stiff = jnp.stack([sum(stiff_d[i][j] * rows[j] for j in range(4)) for i in range(4)])
    pick_mass = mats["pick_mass"]
    pick_stiff = mats["pick_stiff"]
    along_first_m = jnp.einsum("kx,dxy->dky", pick_mass, v_mass, precision=HIGH)
    along_first_k = jnp.einsum("kx,dxy->dky", pick_stiff, v_mass, precision=HIGH) + jnp.einsum(
        "kx,dxy->dky", pick_mass, v_stiff, precision=HIGH
    )
    flat = jnp.concatenate([along_first_m.reshape(-1, second), along_first_k.reshape(-1, second)], 1)
    element = jnp.dot(flat, mats["lanes"], precision=HIGH)
    element = element.reshape(depth, 4, first_el, 4, second_el) * conduct.reshape(
        1, 1, first_el, 1, second_el
    )
    scatter_second = mats["scatter_second"]
    spread = jnp.dot(element.reshape(-1, 4 * second_el), scatter_second, precision=HIGH)
    spread = spread.reshape(depth, 4 * first_el, second)
    scatter_first = mats["scatter_first"]
    return jnp.einsum("xk,dky->dxy", scatter_first, spread, precision=HIGH)


def torso_stage(values, scalars):
    count = lax.axis_size("torso")
    if count == 1:
        return values, scalars
    if count != 2:
        raise NotImplementedError("torso size")
    me = lax.axis_index("torso")
    face = jnp.where(me == 0, values[-1], values[0])
    extra = None
    if scalars is not None:
        extra = jnp.pad(scalars, (0, values.shape[2] - scalars.shape[0]))[None, :]
        face = jnp.concatenate([face, extra], 0)
    got = lax.ppermute(face, "torso", [(0, 1), (1, 0)])
    rows = values.shape[1]
    got_face = got[:rows]
    values = values.at[-1].add(jnp.where(me == 0, got_face, 0.0))
    values = values.at[0].add(jnp.where(me == 1, got_face, 0.0))
    if scalars is not None:
        scalars = scalars + got[rows, : scalars.shape[0]]
    return values, scalars


def plane_exchange(pieces, width, scalars, tie=None):
    count_x, count_y = lax.axis_size("hx"), lax.axis_size("hy")
    me_x, me_y = lax.axis_index("hx"), lax.axis_index("hy")
    rows = []
    for code in range(9):
        offset = (code // 3 - 1, code % 3 - 1)
        piece = pieces.get(offset)
        row = jnp.zeros((width,), jnp.float32) if piece is None else jnp.pad(piece, (0, width - piece.shape[0]))
        if scalars is not None:
            row = jnp.concatenate([row, scalars])
        rows.append(row)
    table = jnp.stack(rows)
    peers = jnp.arange(count_x * count_y, dtype=jnp.int32)
    off_x = peers // count_y - me_x
    off_y = peers % count_y - me_y
    near = (jnp.abs(off_x) <= 1) & (jnp.abs(off_y) <= 1)
    code_of = jnp.where(near, (off_x + 1) * 3 + (off_y + 1), 4)
    send = jnp.broadcast_to(table[4][None, :], (count_x * count_y, table.shape[1]))
    for code in range(9):
        if code != 4:
            send = jnp.where(code_of[:, None] == code, table[code][None, :], send)
    if tie is not None:
        send, tie = lax.optimization_barrier((send, tie))
    got = lax.all_to_all(send, ("hx", "hy"), 0, 0, tiled=True)
    received = {}
    for offset in pieces:
        src_x, src_y = me_x + offset[0], me_y + offset[1]
        valid = (src_x >= 0) & (src_x < count_x) & (src_y >= 0) & (src_y < count_y)
        src = jnp.clip(src_x, 0, count_x - 1) * count_y + jnp.clip(src_y, 0, count_y - 1)
        row = lax.dynamic_index_in_dim(got, src, 0, keepdims=False)
        received[offset] = jnp.where(valid, row[: pieces[offset].shape[0]], 0.0)
    total = None
    if scalars is not None:
        total = jnp.sum(got[:, width:], axis=0)
    return received, total, tie


def face_sums(values, scalars=None, tie=None):
    values, scalars = torso_stage(values, scalars)
    depth, first, second = values.shape
    pieces = {
        (1, 0): values[:, -1, :].reshape(-1),
        (-1, 0): values[:, 0, :].reshape(-1),
        (0, 1): values[:, :, -1].reshape(-1),
        (0, -1): values[:, :, 0].reshape(-1),
        (1, 1): values[:, -1, -1],
        (1, -1): values[:, -1, 0],
        (-1, 1): values[:, 0, -1],
        (-1, -1): values[:, 0, 0],
    }
    got, total, tie = plane_exchange(pieces, depth * second, scalars, tie)
    at_low = ((0, 0), (0, first - 1))
    at_high = ((0, 0), (first - 1, 0))
    low_second = got[(0, -1)].reshape(depth, first)
    low_second = low_second + jnp.pad(got[(-1, -1)][:, None], at_low)
    low_second = low_second + jnp.pad(got[(1, -1)][:, None], at_high)
    high_second = got[(0, 1)].reshape(depth, first)
    high_second = high_second + jnp.pad(got[(-1, 1)][:, None], at_low)
    high_second = high_second + jnp.pad(got[(1, 1)][:, None], at_high)
    along_first = jnp.pad(got[(-1, 0)].reshape(depth, 1, second), ((0, 0), (0, first - 1), (0, 0)))
    along_first = along_first + jnp.pad(
        got[(1, 0)].reshape(depth, 1, second), ((0, 0), (first - 1, 0), (0, 0))
    )
    along_second = jnp.pad(low_second[:, :, None], ((0, 0), (0, 0), (0, second - 1)))
    along_second = along_second + jnp.pad(
        high_second[:, :, None], ((0, 0), (0, 0), (second - 1, 0))
    )
    summed = values + along_first + along_second
    if tie is None:
        return summed, total
    return summed, total, tie


def rim_plane(plane, rim):
    first, second = plane.shape
    pieces = {
        (1, 0): plane[-rim:, :].reshape(-1),
        (-1, 0): plane[:rim, :].reshape(-1),
        (0, 1): plane[:, -rim:].reshape(-1),
        (0, -1): plane[:, :rim].reshape(-1),
        (1, 1): plane[-rim:, -rim:].reshape(-1),
        (1, -1): plane[-rim:, :rim].reshape(-1),
        (-1, 1): plane[:rim, -rim:].reshape(-1),
        (-1, -1): plane[:rim, :rim].reshape(-1),
    }
    got, _, _ = plane_exchange(pieces, rim * second, None)
    top = jnp.concatenate(
        [got[(-1, -1)].reshape(rim, rim), got[(-1, 0)].reshape(rim, second), got[(-1, 1)].reshape(rim, rim)], 1
    )
    middle = jnp.concatenate(
        [got[(0, -1)].reshape(first, rim), plane, got[(0, 1)].reshape(first, rim)], 1
    )
    bottom = jnp.concatenate(
        [got[(1, -1)].reshape(rim, rim), got[(1, 0)].reshape(rim, second), got[(1, 1)].reshape(rim, rim)], 1
    )
    return jnp.concatenate([top, middle, bottom], 0)


def line_factors(length, block_id, block_count):
    position = jnp.arange(length)
    at_start = (position == 0) & (block_id == 0)
    at_end = (position == length - 1) & (block_id == block_count - 1)
    mass_line = jnp.where(position % 3 == 0, jnp.where(at_start | at_end, 0.125, 0.25), 0.375)
    shared = (position == 0) & (block_id > 0) | (position == length - 1) & (
        block_id < block_count - 1
    )
    weight = jnp.where(shared, 0.5, 1.0)
    return (mass_line.astype(jnp.float32), weight.astype(jnp.float32))


def factor_grid(depth_line, first_line, second_line):
    return depth_line[:, None, None] * first_line[None, :, None] * second_line[None, None, :]


def node_table(matrix, labels, kind_count):
    out = matrix[kind_count - 1][:, None]
    for kind in range(kind_count - 2, -1, -1):
        out = jnp.where(labels == kind, matrix[kind][:, None], out)
    return out


def ext_index(target, anchor, length_local, rim_width):
    relative = target - anchor
    return jnp.where(
        relative < 0,
        rim_width - 1 + relative,
        jnp.where(relative > length_local - 1, rim_width + relative + 1, rim_width + relative),
    )


def per_device(
    potential,
    gating,
    cell_type,
    drug_class,
    half_point,
    gate_slope,
    time_const,
    max_conduct,
    reversal,
    drug_block,
    heart_cond,
    torso_cond,
    epi_target,
):
    depth_len, first_len, second_len = potential.shape
    torso_len = 3 * torso_cond.shape[0] + 1
    index_torso = lax.axis_index("torso")
    index_first = lax.axis_index("hx")
    index_second = lax.axis_index("hy")
    heart_depth, unused_depth = line_factors(depth_len, index_torso, lax.axis_size("torso"))
    first_mass, first_weight = line_factors(first_len, index_first, lax.axis_size("hx"))
    second_mass, second_weight = line_factors(second_len, index_second, lax.axis_size("hy"))
    torso_depth, torso_depth_weight = line_factors(torso_len, index_torso, lax.axis_size("torso"))
    heart_mass = factor_grid(heart_depth, first_mass, second_mass)
    torso_mass = factor_grid(torso_depth, first_mass, second_mass)
    torso_weight = factor_grid(torso_depth_weight, first_weight, second_weight)
    type_flat = cell_type.reshape(1, -1)
    class_flat = drug_class.reshape(1, -1)
    half_nodes = node_table(half_point, type_flat, TYPES)
    slope_nodes = node_table(gate_slope, type_flat, TYPES)
    decay_nodes = node_table(jnp.exp(-time_step / time_const), type_flat, TYPES)
    cond_nodes = node_table(max_conduct, type_flat, TYPES) * node_table(
        drug_block, class_flat, CLASSES
    )
    gate_flat = gating.reshape(gating.shape[0], -1)
    mats = element_matrices(first_len, second_len)
    for repeat in range(STEPS):
        diffusion, _, tied = face_sums(local_products(potential, heart_cond, mats), tie=potential)
        volts = tied.reshape(1, -1)
        inf_value = jax.nn.sigmoid((volts - half_nodes) * slope_nodes)
        gate_flat = inf_value + (gate_flat - inf_value) * decay_nodes
        current = jnp.sum(cond_nodes * gate_flat * (volts - reversal[:, None]), 0)
        potential = potential - time_step * (
            diffusion / heart_mass + current.reshape(potential.shape)
        )
    new_gating = gate_flat.reshape(gating.shape)

    rim_width = REACH + 1
    extended = rim_plane(potential[0], rim_width)
    distinct_second = lax.axis_size("hy") * (second_len - 1) + 1
    target_first = epi_target // distinct_second
    target_second = epi_target % distinct_second
    place_first = ext_index(target_first, index_first * (first_len - 1), first_len, rim_width)
    place_second = ext_index(target_second, index_second * (second_len - 1), second_len, rim_width)
    shift_first = place_first - rim_width - jnp.arange(first_len)[:, None]
    shift_second = place_second - rim_width - jnp.arange(second_len)[None, :]
    picked_values = jnp.zeros((first_len, second_len), jnp.float32)
    for step_first in range(-rim_width, rim_width + 1):
        rows = extended[rim_width + step_first : rim_width + step_first + first_len]
        along = jnp.zeros((first_len, second_len), jnp.float32)
        for step_second in range(-rim_width, rim_width + 1):
            window = rows[:, rim_width + step_second : rim_width + step_second + second_len]
            along = jnp.where(shift_second == step_second, window, along)
        picked_values = jnp.where(shift_first == step_first, along, picked_values)
    plane = jnp.where(index_torso == 0, picked_values, 0.0)
    rhs = jnp.concatenate(
        [plane[None], jnp.zeros((torso_len - 1, first_len, second_len), jnp.float32)], 0
    )

    mass_shift = torso_shift * torso_mass
    weighted_mass = torso_weight * mass_shift
    zero_lanes = 0.0 * torso_weight[0, 0]

    def exchange(residual, extra):
        local = local_products(residual, torso_cond, mats)
        terms = [
            torso_weight * residual * residual,
            residual * local + weighted_mass * residual * residual,
        ] + extra(local)
        partial = jnp.sum(jnp.sum(jnp.stack(terms), axis=(1, 2)), axis=1)
        summed, sums = face_sums(local, partial)
        return summed + mass_shift * residual, sums[:, None] + zero_lanes[None, :]

    image, sums = exchange(rhs, lambda local: [])
    norm_now = sums[0]
    curvature = sums[1]
    step_size = norm_now / curvature
    solution = step_size * rhs
    direction = rhs
    residual = rhs - step_size * image

    def later_turn(turn_index, state_tuple):
        solution, residual, direction, image, norm_now, curvature = state_tuple
        s_image, sums = exchange(
            residual,
            lambda local: [
                torso_weight * residual * image,
                direction * local + weighted_mass * direction * residual,
            ],
        )
        norm_next = sums[0]
        ratio = norm_next / norm_now
        curvature = sums[1] + ratio * (sums[2] + sums[3]) + ratio * ratio * curvature
        direction = residual + ratio * direction
        image = s_image + ratio * image
        step_size = norm_next / curvature
        solution = solution + step_size * direction
        residual = residual - step_size * image
        return (solution, residual, direction, image, norm_next, curvature)

    state = (solution, residual, direction, image, norm_now, curvature)
    solution = lax.fori_loop(1, ITERS, later_turn, state)[0]
    return (potential, new_gating, solution)


def solution(mesh):
    placed = (
        P("torso", "hx", "hy"),
        P(None, "torso", "hx", "hy"),
        P("torso", "hx", "hy"),
        P("torso", "hx", "hy"),
        P(),
        P(),
        P(),
        P(),
        P(),
        P(),
        P("torso", "hx", "hy"),
        P("torso", "hx", "hy"),
        P("hx", "hy"),
    )
    return jax.shard_map(
        per_device,
        mesh=mesh,
        in_specs=placed,
        out_specs=(P("torso", "hx", "hy"), P(None, "torso", "hx", "hy"), P("torso", "hx", "hy")),
        check_vma=False,
    )
```

```python
import jax
import jax.numpy as jnp
import numpy as np
from jax import lax
from jax.sharding import PartitionSpec as P

TYPES = 3
CLASSES = 4
STEPS = 2
ITERS = 4
REACH = 2


STIFF_LINE = (
    np.array(
        [
            [148.0, -189.0, 54.0, -13.0],
            [-189.0, 432.0, -297.0, 54.0],
            [54.0, -297.0, 432.0, -189.0],
            [-13.0, 54.0, -189.0, 148.0],
        ]
    )
    / 40.0
)
MASS_LINE = (
    np.array(
        [
            [128.0, 99.0, -36.0, 19.0],
            [99.0, 648.0, -81.0, -36.0],
            [-36.0, -81.0, 648.0, 99.0],
            [19.0, -36.0, 99.0, 128.0],
        ]
    )
    / 1680.0
)
time_step = 0.002
torso_shift = 0.02
HIGH = lax.Precision.HIGHEST


def gather_matrix(length, line):
    elements = (length - 1) // 3
    shape = (length, 4, elements)
    node = lax.broadcasted_iota(jnp.int32, shape, 0)
    offset = lax.broadcasted_iota(jnp.int32, shape, 1)
    local = node - 3 * lax.broadcasted_iota(jnp.int32, shape, 2)
    out = jnp.zeros(shape, jnp.float32)
    for a in range(4):
        for j in range(4):
            if line[a, j] != 0.0:
                out = jnp.where((offset == a) & (local == j), jnp.float32(line[a, j]), out)
    return out.reshape(length, 4 * elements)


def element_matrices(first, second):
    return dict(
        pick_mass=gather_matrix(first, MASS_LINE).T,
        pick_stiff=gather_matrix(first, STIFF_LINE).T,
        lanes_k=gather_matrix(second, STIFF_LINE),
        lanes_m=gather_matrix(second, MASS_LINE),
        scatter_second=gather_matrix(second, np.eye(4)).T,
        scatter_first=gather_matrix(first, np.eye(4)),
    )


def local_products(values, conduct, mats, merged=False):
    depth, first, second = values.shape
    first_el, second_el = conduct.shape[1], conduct.shape[2]
    mass_d = [[float(MASS_LINE[i, j]) for j in range(4)] for i in range(4)]
    stiff_d = [[float(STIFF_LINE[i, j]) for j in range(4)] for i in range(4)]
    rows = [values[j] for j in range(depth)]
    v_mass = jnp.stack([sum(mass_d[i][j] * rows[j] for j in range(4)) for i in range(4)])
    v_stiff = jnp.stack([sum(stiff_d[i][j] * rows[j] for j in range(4)) for i in range(4)])
    pick_mass = mats["pick_mass"]
    pick_stiff = mats["pick_stiff"]
    along_first_m = jnp.einsum("kx,dxy->dky", pick_mass, v_mass, precision=HIGH)
    along_first_k = jnp.einsum("kx,dxy->dky", pick_stiff, v_mass, precision=HIGH) + jnp.einsum(
        "kx,dxy->dky", pick_mass, v_stiff, precision=HIGH
    )
    flat_m = along_first_m.reshape(-1, second)
    flat_k = along_first_k.reshape(-1, second)
    if merged:
        lanes = jnp.concatenate([mats["lanes_k"], mats["lanes_m"]], 0)
        element = jnp.dot(jnp.concatenate([flat_m, flat_k], 1), lanes, precision=HIGH)
    else:
        element = jnp.dot(flat_m, mats["lanes_k"], precision=HIGH) + jnp.dot(
            flat_k, mats["lanes_m"], precision=HIGH
        )
    element = element.reshape(depth, 4, first_el, 4, second_el) * conduct.reshape(
        1, 1, first_el, 1, second_el
    )
    scatter_second = mats["scatter_second"]
    spread = jnp.dot(element.reshape(-1, 4 * second_el), scatter_second, precision=HIGH)
    spread = spread.reshape(depth, 4 * first_el, second)
    scatter_first = mats["scatter_first"]
    return jnp.einsum("xk,dky->dxy", scatter_first, spread, precision=HIGH)


def torso_stage(values, scalars):
    count = lax.axis_size("torso")
    if count == 1:
        return values, scalars
    if count != 2:
        raise NotImplementedError("torso size")
    me = lax.axis_index("torso")
    face = jnp.where(me == 0, values[-1], values[0])
    extra = None
    if scalars is not None:
        extra = jnp.pad(scalars, (0, values.shape[2] - scalars.shape[0]))[None, :]
        face = jnp.concatenate([face, extra], 0)
    got = lax.ppermute(face, "torso", [(0, 1), (1, 0)])
    rows = values.shape[1]
    got_face = got[:rows]
    values = values.at[-1].add(jnp.where(me == 0, got_face, 0.0))
    values = values.at[0].add(jnp.where(me == 1, got_face, 0.0))
    if scalars is not None:
        scalars = scalars + got[rows, : scalars.shape[0]]
    return values, scalars


def plane_exchange(pieces, width, scalars, tie=None):
    count_x, count_y = lax.axis_size("hx"), lax.axis_size("hy")
    me_x, me_y = lax.axis_index("hx"), lax.axis_index("hy")
    rows = []
    for code in range(9):
        offset = (code // 3 - 1, code % 3 - 1)
        piece = pieces.get(offset)
        row = jnp.zeros((width,), jnp.float32) if piece is None else jnp.pad(piece, (0, width - piece.shape[0]))
        if scalars is not None:
            row = jnp.concatenate([row, scalars])
        rows.append(row)
    table = jnp.stack(rows)
    peers = jnp.arange(count_x * count_y, dtype=jnp.int32)
    off_x = peers // count_y - me_x
    off_y = peers % count_y - me_y
    near = (jnp.abs(off_x) <= 1) & (jnp.abs(off_y) <= 1)
    code_of = jnp.where(near, (off_x + 1) * 3 + (off_y + 1), 4)
    send = jnp.broadcast_to(table[4][None, :], (count_x * count_y, table.shape[1]))
    for code in range(9):
        if code != 4:
            send = jnp.where(code_of[:, None] == code, table[code][None, :], send)
    if tie is not None:
        send, tie = lax.optimization_barrier((send, tie))
    got = lax.all_to_all(send, ("hx", "hy"), 0, 0, tiled=True)
    received = {}
    for offset in pieces:
        src_x, src_y = me_x + offset[0], me_y + offset[1]
        valid = (src_x >= 0) & (src_x < count_x) & (src_y >= 0) & (src_y < count_y)
        src = jnp.clip(src_x, 0, count_x - 1) * count_y + jnp.clip(src_y, 0, count_y - 1)
        row = lax.dynamic_index_in_dim(got, src, 0, keepdims=False)
        received[offset] = jnp.where(valid, row[: pieces[offset].shape[0]], 0.0)
    total = None
    if scalars is not None:
        total = jnp.sum(got[:, width:], axis=0)
    return received, total, tie


def face_sums(values, scalars=None, tie=None):
    values, scalars = torso_stage(values, scalars)
    depth, first, second = values.shape
    pieces = {
        (1, 0): values[:, -1, :].reshape(-1),
        (-1, 0): values[:, 0, :].reshape(-1),
        (0, 1): values[:, :, -1].reshape(-1),
        (0, -1): values[:, :, 0].reshape(-1),
        (1, 1): values[:, -1, -1],
        (1, -1): values[:, -1, 0],
        (-1, 1): values[:, 0, -1],
        (-1, -1): values[:, 0, 0],
    }
    got, total, tie = plane_exchange(pieces, depth * second, scalars, tie)
    at_low = ((0, 0), (0, first - 1))
    at_high = ((0, 0), (first - 1, 0))
    low_second = got[(0, -1)].reshape(depth, first)
    low_second = low_second + jnp.pad(got[(-1, -1)][:, None], at_low)
    low_second = low_second + jnp.pad(got[(1, -1)][:, None], at_high)
    high_second = got[(0, 1)].reshape(depth, first)
    high_second = high_second + jnp.pad(got[(-1, 1)][:, None], at_low)
    high_second = high_second + jnp.pad(got[(1, 1)][:, None], at_high)
    along_first = jnp.pad(got[(-1, 0)].reshape(depth, 1, second), ((0, 0), (0, first - 1), (0, 0)))
    along_first = along_first + jnp.pad(
        got[(1, 0)].reshape(depth, 1, second), ((0, 0), (first - 1, 0), (0, 0))
    )
    along_second = jnp.pad(low_second[:, :, None], ((0, 0), (0, 0), (0, second - 1)))
    along_second = along_second + jnp.pad(
        high_second[:, :, None], ((0, 0), (0, 0), (second - 1, 0))
    )
    summed = values + along_first + along_second
    if tie is None:
        return summed, total
    return summed, total, tie


def rim_plane(plane, rim):
    first, second = plane.shape
    pieces = {
        (1, 0): plane[-rim:, :].reshape(-1),
        (-1, 0): plane[:rim, :].reshape(-1),
        (0, 1): plane[:, -rim:].reshape(-1),
        (0, -1): plane[:, :rim].reshape(-1),
        (1, 1): plane[-rim:, -rim:].reshape(-1),
        (1, -1): plane[-rim:, :rim].reshape(-1),
        (-1, 1): plane[:rim, -rim:].reshape(-1),
        (-1, -1): plane[:rim, :rim].reshape(-1),
    }
    got, _, _ = plane_exchange(pieces, rim * second, None)
    top = jnp.concatenate(
        [got[(-1, -1)].reshape(rim, rim), got[(-1, 0)].reshape(rim, second), got[(-1, 1)].reshape(rim, rim)], 1
    )
    middle = jnp.concatenate(
        [got[(0, -1)].reshape(first, rim), plane, got[(0, 1)].reshape(first, rim)], 1
    )
    bottom = jnp.concatenate(
        [got[(1, -1)].reshape(rim, rim), got[(1, 0)].reshape(rim, second), got[(1, 1)].reshape(rim, rim)], 1
    )
    return jnp.concatenate([top, middle, bottom], 0)


def line_factors(length, block_id, block_count):
    position = jnp.arange(length)
    at_start = (position == 0) & (block_id == 0)
    at_end = (position == length - 1) & (block_id == block_count - 1)
    mass_line = jnp.where(position % 3 == 0, jnp.where(at_start | at_end, 0.125, 0.25), 0.375)
    shared = (position == 0) & (block_id > 0) | (position == length - 1) & (
        block_id < block_count - 1
    )
    weight = jnp.where(shared, 0.5, 1.0)
    return (mass_line.astype(jnp.float32), weight.astype(jnp.float32))


def factor_grid(depth_line, first_line, second_line):
    return depth_line[:, None, None] * first_line[None, :, None] * second_line[None, None, :]


def node_table(matrix, labels, kind_count):
    out = matrix[kind_count - 1][:, None]
    for kind in range(kind_count - 2, -1, -1):
        out = jnp.where(labels == kind, matrix[kind][:, None], out)
    return out


def ext_index(target, anchor, length_local, rim_width):
    relative = target - anchor
    return jnp.where(
        relative < 0,
        rim_width - 1 + relative,
        jnp.where(relative > length_local - 1, rim_width + relative + 1, rim_width + relative),
    )


def per_device(
    potential,
    gating,
    cell_type,
    drug_class,
    half_point,
    gate_slope,
    time_const,
    max_conduct,
    reversal,
    drug_block,
    heart_cond,
    torso_cond,
    epi_target,
):
    depth_len, first_len, second_len = potential.shape
    torso_len = 3 * torso_cond.shape[0] + 1
    index_torso = lax.axis_index("torso")
    index_first = lax.axis_index("hx")
    index_second = lax.axis_index("hy")
    heart_depth, unused_depth = line_factors(depth_len, index_torso, lax.axis_size("torso"))
    first_mass, first_weight = line_factors(first_len, index_first, lax.axis_size("hx"))
    second_mass, second_weight = line_factors(second_len, index_second, lax.axis_size("hy"))
    torso_depth, torso_depth_weight = line_factors(torso_len, index_torso, lax.axis_size("torso"))
    heart_mass = factor_grid(heart_depth, first_mass, second_mass)
    torso_mass = factor_grid(torso_depth, first_mass, second_mass)
    torso_weight = factor_grid(torso_depth_weight, first_weight, second_weight)
    type_flat = cell_type.reshape(1, -1)
    class_flat = drug_class.reshape(1, -1)
    half_nodes = node_table(half_point, type_flat, TYPES)
    slope_nodes = node_table(gate_slope, type_flat, TYPES)
    decay_nodes = node_table(jnp.exp(-time_step / time_const), type_flat, TYPES)
    cond_nodes = node_table(max_conduct, type_flat, TYPES) * node_table(
        drug_block, class_flat, CLASSES
    )
    gate_flat = gating.reshape(gating.shape[0], -1)
    mats = element_matrices(first_len, second_len)
    for repeat in range(STEPS):
        diffusion, _, tied = face_sums(local_products(potential, heart_cond, mats), tie=potential)
        volts = tied.reshape(1, -1)
        inf_value = jax.nn.sigmoid((volts - half_nodes) * slope_nodes)
        gate_flat = inf_value + (gate_flat - inf_value) * decay_nodes
        current = jnp.sum(cond_nodes * gate_flat * (volts - reversal[:, None]), 0)
        potential = potential - time_step * (
            diffusion / heart_mass + current.reshape(potential.shape)
        )
    new_gating = gate_flat.reshape(gating.shape)

    rim_width = REACH + 1
    extended = rim_plane(potential[0], rim_width)
    distinct_second = lax.axis_size("hy") * (second_len - 1) + 1
    target_first = epi_target // distinct_second
    target_second = epi_target % distinct_second
    place_first = ext_index(target_first, index_first * (first_len - 1), first_len, rim_width)
    place_second = ext_index(target_second, index_second * (second_len - 1), second_len, rim_width)
    shift_first = place_first - rim_width - jnp.arange(first_len)[:, None]
    shift_second = place_second - rim_width - jnp.arange(second_len)[None, :]
    picked_values = jnp.zeros((first_len, second_len), jnp.float32)
    for step_first in range(-rim_width, rim_width + 1):
        rows = extended[rim_width + step_first : rim_width + step_first + first_len]
        along = jnp.zeros((first_len, second_len), jnp.float32)
        for step_second in range(-rim_width, rim_width + 1):
            window = rows[:, rim_width + step_second : rim_width + step_second + second_len]
            along = jnp.where(shift_second == step_second, window, along)
        picked_values = jnp.where(shift_first == step_first, along, picked_values)
    plane = jnp.where(index_torso == 0, picked_values, 0.0)
    rhs = jnp.concatenate(
        [plane[None], jnp.zeros((torso_len - 1, first_len, second_len), jnp.float32)], 0
    )

    mass_shift = torso_shift * torso_mass
    weighted_mass = torso_weight * mass_shift
    zero_lanes = 0.0 * torso_weight[0, 0]

    def exchange(residual, extra):
        local = local_products(residual, torso_cond, mats, merged=True)
        terms = [
            torso_weight * residual * residual,
            residual * local + weighted_mass * residual * residual,
        ] + extra(local)
        partial = jnp.sum(jnp.sum(jnp.stack(terms), axis=(1, 2)), axis=1)
        summed, sums = face_sums(local, partial)
        return summed + mass_shift * residual, sums[:, None] + zero_lanes[None, :]

    image, sums = exchange(rhs, lambda local: [])
    norm_now = sums[0]
    curvature = sums[1]
    step_size = norm_now / curvature
    solution = step_size * rhs
    direction = rhs
    residual = rhs - step_size * image

    def later_turn(turn_index, state_tuple):
        solution, residual, direction, image, norm_now, curvature = state_tuple
        s_image, sums = exchange(
            residual,
            lambda local: [
                torso_weight * residual * image,
                direction * local + weighted_mass * direction * residual,
            ],
        )
        norm_next = sums[0]
        ratio = norm_next / norm_now
        curvature = sums[1] + ratio * (sums[2] + sums[3]) + ratio * ratio * curvature
        direction = residual + ratio * direction
        image = s_image + ratio * image
        step_size = norm_next / curvature
        solution = solution + step_size * direction
        residual = residual - step_size * image
        return (solution, residual, direction, image, norm_next, curvature)

    state = (solution, residual, direction, image, norm_now, curvature)
    solution = lax.fori_loop(1, ITERS, later_turn, state)[0]
    return (potential, new_gating, solution)


def solution(mesh):
    placed = (
        P("torso", "hx", "hy"),
        P(None, "torso", "hx", "hy"),
        P("torso", "hx", "hy"),
        P("torso", "hx", "hy"),
        P(),
        P(),
        P(),
        P(),
        P(),
        P(),
        P("torso", "hx", "hy"),
        P("torso", "hx", "hy"),
        P("hx", "hy"),
    )
    return jax.shard_map(
        per_device,
        mesh=mesh,
        in_specs=placed,
        out_specs=(P("torso", "hx", "hy"), P(None, "torso", "hx", "hy"), P("torso", "hx", "hy")),
        check_vma=False,
    )
```

```python
import jax
import jax.numpy as jnp
import numpy as np
from jax import lax
from jax.sharding import PartitionSpec as P

TYPES = 3
CLASSES = 4
STEPS = 2
ITERS = 4
REACH = 2


STIFF_LINE = (
    np.array(
        [
            [148.0, -189.0, 54.0, -13.0],
            [-189.0, 432.0, -297.0, 54.0],
            [54.0, -297.0, 432.0, -189.0],
            [-13.0, 54.0, -189.0, 148.0],
        ]
    )
    / 40.0
)
MASS_LINE = (
    np.array(
        [
            [128.0, 99.0, -36.0, 19.0],
            [99.0, 648.0, -81.0, -36.0],
            [-36.0, -81.0, 648.0, 99.0],
            [19.0, -36.0, 99.0, 128.0],
        ]
    )
    / 1680.0
)
time_step = 0.002
torso_shift = 0.02
HIGH = lax.Precision.HIGHEST


def gather_matrix(length, line):
    elements = (length - 1) // 3
    shape = (length, 4, elements)
    node = lax.broadcasted_iota(jnp.int32, shape, 0)
    offset = lax.broadcasted_iota(jnp.int32, shape, 1)
    local = node - 3 * lax.broadcasted_iota(jnp.int32, shape, 2)
    out = jnp.zeros(shape, jnp.float32)
    for a in range(4):
        for j in range(4):
            if line[a, j] != 0.0:
                out = jnp.where((offset == a) & (local == j), jnp.float32(line[a, j]), out)
    return out.reshape(length, 4 * elements)


def element_matrices(first, second):
    return dict(
        pick_mass=gather_matrix(first, MASS_LINE).T,
        pick_stiff=gather_matrix(first, STIFF_LINE).T,
        lanes_k=gather_matrix(second, STIFF_LINE),
        lanes_m=gather_matrix(second, MASS_LINE),
        lanes=jnp.stack([gather_matrix(second, STIFF_LINE), gather_matrix(second, MASS_LINE)]).reshape(
            2 * second, -1
        ),
        scatter_second=gather_matrix(second, np.eye(4)).T,
        scatter_first=gather_matrix(first, np.eye(4)),
    )


def local_products(values, conduct, mats, merged=False):
    depth, first, second = values.shape
    first_el, second_el = conduct.shape[1], conduct.shape[2]
    mass_d = [[float(MASS_LINE[i, j]) for j in range(4)] for i in range(4)]
    stiff_d = [[float(STIFF_LINE[i, j]) for j in range(4)] for i in range(4)]
    rows = [values[j] for j in range(depth)]
    v_mass = jnp.stack([sum(mass_d[i][j] * rows[j] for j in range(4)) for i in range(4)])
    v_stiff = jnp.stack([sum(stiff_d[i][j] * rows[j] for j in range(4)) for i in range(4)])
    pick_mass = mats["pick_mass"]
    pick_stiff = mats["pick_stiff"]
    along_first_m = jnp.einsum("kx,dxy->dky", pick_mass, v_mass, precision=HIGH)
    along_first_k = jnp.einsum("kx,dxy->dky", pick_stiff, v_mass, precision=HIGH) + jnp.einsum(
        "kx,dxy->dky", pick_mass, v_stiff, precision=HIGH
    )
    flat_m = along_first_m.reshape(-1, second)
    flat_k = along_first_k.reshape(-1, second)
    if merged:
        element = jnp.dot(jnp.concatenate([flat_m, flat_k], 1), mats["lanes"], precision=HIGH)
    else:
        element = jnp.dot(flat_m, mats["lanes_k"], precision=HIGH) + jnp.dot(
            flat_k, mats["lanes_m"], precision=HIGH
        )
    element = element.reshape(depth, 4, first_el, 4, second_el) * conduct.reshape(
        1, 1, first_el, 1, second_el
    )
    scatter_second = mats["scatter_second"]
    spread = jnp.dot(element.reshape(-1, 4 * second_el), scatter_second, precision=HIGH)
    spread = spread.reshape(depth, 4 * first_el, second)
    scatter_first = mats["scatter_first"]
    return jnp.einsum("xk,dky->dxy", scatter_first, spread, precision=HIGH)


def torso_stage(values, scalars):
    count = lax.axis_size("torso")
    if count == 1:
        return values, scalars
    if count != 2:
        raise NotImplementedError("torso size")
    me = lax.axis_index("torso")
    face = jnp.where(me == 0, values[-1], values[0])
    extra = None
    if scalars is not None:
        extra = jnp.pad(scalars, (0, values.shape[2] - scalars.shape[0]))[None, :]
        face = jnp.concatenate([face, extra], 0)
    got = lax.ppermute(face, "torso", [(0, 1), (1, 0)])
    rows = values.shape[1]
    got_face = got[:rows]
    values = values.at[-1].add(jnp.where(me == 0, got_face, 0.0))
    values = values.at[0].add(jnp.where(me == 1, got_face, 0.0))
    if scalars is not None:
        scalars = scalars + got[rows, : scalars.shape[0]]
    return values, scalars


def plane_exchange(pieces, width, scalars, tie=None):
    count_x, count_y = lax.axis_size("hx"), lax.axis_size("hy")
    me_x, me_y = lax.axis_index("hx"), lax.axis_index("hy")
    rows = []
    for code in range(9):
        offset = (code // 3 - 1, code % 3 - 1)
        piece = pieces.get(offset)
        row = jnp.zeros((width,), jnp.float32) if piece is None else jnp.pad(piece, (0, width - piece.shape[0]))
        if scalars is not None:
            row = jnp.concatenate([row, scalars])
        rows.append(row)
    table = jnp.stack(rows)
    peers = jnp.arange(count_x * count_y, dtype=jnp.int32)
    off_x = peers // count_y - me_x
    off_y = peers % count_y - me_y
    near = (jnp.abs(off_x) <= 1) & (jnp.abs(off_y) <= 1)
    code_of = jnp.where(near, (off_x + 1) * 3 + (off_y + 1), 4)
    send = jnp.broadcast_to(table[4][None, :], (count_x * count_y, table.shape[1]))
    for code in range(9):
        if code != 4:
            send = jnp.where(code_of[:, None] == code, table[code][None, :], send)
    if tie is not None:
        send, tie = lax.optimization_barrier((send, tie))
    got = lax.all_to_all(send, ("hx", "hy"), 0, 0, tiled=True)
    received = {}
    for offset in pieces:
        src_x, src_y = me_x + offset[0], me_y + offset[1]
        valid = (src_x >= 0) & (src_x < count_x) & (src_y >= 0) & (src_y < count_y)
        src = jnp.clip(src_x, 0, count_x - 1) * count_y + jnp.clip(src_y, 0, count_y - 1)
        row = lax.dynamic_index_in_dim(got, src, 0, keepdims=False)
        received[offset] = jnp.where(valid, row[: pieces[offset].shape[0]], 0.0)
    total = None
    if scalars is not None:
        total = jnp.sum(got[:, width:], axis=0)
    return received, total, tie


def face_sums(values, scalars=None, tie=None):
    values, scalars = torso_stage(values, scalars)
    depth, first, second = values.shape
    pieces = {
        (1, 0): values[:, -1, :].reshape(-1),
        (-1, 0): values[:, 0, :].reshape(-1),
        (0, 1): values[:, :, -1].reshape(-1),
        (0, -1): values[:, :, 0].reshape(-1),
        (1, 1): values[:, -1, -1],
        (1, -1): values[:, -1, 0],
        (-1, 1): values[:, 0, -1],
        (-1, -1): values[:, 0, 0],
    }
    got, total, tie = plane_exchange(pieces, depth * second, scalars, tie)
    at_low = ((0, 0), (0, first - 1))
    at_high = ((0, 0), (first - 1, 0))
    low_second = got[(0, -1)].reshape(depth, first)
    low_second = low_second + jnp.pad(got[(-1, -1)][:, None], at_low)
    low_second = low_second + jnp.pad(got[(1, -1)][:, None], at_high)
    high_second = got[(0, 1)].reshape(depth, first)
    high_second = high_second + jnp.pad(got[(-1, 1)][:, None], at_low)
    high_second = high_second + jnp.pad(got[(1, 1)][:, None], at_high)
    along_first = jnp.pad(got[(-1, 0)].reshape(depth, 1, second), ((0, 0), (0, first - 1), (0, 0)))
    along_first = along_first + jnp.pad(
        got[(1, 0)].reshape(depth, 1, second), ((0, 0), (first - 1, 0), (0, 0))
    )
    along_second = jnp.pad(low_second[:, :, None], ((0, 0), (0, 0), (0, second - 1)))
    along_second = along_second + jnp.pad(
        high_second[:, :, None], ((0, 0), (0, 0), (second - 1, 0))
    )
    summed = values + along_first + along_second
    if tie is None:
        return summed, total
    return summed, total, tie


def rim_plane(plane, rim):
    first, second = plane.shape
    pieces = {
        (1, 0): plane[-rim:, :].reshape(-1),
        (-1, 0): plane[:rim, :].reshape(-1),
        (0, 1): plane[:, -rim:].reshape(-1),
        (0, -1): plane[:, :rim].reshape(-1),
        (1, 1): plane[-rim:, -rim:].reshape(-1),
        (1, -1): plane[-rim:, :rim].reshape(-1),
        (-1, 1): plane[:rim, -rim:].reshape(-1),
        (-1, -1): plane[:rim, :rim].reshape(-1),
    }
    got, _, _ = plane_exchange(pieces, rim * second, None)
    top = jnp.concatenate(
        [got[(-1, -1)].reshape(rim, rim), got[(-1, 0)].reshape(rim, second), got[(-1, 1)].reshape(rim, rim)], 1
    )
    middle = jnp.concatenate(
        [got[(0, -1)].reshape(first, rim), plane, got[(0, 1)].reshape(first, rim)], 1
    )
    bottom = jnp.concatenate(
        [got[(1, -1)].reshape(rim, rim), got[(1, 0)].reshape(rim, second), got[(1, 1)].reshape(rim, rim)], 1
    )
    return jnp.concatenate([top, middle, bottom], 0)


def line_factors(length, block_id, block_count):
    position = jnp.arange(length)
    at_start = (position == 0) & (block_id == 0)
    at_end = (position == length - 1) & (block_id == block_count - 1)
    mass_line = jnp.where(position % 3 == 0, jnp.where(at_start | at_end, 0.125, 0.25), 0.375)
    shared = (position == 0) & (block_id > 0) | (position == length - 1) & (
        block_id < block_count - 1
    )
    weight = jnp.where(shared, 0.5, 1.0)
    return (mass_line.astype(jnp.float32), weight.astype(jnp.float32))


def factor_grid(depth_line, first_line, second_line):
    return depth_line[:, None, None] * first_line[None, :, None] * second_line[None, None, :]


def node_table(matrix, labels, kind_count):
    out = matrix[kind_count - 1][:, None]
    for kind in range(kind_count - 2, -1, -1):
        out = jnp.where(labels == kind, matrix[kind][:, None], out)
    return out


def ext_index(target, anchor, length_local, rim_width):
    relative = target - anchor
    return jnp.where(
        relative < 0,
        rim_width - 1 + relative,
        jnp.where(relative > length_local - 1, rim_width + relative + 1, rim_width + relative),
    )


def per_device(
    potential,
    gating,
    cell_type,
    drug_class,
    half_point,
    gate_slope,
    time_const,
    max_conduct,
    reversal,
    drug_block,
    heart_cond,
    torso_cond,
    epi_target,
):
    depth_len, first_len, second_len = potential.shape
    torso_len = 3 * torso_cond.shape[0] + 1
    index_torso = lax.axis_index("torso")
    index_first = lax.axis_index("hx")
    index_second = lax.axis_index("hy")
    heart_depth, unused_depth = line_factors(depth_len, index_torso, lax.axis_size("torso"))
    first_mass, first_weight = line_factors(first_len, index_first, lax.axis_size("hx"))
    second_mass, second_weight = line_factors(second_len, index_second, lax.axis_size("hy"))
    torso_depth, torso_depth_weight = line_factors(torso_len, index_torso, lax.axis_size("torso"))
    heart_mass = factor_grid(heart_depth, first_mass, second_mass)
    torso_mass = factor_grid(torso_depth, first_mass, second_mass)
    torso_weight = factor_grid(torso_depth_weight, first_weight, second_weight)
    type_flat = cell_type.reshape(1, -1)
    class_flat = drug_class.reshape(1, -1)
    half_nodes = node_table(half_point, type_flat, TYPES)
    slope_nodes = node_table(gate_slope, type_flat, TYPES)
    decay_nodes = node_table(jnp.exp(-time_step / time_const), type_flat, TYPES)
    cond_nodes = node_table(max_conduct, type_flat, TYPES) * node_table(
        drug_block, class_flat, CLASSES
    )
    gate_flat = gating.reshape(gating.shape[0], -1)
    mats = element_matrices(first_len, second_len)
    for repeat in range(STEPS):
        diffusion, _, tied = face_sums(local_products(potential, heart_cond, mats), tie=potential)
        volts = tied.reshape(1, -1)
        inf_value = jax.nn.sigmoid((volts - half_nodes) * slope_nodes)
        gate_flat = inf_value + (gate_flat - inf_value) * decay_nodes
        current = jnp.sum(cond_nodes * gate_flat * (volts - reversal[:, None]), 0)
        potential = potential - time_step * (
            diffusion / heart_mass + current.reshape(potential.shape)
        )
    new_gating = gate_flat.reshape(gating.shape)

    rim_width = REACH + 1
    extended = rim_plane(potential[0], rim_width)
    distinct_second = lax.axis_size("hy") * (second_len - 1) + 1
    target_first = epi_target // distinct_second
    target_second = epi_target % distinct_second
    place_first = ext_index(target_first, index_first * (first_len - 1), first_len, rim_width)
    place_second = ext_index(target_second, index_second * (second_len - 1), second_len, rim_width)
    shift_first = place_first - rim_width - jnp.arange(first_len)[:, None]
    shift_second = place_second - rim_width - jnp.arange(second_len)[None, :]
    picked_values = jnp.zeros((first_len, second_len), jnp.float32)
    for step_first in range(-rim_width, rim_width + 1):
        rows = extended[rim_width + step_first : rim_width + step_first + first_len]
        along = jnp.zeros((first_len, second_len), jnp.float32)
        for step_second in range(-rim_width, rim_width + 1):
            window = rows[:, rim_width + step_second : rim_width + step_second + second_len]
            along = jnp.where(shift_second == step_second, window, along)
        picked_values = jnp.where(shift_first == step_first, along, picked_values)
    plane = jnp.where(index_torso == 0, picked_values, 0.0)
    rhs = jnp.concatenate(
        [plane[None], jnp.zeros((torso_len - 1, first_len, second_len), jnp.float32)], 0
    )

    mass_shift = torso_shift * torso_mass
    weighted_mass = torso_weight * mass_shift
    zero_lanes = 0.0 * torso_weight[0, 0]

    def exchange(residual, extra):
        local = local_products(residual, torso_cond, mats, merged=True)
        terms = [
            torso_weight * residual * residual,
            residual * local + weighted_mass * residual * residual,
        ] + extra(local)
        partial = jnp.sum(jnp.sum(jnp.stack(terms), axis=(1, 2)), axis=1)
        summed, sums = face_sums(local, partial)
        return summed + mass_shift * residual, sums[:, None] + zero_lanes[None, :]

    image, sums = exchange(rhs, lambda local: [])
    norm_now = sums[0]
    curvature = sums[1]
    step_size = norm_now / curvature
    solution = step_size * rhs
    direction = rhs
    residual = rhs - step_size * image

    def later_turn(turn_index, state_tuple):
        solution, residual, direction, image, norm_now, curvature = state_tuple
        s_image, sums = exchange(
            residual,
            lambda local: [
                torso_weight * residual * image,
                direction * local + weighted_mass * direction * residual,
            ],
        )
        norm_next = sums[0]
        ratio = norm_next / norm_now
        curvature = sums[1] + ratio * (sums[2] + sums[3]) + ratio * ratio * curvature
        direction = residual + ratio * direction
        image = s_image + ratio * image
        step_size = norm_next / curvature
        solution = solution + step_size * direction
        residual = residual - step_size * image
        return (solution, residual, direction, image, norm_next, curvature)

    state = (solution, residual, direction, image, norm_now, curvature)
    solution = lax.fori_loop(1, ITERS, later_turn, state)[0]
    return (potential, new_gating, solution)


def solution(mesh):
    placed = (
        P("torso", "hx", "hy"),
        P(None, "torso", "hx", "hy"),
        P("torso", "hx", "hy"),
        P("torso", "hx", "hy"),
        P(),
        P(),
        P(),
        P(),
        P(),
        P(),
        P("torso", "hx", "hy"),
        P("torso", "hx", "hy"),
        P("hx", "hy"),
    )
    return jax.shard_map(
        per_device,
        mesh=mesh,
        in_specs=placed,
        out_specs=(P("torso", "hx", "hy"), P(None, "torso", "hx", "hy"), P("torso", "hx", "hy")),
        check_vma=False,
    )
```

```python
import jax
import jax.numpy as jnp
import numpy as np
from jax import lax
from jax.sharding import PartitionSpec as P

TYPES = 3
CLASSES = 4
STEPS = 2
ITERS = 4
REACH = 2


STIFF_LINE = (
    np.array(
        [
            [148.0, -189.0, 54.0, -13.0],
            [-189.0, 432.0, -297.0, 54.0],
            [54.0, -297.0, 432.0, -189.0],
            [-13.0, 54.0, -189.0, 148.0],
        ]
    )
    / 40.0
)
MASS_LINE = (
    np.array(
        [
            [128.0, 99.0, -36.0, 19.0],
            [99.0, 648.0, -81.0, -36.0],
            [-36.0, -81.0, 648.0, 99.0],
            [19.0, -36.0, 99.0, 128.0],
        ]
    )
    / 1680.0
)
time_step = 0.002
torso_shift = 0.02
HIGH = lax.Precision.HIGHEST


def gather_matrix(length, line):
    elements = (length - 1) // 3
    shape = (length, 4, elements)
    node = lax.broadcasted_iota(jnp.int32, shape, 0)
    offset = lax.broadcasted_iota(jnp.int32, shape, 1)
    local = node - 3 * lax.broadcasted_iota(jnp.int32, shape, 2)
    out = jnp.zeros(shape, jnp.float32)
    for a in range(4):
        for j in range(4):
            if line[a, j] != 0.0:
                out = jnp.where((offset == a) & (local == j), jnp.float32(line[a, j]), out)
    return out.reshape(length, 4 * elements)


def element_matrices(first, second):
    return dict(
        pick_mass=gather_matrix(first, MASS_LINE).T,
        pick_stiff=gather_matrix(first, STIFF_LINE).T,
        lanes_k=gather_matrix(second, STIFF_LINE),
        lanes_m=gather_matrix(second, MASS_LINE),
        lanes=jnp.stack([gather_matrix(second, STIFF_LINE), gather_matrix(second, MASS_LINE)]).reshape(
            2 * second, -1
        ),
        scatter_second=gather_matrix(second, np.eye(4)).T,
        scatter_first=gather_matrix(first, np.eye(4)),
    )


def local_products(values, conduct, mats, merged=False):
    depth, first, second = values.shape
    first_el, second_el = conduct.shape[1], conduct.shape[2]
    mass_d = [[float(MASS_LINE[i, j]) for j in range(4)] for i in range(4)]
    stiff_d = [[float(STIFF_LINE[i, j]) for j in range(4)] for i in range(4)]
    rows = [values[j] for j in range(depth)]
    v_mass = jnp.stack([sum(mass_d[i][j] * rows[j] for j in range(4)) for i in range(4)])
    v_stiff = jnp.stack([sum(stiff_d[i][j] * rows[j] for j in range(4)) for i in range(4)])
    pick_mass = mats["pick_mass"]
    pick_stiff = mats["pick_stiff"]
    along_first_m = jnp.einsum("kx,dxy->dky", pick_mass, v_mass, precision=HIGH)
    along_first_k = jnp.einsum("kx,dxy->dky", pick_stiff, v_mass, precision=HIGH) + jnp.einsum(
        "kx,dxy->dky", pick_mass, v_stiff, precision=HIGH
    )
    flat_m = along_first_m.reshape(-1, second)
    flat_k = along_first_k.reshape(-1, second)
    if merged:
        element = jnp.dot(jnp.concatenate([flat_m, flat_k], 1), mats["lanes"], precision=HIGH)
    else:
        element = jnp.dot(flat_m, mats["lanes_k"], precision=HIGH) + jnp.dot(
            flat_k, mats["lanes_m"], precision=HIGH
        )
    element = element.reshape(depth, 4, first_el, 4, second_el) * conduct.reshape(
        1, 1, first_el, 1, second_el
    )
    scatter_second = mats["scatter_second"]
    spread = jnp.dot(element.reshape(-1, 4 * second_el), scatter_second, precision=HIGH)
    spread = spread.reshape(depth, 4 * first_el, second)
    scatter_first = mats["scatter_first"]
    return jnp.einsum("xk,dky->dxy", scatter_first, spread, precision=HIGH)


def torso_stage(values, scalars):
    count = lax.axis_size("torso")
    if count == 1:
        return values, scalars
    if count != 2:
        raise NotImplementedError("torso size")
    me = lax.axis_index("torso")
    face = jnp.where(me == 0, values[-1], values[0])
    extra = None
    if scalars is not None:
        extra = jnp.pad(scalars, (0, values.shape[2] - scalars.shape[0]))[None, :]
        face = jnp.concatenate([face, extra], 0)
    got = lax.ppermute(face, "torso", [(0, 1), (1, 0)])
    rows = values.shape[1]
    got_face = got[:rows]
    values = values.at[-1].add(jnp.where(me == 0, got_face, 0.0))
    values = values.at[0].add(jnp.where(me == 1, got_face, 0.0))
    if scalars is not None:
        scalars = scalars + got[rows, : scalars.shape[0]]
    return values, scalars


def plane_exchange(pieces, width, scalars, tie=None):
    count_x, count_y = lax.axis_size("hx"), lax.axis_size("hy")
    me_x, me_y = lax.axis_index("hx"), lax.axis_index("hy")
    rows = []
    for code in range(9):
        offset = (code // 3 - 1, code % 3 - 1)
        piece = pieces.get(offset)
        row = jnp.zeros((width,), jnp.float32) if piece is None else jnp.pad(piece, (0, width - piece.shape[0]))
        if scalars is not None:
            row = jnp.concatenate([row, scalars])
        rows.append(row)
    table = jnp.stack(rows)
    peers = jnp.arange(count_x * count_y, dtype=jnp.int32)
    off_x = peers // count_y - me_x
    off_y = peers % count_y - me_y
    near = (jnp.abs(off_x) <= 1) & (jnp.abs(off_y) <= 1)
    code_of = jnp.where(near, (off_x + 1) * 3 + (off_y + 1), 4)
    send = jnp.broadcast_to(table[4][None, :], (count_x * count_y, table.shape[1]))
    for code in range(9):
        if code != 4:
            send = jnp.where(code_of[:, None] == code, table[code][None, :], send)
    if tie is not None:
        send, tie = lax.optimization_barrier((send, tie))
    got = lax.all_to_all(send, ("hx", "hy"), 0, 0, tiled=True)
    received = {}
    for offset in pieces:
        src_x, src_y = me_x + offset[0], me_y + offset[1]
        valid = (src_x >= 0) & (src_x < count_x) & (src_y >= 0) & (src_y < count_y)
        src = jnp.clip(src_x, 0, count_x - 1) * count_y + jnp.clip(src_y, 0, count_y - 1)
        row = lax.dynamic_index_in_dim(got, src, 0, keepdims=False)
        received[offset] = jnp.where(valid, row[: pieces[offset].shape[0]], 0.0)
    total = None
    if scalars is not None:
        total = jnp.sum(got[:, width:], axis=0)
    return received, total, tie


def face_sums(values, scalars=None, tie=None):
    values, scalars = torso_stage(values, scalars)
    depth, first, second = values.shape
    pieces = {
        (1, 0): values[:, -1, :].reshape(-1),
        (-1, 0): values[:, 0, :].reshape(-1),
        (0, 1): values[:, :, -1].reshape(-1),
        (0, -1): values[:, :, 0].reshape(-1),
        (1, 1): values[:, -1, -1],
        (1, -1): values[:, -1, 0],
        (-1, 1): values[:, 0, -1],
        (-1, -1): values[:, 0, 0],
    }
    got, total, tie = plane_exchange(pieces, depth * second, scalars, tie)
    at_low = ((0, 0), (0, first - 1))
    at_high = ((0, 0), (first - 1, 0))
    low_second = got[(0, -1)].reshape(depth, first)
    low_second = low_second + jnp.pad(got[(-1, -1)][:, None], at_low)
    low_second = low_second + jnp.pad(got[(1, -1)][:, None], at_high)
    high_second = got[(0, 1)].reshape(depth, first)
    high_second = high_second + jnp.pad(got[(-1, 1)][:, None], at_low)
    high_second = high_second + jnp.pad(got[(1, 1)][:, None], at_high)
    along_first = jnp.pad(got[(-1, 0)].reshape(depth, 1, second), ((0, 0), (0, first - 1), (0, 0)))
    along_first = along_first + jnp.pad(
        got[(1, 0)].reshape(depth, 1, second), ((0, 0), (first - 1, 0), (0, 0))
    )
    along_second = jnp.pad(low_second[:, :, None], ((0, 0), (0, 0), (0, second - 1)))
    along_second = along_second + jnp.pad(
        high_second[:, :, None], ((0, 0), (0, 0), (second - 1, 0))
    )
    summed = values + along_first + along_second
    if tie is None:
        return summed, total
    return summed, total, tie


def rim_plane(plane, rim):
    first, second = plane.shape
    pieces = {
        (1, 0): plane[-rim:, :].reshape(-1),
        (-1, 0): plane[:rim, :].reshape(-1),
        (0, 1): plane[:, -rim:].reshape(-1),
        (0, -1): plane[:, :rim].reshape(-1),
        (1, 1): plane[-rim:, -rim:].reshape(-1),
        (1, -1): plane[-rim:, :rim].reshape(-1),
        (-1, 1): plane[:rim, -rim:].reshape(-1),
        (-1, -1): plane[:rim, :rim].reshape(-1),
    }
    got, _, _ = plane_exchange(pieces, rim * second, None)
    top = jnp.concatenate(
        [got[(-1, -1)].reshape(rim, rim), got[(-1, 0)].reshape(rim, second), got[(-1, 1)].reshape(rim, rim)], 1
    )
    middle = jnp.concatenate(
        [got[(0, -1)].reshape(first, rim), plane, got[(0, 1)].reshape(first, rim)], 1
    )
    bottom = jnp.concatenate(
        [got[(1, -1)].reshape(rim, rim), got[(1, 0)].reshape(rim, second), got[(1, 1)].reshape(rim, rim)], 1
    )
    return jnp.concatenate([top, middle, bottom], 0)


def line_factors(length, block_id, block_count):
    position = jnp.arange(length)
    at_start = (position == 0) & (block_id == 0)
    at_end = (position == length - 1) & (block_id == block_count - 1)
    mass_line = jnp.where(position % 3 == 0, jnp.where(at_start | at_end, 0.125, 0.25), 0.375)
    shared = (position == 0) & (block_id > 0) | (position == length - 1) & (
        block_id < block_count - 1
    )
    weight = jnp.where(shared, 0.5, 1.0)
    return (mass_line.astype(jnp.float32), weight.astype(jnp.float32))


def factor_grid(depth_line, first_line, second_line):
    return depth_line[:, None, None] * first_line[None, :, None] * second_line[None, None, :]


def node_table(matrix, labels, kind_count):
    out = matrix[kind_count - 1][:, None]
    for kind in range(kind_count - 2, -1, -1):
        out = jnp.where(labels == kind, matrix[kind][:, None], out)
    return out


def ext_index(target, anchor, length_local, rim_width):
    relative = target - anchor
    return jnp.where(
        relative < 0,
        rim_width - 1 + relative,
        jnp.where(relative > length_local - 1, rim_width + relative + 1, rim_width + relative),
    )


def per_device(
    potential,
    gating,
    cell_type,
    drug_class,
    half_point,
    gate_slope,
    time_const,
    max_conduct,
    reversal,
    drug_block,
    heart_cond,
    torso_cond,
    epi_target,
):
    depth_len, first_len, second_len = potential.shape
    torso_len = 3 * torso_cond.shape[0] + 1
    index_torso = lax.axis_index("torso")
    index_first = lax.axis_index("hx")
    index_second = lax.axis_index("hy")
    heart_depth, unused_depth = line_factors(depth_len, index_torso, lax.axis_size("torso"))
    first_mass, first_weight = line_factors(first_len, index_first, lax.axis_size("hx"))
    second_mass, second_weight = line_factors(second_len, index_second, lax.axis_size("hy"))
    torso_depth, torso_depth_weight = line_factors(torso_len, index_torso, lax.axis_size("torso"))
    heart_mass = factor_grid(heart_depth, first_mass, second_mass)
    torso_mass = factor_grid(torso_depth, first_mass, second_mass)
    torso_weight = factor_grid(torso_depth_weight, first_weight, second_weight)
    type_flat = cell_type.reshape(1, -1)
    class_flat = drug_class.reshape(1, -1)
    half_nodes = node_table(half_point, type_flat, TYPES)
    slope_nodes = node_table(gate_slope, type_flat, TYPES)
    decay_nodes = node_table(jnp.exp(-time_step / time_const), type_flat, TYPES)
    cond_nodes = node_table(max_conduct, type_flat, TYPES) * node_table(
        drug_block, class_flat, CLASSES
    )
    gate_flat = gating.reshape(gating.shape[0], -1)
    mats = element_matrices(first_len, second_len)
    for repeat in range(STEPS):
        diffusion, _, tied = face_sums(local_products(potential, heart_cond, mats), tie=potential)
        volts = tied.reshape(1, -1)
        inf_value = jax.nn.sigmoid((volts - half_nodes) * slope_nodes)
        gate_flat = inf_value + (gate_flat - inf_value) * decay_nodes
        current = jnp.sum(cond_nodes * gate_flat * (volts - reversal[:, None]), 0)
        potential = potential - time_step * (
            diffusion / heart_mass + current.reshape(potential.shape)
        )
    new_gating = gate_flat.reshape(gating.shape)

    rim_width = REACH + 1
    extended = rim_plane(potential[0], rim_width)
    distinct_second = lax.axis_size("hy") * (second_len - 1) + 1
    target_first = epi_target // distinct_second
    target_second = epi_target % distinct_second
    place_first = ext_index(target_first, index_first * (first_len - 1), first_len, rim_width)
    place_second = ext_index(target_second, index_second * (second_len - 1), second_len, rim_width)
    shift_first = place_first - rim_width - jnp.arange(first_len)[:, None]
    shift_second = place_second - rim_width - jnp.arange(second_len)[None, :]
    picked_values = jnp.zeros((first_len, second_len), jnp.float32)
    for step_first in range(-rim_width, rim_width + 1):
        rows = extended[rim_width + step_first : rim_width + step_first + first_len]
        along = jnp.zeros((first_len, second_len), jnp.float32)
        for step_second in range(-rim_width, rim_width + 1):
            window = rows[:, rim_width + step_second : rim_width + step_second + second_len]
            along = jnp.where(shift_second == step_second, window, along)
        picked_values = jnp.where(shift_first == step_first, along, picked_values)
    plane = jnp.where(index_torso == 0, picked_values, 0.0)
    rhs = jnp.concatenate(
        [plane[None], jnp.zeros((torso_len - 1, first_len, second_len), jnp.float32)], 0
    )

    mass_shift = torso_shift * torso_mass
    weighted_mass = torso_weight * mass_shift
    zero_lanes = 0.0 * torso_weight[0, 0]

    def exchange(residual, extra):
        local = local_products(residual, torso_cond, mats, merged=True)
        terms = [
            torso_weight * residual * residual,
            residual * local + weighted_mass * residual * residual,
        ] + extra(local)
        partial = jnp.sum(jnp.sum(jnp.stack(terms), axis=(1, 2)), axis=1)
        summed, sums = face_sums(local, partial)
        return summed + mass_shift * residual, sums[:, None] + zero_lanes[None, :]

    image, sums = exchange(rhs, lambda local: [])
    norm_now = sums[0]
    curvature = sums[1]
    step_size = norm_now / curvature
    solution = step_size * rhs
    direction = rhs
    residual = rhs - step_size * image

    def later_turn(turn_index, state_tuple):
        solution, residual, direction, image, norm_now, curvature = state_tuple
        s_image, sums = exchange(
            residual,
            lambda local: [
                torso_weight * residual * image,
                direction * local + weighted_mass * direction * residual,
            ],
        )
        norm_next = sums[0]
        ratio = norm_next / norm_now
        curvature = sums[1] + ratio * (sums[2] + sums[3]) + ratio * ratio * curvature
        direction = residual + ratio * direction
        image = s_image + ratio * image
        step_size = norm_next / curvature
        solution = solution + step_size * direction
        residual = residual - step_size * image
        return (solution, residual, direction, image, norm_next, curvature)

    state = (solution, residual, direction, image, norm_now, curvature)
    for turn_index in range(1, ITERS):
        state = later_turn(turn_index, state)
    solution = state[0]
    return (potential, new_gating, solution)


def solution(mesh):
    placed = (
        P("torso", "hx", "hy"),
        P(None, "torso", "hx", "hy"),
        P("torso", "hx", "hy"),
        P("torso", "hx", "hy"),
        P(),
        P(),
        P(),
        P(),
        P(),
        P(),
        P("torso", "hx", "hy"),
        P("torso", "hx", "hy"),
        P("hx", "hy"),
    )
    return jax.shard_map(
        per_device,
        mesh=mesh,
        in_specs=placed,
        out_specs=(P("torso", "hx", "hy"), P(None, "torso", "hx", "hy"), P("torso", "hx", "hy")),
        check_vma=False,
    )
```

```python
import jax
import jax.numpy as jnp
import numpy as np
from jax import lax
from jax.sharding import PartitionSpec as P

TYPES = 3
CLASSES = 4
STEPS = 2
ITERS = 4
REACH = 2


STIFF_LINE = (
    np.array(
        [
            [148.0, -189.0, 54.0, -13.0],
            [-189.0, 432.0, -297.0, 54.0],
            [54.0, -297.0, 432.0, -189.0],
            [-13.0, 54.0, -189.0, 148.0],
        ]
    )
    / 40.0
)
MASS_LINE = (
    np.array(
        [
            [128.0, 99.0, -36.0, 19.0],
            [99.0, 648.0, -81.0, -36.0],
            [-36.0, -81.0, 648.0, 99.0],
            [19.0, -36.0, 99.0, 128.0],
        ]
    )
    / 1680.0
)
time_step = 0.002
torso_shift = 0.02
HIGH = lax.Precision.HIGHEST


def gather_matrix(length, line):
    elements = (length - 1) // 3
    shape = (length, 4, elements)
    node = lax.broadcasted_iota(jnp.int32, shape, 0)
    offset = lax.broadcasted_iota(jnp.int32, shape, 1)
    local = node - 3 * lax.broadcasted_iota(jnp.int32, shape, 2)
    out = jnp.zeros(shape, jnp.float32)
    for a in range(4):
        for j in range(4):
            if line[a, j] != 0.0:
                out = jnp.where((offset == a) & (local == j), jnp.float32(line[a, j]), out)
    return out.reshape(length, 4 * elements)


def element_matrices(first, second):
    return dict(
        pick_mass=gather_matrix(first, MASS_LINE).T,
        pick_stiff=gather_matrix(first, STIFF_LINE).T,
        pick_both=jnp.stack([gather_matrix(first, MASS_LINE).T, gather_matrix(first, STIFF_LINE).T]).reshape(
            -1, first
        ),
        lanes_k=gather_matrix(second, STIFF_LINE),
        lanes_m=gather_matrix(second, MASS_LINE),
        lanes=jnp.stack([gather_matrix(second, STIFF_LINE), gather_matrix(second, MASS_LINE)]).reshape(
            2 * second, -1
        ),
        scatter_second=gather_matrix(second, np.eye(4)).T,
        scatter_first=gather_matrix(first, np.eye(4)),
    )


def local_products(values, conduct, mats, merged=False):
    depth, first, second = values.shape
    first_el, second_el = conduct.shape[1], conduct.shape[2]
    mass_d = [[float(MASS_LINE[i, j]) for j in range(4)] for i in range(4)]
    stiff_d = [[float(STIFF_LINE[i, j]) for j in range(4)] for i in range(4)]
    rows = [values[j] for j in range(depth)]
    v_mass = jnp.stack([sum(mass_d[i][j] * rows[j] for j in range(4)) for i in range(4)])
    v_stiff = jnp.stack([sum(stiff_d[i][j] * rows[j] for j in range(4)) for i in range(4)])
    pick_mass = mats["pick_mass"]
    pick_stiff = mats["pick_stiff"]
    if merged:
        both = jnp.einsum("kx,dxy->dky", mats["pick_both"], v_mass, precision=HIGH)
        along_first_m = both[:, : pick_mass.shape[0]]
        along_first_k = both[:, pick_mass.shape[0] :] + jnp.einsum(
            "kx,dxy->dky", pick_mass, v_stiff, precision=HIGH
        )
    else:
        along_first_m = jnp.einsum("kx,dxy->dky", pick_mass, v_mass, precision=HIGH)
        along_first_k = jnp.einsum("kx,dxy->dky", pick_stiff, v_mass, precision=HIGH) + jnp.einsum(
            "kx,dxy->dky", pick_mass, v_stiff, precision=HIGH
        )
    flat_m = along_first_m.reshape(-1, second)
    flat_k = along_first_k.reshape(-1, second)
    if merged:
        element = jnp.dot(jnp.concatenate([flat_m, flat_k], 1), mats["lanes"], precision=HIGH)
    else:
        element = jnp.dot(flat_m, mats["lanes_k"], precision=HIGH) + jnp.dot(
            flat_k, mats["lanes_m"], precision=HIGH
        )
    element = element.reshape(depth, 4, first_el, 4, second_el) * conduct.reshape(
        1, 1, first_el, 1, second_el
    )
    scatter_second = mats["scatter_second"]
    spread = jnp.dot(element.reshape(-1, 4 * second_el), scatter_second, precision=HIGH)
    spread = spread.reshape(depth, 4 * first_el, second)
    scatter_first = mats["scatter_first"]
    return jnp.einsum("xk,dky->dxy", scatter_first, spread, precision=HIGH)


def torso_stage(values, scalars):
    count = lax.axis_size("torso")
    if count == 1:
        return values, scalars
    if count != 2:
        raise NotImplementedError("torso size")
    me = lax.axis_index("torso")
    face = jnp.where(me == 0, values[-1], values[0])
    extra = None
    if scalars is not None:
        extra = jnp.pad(scalars, (0, values.shape[2] - scalars.shape[0]))[None, :]
        face = jnp.concatenate([face, extra], 0)
    got = lax.ppermute(face, "torso", [(0, 1), (1, 0)])
    rows = values.shape[1]
    got_face = got[:rows]
    values = values.at[-1].add(jnp.where(me == 0, got_face, 0.0))
    values = values.at[0].add(jnp.where(me == 1, got_face, 0.0))
    if scalars is not None:
        scalars = scalars + got[rows, : scalars.shape[0]]
    return values, scalars


def plane_exchange(pieces, width, scalars, tie=None):
    count_x, count_y = lax.axis_size("hx"), lax.axis_size("hy")
    me_x, me_y = lax.axis_index("hx"), lax.axis_index("hy")
    rows = []
    for code in range(9):
        offset = (code // 3 - 1, code % 3 - 1)
        piece = pieces.get(offset)
        row = jnp.zeros((width,), jnp.float32) if piece is None else jnp.pad(piece, (0, width - piece.shape[0]))
        if scalars is not None:
            row = jnp.concatenate([row, scalars])
        rows.append(row)
    table = jnp.stack(rows)
    peers = jnp.arange(count_x * count_y, dtype=jnp.int32)
    off_x = peers // count_y - me_x
    off_y = peers % count_y - me_y
    near = (jnp.abs(off_x) <= 1) & (jnp.abs(off_y) <= 1)
    code_of = jnp.where(near, (off_x + 1) * 3 + (off_y + 1), 4)
    send = jnp.broadcast_to(table[4][None, :], (count_x * count_y, table.shape[1]))
    for code in range(9):
        if code != 4:
            send = jnp.where(code_of[:, None] == code, table[code][None, :], send)
    if tie is not None:
        send, tie = lax.optimization_barrier((send, tie))
    got = lax.all_to_all(send, ("hx", "hy"), 0, 0, tiled=True)
    received = {}
    for offset in pieces:
        src_x, src_y = me_x + offset[0], me_y + offset[1]
        valid = (src_x >= 0) & (src_x < count_x) & (src_y >= 0) & (src_y < count_y)
        src = jnp.clip(src_x, 0, count_x - 1) * count_y + jnp.clip(src_y, 0, count_y - 1)
        row = lax.dynamic_index_in_dim(got, src, 0, keepdims=False)
        received[offset] = jnp.where(valid, row[: pieces[offset].shape[0]], 0.0)
    total = None
    if scalars is not None:
        total = jnp.sum(got[:, width:], axis=0)
    return received, total, tie


def face_sums(values, scalars=None, tie=None):
    values, scalars = torso_stage(values, scalars)
    depth, first, second = values.shape
    pieces = {
        (1, 0): values[:, -1, :].reshape(-1),
        (-1, 0): values[:, 0, :].reshape(-1),
        (0, 1): values[:, :, -1].reshape(-1),
        (0, -1): values[:, :, 0].reshape(-1),
        (1, 1): values[:, -1, -1],
        (1, -1): values[:, -1, 0],
        (-1, 1): values[:, 0, -1],
        (-1, -1): values[:, 0, 0],
    }
    got, total, tie = plane_exchange(pieces, depth * second, scalars, tie)
    at_low = ((0, 0), (0, first - 1))
    at_high = ((0, 0), (first - 1, 0))
    low_second = got[(0, -1)].reshape(depth, first)
    low_second = low_second + jnp.pad(got[(-1, -1)][:, None], at_low)
    low_second = low_second + jnp.pad(got[(1, -1)][:, None], at_high)
    high_second = got[(0, 1)].reshape(depth, first)
    high_second = high_second + jnp.pad(got[(-1, 1)][:, None], at_low)
    high_second = high_second + jnp.pad(got[(1, 1)][:, None], at_high)
    along_first = jnp.pad(got[(-1, 0)].reshape(depth, 1, second), ((0, 0), (0, first - 1), (0, 0)))
    along_first = along_first + jnp.pad(
        got[(1, 0)].reshape(depth, 1, second), ((0, 0), (first - 1, 0), (0, 0))
    )
    along_second = jnp.pad(low_second[:, :, None], ((0, 0), (0, 0), (0, second - 1)))
    along_second = along_second + jnp.pad(
        high_second[:, :, None], ((0, 0), (0, 0), (second - 1, 0))
    )
    summed = values + along_first + along_second
    if tie is None:
        return summed, total
    return summed, total, tie


def rim_plane(plane, rim):
    first, second = plane.shape
    pieces = {
        (1, 0): plane[-rim:, :].reshape(-1),
        (-1, 0): plane[:rim, :].reshape(-1),
        (0, 1): plane[:, -rim:].reshape(-1),
        (0, -1): plane[:, :rim].reshape(-1),
        (1, 1): plane[-rim:, -rim:].reshape(-1),
        (1, -1): plane[-rim:, :rim].reshape(-1),
        (-1, 1): plane[:rim, -rim:].reshape(-1),
        (-1, -1): plane[:rim, :rim].reshape(-1),
    }
    got, _, _ = plane_exchange(pieces, rim * second, None)
    top = jnp.concatenate(
        [got[(-1, -1)].reshape(rim, rim), got[(-1, 0)].reshape(rim, second), got[(-1, 1)].reshape(rim, rim)], 1
    )
    middle = jnp.concatenate(
        [got[(0, -1)].reshape(first, rim), plane, got[(0, 1)].reshape(first, rim)], 1
    )
    bottom = jnp.concatenate(
        [got[(1, -1)].reshape(rim, rim), got[(1, 0)].reshape(rim, second), got[(1, 1)].reshape(rim, rim)], 1
    )
    return jnp.concatenate([top, middle, bottom], 0)


def line_factors(length, block_id, block_count):
    position = jnp.arange(length)
    at_start = (position == 0) & (block_id == 0)
    at_end = (position == length - 1) & (block_id == block_count - 1)
    mass_line = jnp.where(position % 3 == 0, jnp.where(at_start | at_end, 0.125, 0.25), 0.375)
    shared = (position == 0) & (block_id > 0) | (position == length - 1) & (
        block_id < block_count - 1
    )
    weight = jnp.where(shared, 0.5, 1.0)
    return (mass_line.astype(jnp.float32), weight.astype(jnp.float32))


def factor_grid(depth_line, first_line, second_line):
    return depth_line[:, None, None] * first_line[None, :, None] * second_line[None, None, :]


def node_table(matrix, labels, kind_count):
    out = matrix[kind_count - 1][:, None]
    for kind in range(kind_count - 2, -1, -1):
        out = jnp.where(labels == kind, matrix[kind][:, None], out)
    return out


def ext_index(target, anchor, length_local, rim_width):
    relative = target - anchor
    return jnp.where(
        relative < 0,
        rim_width - 1 + relative,
        jnp.where(relative > length_local - 1, rim_width + relative + 1, rim_width + relative),
    )


def per_device(
    potential,
    gating,
    cell_type,
    drug_class,
    half_point,
    gate_slope,
    time_const,
    max_conduct,
    reversal,
    drug_block,
    heart_cond,
    torso_cond,
    epi_target,
):
    depth_len, first_len, second_len = potential.shape
    torso_len = 3 * torso_cond.shape[0] + 1
    index_torso = lax.axis_index("torso")
    index_first = lax.axis_index("hx")
    index_second = lax.axis_index("hy")
    heart_depth, unused_depth = line_factors(depth_len, index_torso, lax.axis_size("torso"))
    first_mass, first_weight = line_factors(first_len, index_first, lax.axis_size("hx"))
    second_mass, second_weight = line_factors(second_len, index_second, lax.axis_size("hy"))
    torso_depth, torso_depth_weight = line_factors(torso_len, index_torso, lax.axis_size("torso"))
    heart_mass = factor_grid(heart_depth, first_mass, second_mass)
    torso_mass = factor_grid(torso_depth, first_mass, second_mass)
    torso_weight = factor_grid(torso_depth_weight, first_weight, second_weight)
    type_flat = cell_type.reshape(1, -1)
    class_flat = drug_class.reshape(1, -1)
    half_nodes = node_table(half_point, type_flat, TYPES)
    slope_nodes = node_table(gate_slope, type_flat, TYPES)
    decay_nodes = node_table(jnp.exp(-time_step / time_const), type_flat, TYPES)
    cond_nodes = node_table(max_conduct, type_flat, TYPES) * node_table(
        drug_block, class_flat, CLASSES
    )
    gate_flat = gating.reshape(gating.shape[0], -1)
    mats = element_matrices(first_len, second_len)
    for repeat in range(STEPS):
        diffusion, _, tied = face_sums(local_products(potential, heart_cond, mats), tie=potential)
        volts = tied.reshape(1, -1)
        inf_value = jax.nn.sigmoid((volts - half_nodes) * slope_nodes)
        gate_flat = inf_value + (gate_flat - inf_value) * decay_nodes
        current = jnp.sum(cond_nodes * gate_flat * (volts - reversal[:, None]), 0)
        potential = potential - time_step * (
            diffusion / heart_mass + current.reshape(potential.shape)
        )
    new_gating = gate_flat.reshape(gating.shape)

    rim_width = REACH + 1
    extended = rim_plane(potential[0], rim_width)
    distinct_second = lax.axis_size("hy") * (second_len - 1) + 1
    target_first = epi_target // distinct_second
    target_second = epi_target % distinct_second
    place_first = ext_index(target_first, index_first * (first_len - 1), first_len, rim_width)
    place_second = ext_index(target_second, index_second * (second_len - 1), second_len, rim_width)
    shift_first = place_first - rim_width - jnp.arange(first_len)[:, None]
    shift_second = place_second - rim_width - jnp.arange(second_len)[None, :]
    picked_values = jnp.zeros((first_len, second_len), jnp.float32)
    for step_first in range(-rim_width, rim_width + 1):
        rows = extended[rim_width + step_first : rim_width + step_first + first_len]
        along = jnp.zeros((first_len, second_len), jnp.float32)
        for step_second in range(-rim_width, rim_width + 1):
            window = rows[:, rim_width + step_second : rim_width + step_second + second_len]
            along = jnp.where(shift_second == step_second, window, along)
        picked_values = jnp.where(shift_first == step_first, along, picked_values)
    plane = jnp.where(index_torso == 0, picked_values, 0.0)
    rhs = jnp.concatenate(
        [plane[None], jnp.zeros((torso_len - 1, first_len, second_len), jnp.float32)], 0
    )

    mass_shift = torso_shift * torso_mass
    weighted_mass = torso_weight * mass_shift
    zero_lanes = 0.0 * torso_weight[0, 0]

    def exchange(residual, extra):
        local = local_products(residual, torso_cond, mats, merged=True)
        terms = [
            torso_weight * residual * residual,
            residual * local + weighted_mass * residual * residual,
        ] + extra(local)
        partial = jnp.sum(jnp.sum(jnp.stack(terms), axis=(1, 2)), axis=1)
        summed, sums = face_sums(local, partial)
        return summed + mass_shift * residual, sums[:, None] + zero_lanes[None, :]

    image, sums = exchange(rhs, lambda local: [])
    norm_now = sums[0]
    curvature = sums[1]
    step_size = norm_now / curvature
    solution = step_size * rhs
    direction = rhs
    residual = rhs - step_size * image

    def later_turn(turn_index, state_tuple):
        solution, residual, direction, image, norm_now, curvature = state_tuple
        s_image, sums = exchange(
            residual,
            lambda local: [
                torso_weight * residual * image,
                direction * local + weighted_mass * direction * residual,
            ],
        )
        norm_next = sums[0]
        ratio = norm_next / norm_now
        curvature = sums[1] + ratio * (sums[2] + sums[3]) + ratio * ratio * curvature
        direction = residual + ratio * direction
        image = s_image + ratio * image
        step_size = norm_next / curvature
        solution = solution + step_size * direction
        residual = residual - step_size * image
        return (solution, residual, direction, image, norm_next, curvature)

    state = (solution, residual, direction, image, norm_now, curvature)
    solution = lax.fori_loop(1, ITERS, later_turn, state)[0]
    return (potential, new_gating, solution)


def solution(mesh):
    placed = (
        P("torso", "hx", "hy"),
        P(None, "torso", "hx", "hy"),
        P("torso", "hx", "hy"),
        P("torso", "hx", "hy"),
        P(),
        P(),
        P(),
        P(),
        P(),
        P(),
        P("torso", "hx", "hy"),
        P("torso", "hx", "hy"),
        P("hx", "hy"),
    )
    return jax.shard_map(
        per_device,
        mesh=mesh,
        in_specs=placed,
        out_specs=(P("torso", "hx", "hy"), P(None, "torso", "hx", "hy"), P("torso", "hx", "hy")),
        check_vma=False,
    )
```

```python
import jax
import jax.numpy as jnp
import numpy as np
from jax import lax
from jax.sharding import PartitionSpec as P

TYPES = 3
CLASSES = 4
STEPS = 2
ITERS = 4
REACH = 2


STIFF_LINE = (
    np.array(
        [
            [148.0, -189.0, 54.0, -13.0],
            [-189.0, 432.0, -297.0, 54.0],
            [54.0, -297.0, 432.0, -189.0],
            [-13.0, 54.0, -189.0, 148.0],
        ]
    )
    / 40.0
)
MASS_LINE = (
    np.array(
        [
            [128.0, 99.0, -36.0, 19.0],
            [99.0, 648.0, -81.0, -36.0],
            [-36.0, -81.0, 648.0, 99.0],
            [19.0, -36.0, 99.0, 128.0],
        ]
    )
    / 1680.0
)
time_step = 0.002
torso_shift = 0.02
HIGH = lax.Precision.HIGHEST


def gather_matrix(length, line):
    elements = (length - 1) // 3
    shape = (length, 4, elements)
    node = lax.broadcasted_iota(jnp.int32, shape, 0)
    offset = lax.broadcasted_iota(jnp.int32, shape, 1)
    local = node - 3 * lax.broadcasted_iota(jnp.int32, shape, 2)
    out = jnp.zeros(shape, jnp.float32)
    for a in range(4):
        for j in range(4):
            if line[a, j] != 0.0:
                out = jnp.where((offset == a) & (local == j), jnp.float32(line[a, j]), out)
    return out.reshape(length, 4 * elements)


def element_matrices(first, second):
    return dict(
        pick_mass=gather_matrix(first, MASS_LINE).T,
        pick_stiff=gather_matrix(first, STIFF_LINE).T,
        lanes_k=gather_matrix(second, STIFF_LINE),
        lanes_m=gather_matrix(second, MASS_LINE),
        lanes=jnp.stack([gather_matrix(second, STIFF_LINE), gather_matrix(second, MASS_LINE)]).reshape(
            2 * second, -1
        ),
        scatter_second=gather_matrix(second, np.eye(4)).T,
        scatter_first=gather_matrix(first, np.eye(4)),
    )


def local_products(values, conduct, mats, merged=False):
    depth, first, second = values.shape
    first_el, second_el = conduct.shape[1], conduct.shape[2]
    mass_d = [[float(MASS_LINE[i, j]) for j in range(4)] for i in range(4)]
    stiff_d = [[float(STIFF_LINE[i, j]) for j in range(4)] for i in range(4)]
    rows = [values[j] for j in range(depth)]
    v_mass = jnp.stack([sum(mass_d[i][j] * rows[j] for j in range(4)) for i in range(4)])
    v_stiff = jnp.stack([sum(stiff_d[i][j] * rows[j] for j in range(4)) for i in range(4)])
    pick_mass = mats["pick_mass"]
    pick_stiff = mats["pick_stiff"]
    along_first_m = jnp.einsum("kx,dxy->dky", pick_mass, v_mass, precision=HIGH)
    along_first_k = jnp.einsum("kx,dxy->dky", pick_stiff, v_mass, precision=HIGH) + jnp.einsum(
        "kx,dxy->dky", pick_mass, v_stiff, precision=HIGH
    )
    flat_m = along_first_m.reshape(-1, second)
    flat_k = along_first_k.reshape(-1, second)
    if merged:
        element = jnp.dot(jnp.concatenate([flat_m, flat_k], 1), mats["lanes"], precision=HIGH)
    else:
        element = jnp.dot(flat_m, mats["lanes_k"], precision=HIGH) + jnp.dot(
            flat_k, mats["lanes_m"], precision=HIGH
        )
    element = element.reshape(depth, 4, first_el, 4, second_el) * conduct.reshape(
        1, 1, first_el, 1, second_el
    )
    scatter_second = mats["scatter_second"]
    spread = jnp.dot(element.reshape(-1, 4 * second_el), scatter_second, precision=HIGH)
    spread = spread.reshape(depth, 4 * first_el, second)
    scatter_first = mats["scatter_first"]
    return jnp.einsum("xk,dky->dxy", scatter_first, spread, precision=HIGH)


def torso_stage(values, scalars):
    count = lax.axis_size("torso")
    if count == 1:
        return values, scalars
    if count != 2:
        raise NotImplementedError("torso size")
    me = lax.axis_index("torso")
    face = jnp.where(me == 0, values[-1], values[0])
    extra = None
    if scalars is not None:
        extra = jnp.pad(scalars, (0, values.shape[2] - scalars.shape[0]))[None, :]
        face = jnp.concatenate([face, extra], 0)
    got = lax.ppermute(face, "torso", [(0, 1), (1, 0)])
    rows = values.shape[1]
    got_face = got[:rows]
    values = values.at[-1].add(jnp.where(me == 0, got_face, 0.0))
    values = values.at[0].add(jnp.where(me == 1, got_face, 0.0))
    if scalars is not None:
        scalars = scalars + got[rows, : scalars.shape[0]]
    return values, scalars


def plane_exchange(pieces, width, scalars, tie=None):
    count_x, count_y = lax.axis_size("hx"), lax.axis_size("hy")
    me_x, me_y = lax.axis_index("hx"), lax.axis_index("hy")
    rows = []
    for code in range(9):
        offset = (code // 3 - 1, code % 3 - 1)
        piece = pieces.get(offset)
        row = jnp.zeros((width,), jnp.float32) if piece is None else jnp.pad(piece, (0, width - piece.shape[0]))
        if scalars is not None:
            row = jnp.concatenate([row, scalars])
        rows.append(row)
    table = jnp.stack(rows)
    peers = jnp.arange(count_x * count_y, dtype=jnp.int32)
    off_x = peers // count_y - me_x
    off_y = peers % count_y - me_y
    near = (jnp.abs(off_x) <= 1) & (jnp.abs(off_y) <= 1)
    code_of = jnp.where(near, (off_x + 1) * 3 + (off_y + 1), 4)
    send = jnp.broadcast_to(table[4][None, :], (count_x * count_y, table.shape[1]))
    for code in range(9):
        if code != 4:
            send = jnp.where(code_of[:, None] == code, table[code][None, :], send)
    if tie is not None:
        send, tie = lax.optimization_barrier((send, tie))
    got = lax.all_to_all(send, ("hx", "hy"), 0, 0, tiled=True)
    received = {}
    for offset in pieces:
        src_x, src_y = me_x + offset[0], me_y + offset[1]
        valid = (src_x >= 0) & (src_x < count_x) & (src_y >= 0) & (src_y < count_y)
        src = jnp.clip(src_x, 0, count_x - 1) * count_y + jnp.clip(src_y, 0, count_y - 1)
        row = lax.dynamic_index_in_dim(got, src, 0, keepdims=False)
        received[offset] = jnp.where(valid, row[: pieces[offset].shape[0]], 0.0)
    total = None
    if scalars is not None:
        total = jnp.sum(got[:, width:], axis=0)
    return received, total, tie


def face_sums(values, scalars=None, tie=None):
    values, scalars = torso_stage(values, scalars)
    depth, first, second = values.shape
    pieces = {
        (1, 0): values[:, -1, :].reshape(-1),
        (-1, 0): values[:, 0, :].reshape(-1),
        (0, 1): values[:, :, -1].reshape(-1),
        (0, -1): values[:, :, 0].reshape(-1),
        (1, 1): values[:, -1, -1],
        (1, -1): values[:, -1, 0],
        (-1, 1): values[:, 0, -1],
        (-1, -1): values[:, 0, 0],
    }
    got, total, tie = plane_exchange(pieces, depth * second, scalars, tie)
    at_low = ((0, 0), (0, first - 1))
    at_high = ((0, 0), (first - 1, 0))
    low_second = got[(0, -1)].reshape(depth, first)
    low_second = low_second + jnp.pad(got[(-1, -1)][:, None], at_low)
    low_second = low_second + jnp.pad(got[(1, -1)][:, None], at_high)
    high_second = got[(0, 1)].reshape(depth, first)
    high_second = high_second + jnp.pad(got[(-1, 1)][:, None], at_low)
    high_second = high_second + jnp.pad(got[(1, 1)][:, None], at_high)
    along_first = jnp.pad(got[(-1, 0)].reshape(depth, 1, second), ((0, 0), (0, first - 1), (0, 0)))
    along_first = along_first + jnp.pad(
        got[(1, 0)].reshape(depth, 1, second), ((0, 0), (first - 1, 0), (0, 0))
    )
    along_second = jnp.pad(low_second[:, :, None], ((0, 0), (0, 0), (0, second - 1)))
    along_second = along_second + jnp.pad(
        high_second[:, :, None], ((0, 0), (0, 0), (second - 1, 0))
    )
    summed = values + along_first + along_second
    if tie is None:
        return summed, total
    return summed, total, tie


def rim_plane(plane, rim):
    first, second = plane.shape
    pieces = {
        (1, 0): plane[-rim:, :].reshape(-1),
        (-1, 0): plane[:rim, :].reshape(-1),
        (0, 1): plane[:, -rim:].reshape(-1),
        (0, -1): plane[:, :rim].reshape(-1),
        (1, 1): plane[-rim:, -rim:].reshape(-1),
        (1, -1): plane[-rim:, :rim].reshape(-1),
        (-1, 1): plane[:rim, -rim:].reshape(-1),
        (-1, -1): plane[:rim, :rim].reshape(-1),
    }
    got, _, _ = plane_exchange(pieces, rim * second, None)
    top = jnp.concatenate(
        [got[(-1, -1)].reshape(rim, rim), got[(-1, 0)].reshape(rim, second), got[(-1, 1)].reshape(rim, rim)], 1
    )
    middle = jnp.concatenate(
        [got[(0, -1)].reshape(first, rim), plane, got[(0, 1)].reshape(first, rim)], 1
    )
    bottom = jnp.concatenate(
        [got[(1, -1)].reshape(rim, rim), got[(1, 0)].reshape(rim, second), got[(1, 1)].reshape(rim, rim)], 1
    )
    return jnp.concatenate([top, middle, bottom], 0)


def line_factors(length, block_id, block_count):
    position = jnp.arange(length)
    at_start = (position == 0) & (block_id == 0)
    at_end = (position == length - 1) & (block_id == block_count - 1)
    mass_line = jnp.where(position % 3 == 0, jnp.where(at_start | at_end, 0.125, 0.25), 0.375)
    shared = (position == 0) & (block_id > 0) | (position == length - 1) & (
        block_id < block_count - 1
    )
    weight = jnp.where(shared, 0.5, 1.0)
    return (mass_line.astype(jnp.float32), weight.astype(jnp.float32))


def factor_grid(depth_line, first_line, second_line):
    return depth_line[:, None, None] * first_line[None, :, None] * second_line[None, None, :]


def node_table(matrix, labels, kind_count):
    out = matrix[kind_count - 1][:, None]
    for kind in range(kind_count - 2, -1, -1):
        out = jnp.where(labels == kind, matrix[kind][:, None], out)
    return out


def ext_index(target, anchor, length_local, rim_width):
    relative = target - anchor
    return jnp.where(
        relative < 0,
        rim_width - 1 + relative,
        jnp.where(relative > length_local - 1, rim_width + relative + 1, rim_width + relative),
    )


def per_device(
    potential,
    gating,
    cell_type,
    drug_class,
    half_point,
    gate_slope,
    time_const,
    max_conduct,
    reversal,
    drug_block,
    heart_cond,
    torso_cond,
    epi_target,
):
    depth_len, first_len, second_len = potential.shape
    torso_len = 3 * torso_cond.shape[0] + 1
    index_torso = lax.axis_index("torso")
    index_first = lax.axis_index("hx")
    index_second = lax.axis_index("hy")
    heart_depth, unused_depth = line_factors(depth_len, index_torso, lax.axis_size("torso"))
    first_mass, first_weight = line_factors(first_len, index_first, lax.axis_size("hx"))
    second_mass, second_weight = line_factors(second_len, index_second, lax.axis_size("hy"))
    torso_depth, torso_depth_weight = line_factors(torso_len, index_torso, lax.axis_size("torso"))
    heart_mass = factor_grid(heart_depth, first_mass, second_mass)
    torso_mass = factor_grid(torso_depth, first_mass, second_mass)
    torso_weight = factor_grid(torso_depth_weight, first_weight, second_weight)
    type_flat = cell_type.reshape(1, -1)
    class_flat = drug_class.reshape(1, -1)
    half_nodes = node_table(half_point, type_flat, TYPES)
    slope_nodes = node_table(gate_slope, type_flat, TYPES)
    decay_nodes = node_table(jnp.exp(-time_step / time_const), type_flat, TYPES)
    cond_nodes = node_table(max_conduct, type_flat, TYPES) * node_table(
        drug_block, class_flat, CLASSES
    )
    gate_flat = gating.reshape(gating.shape[0], -1)
    mats = element_matrices(first_len, second_len)
    for repeat in range(STEPS):
        diffusion, _, tied = face_sums(local_products(potential, heart_cond, mats, merged=True), tie=potential)
        volts = tied.reshape(1, -1)
        inf_value = jax.nn.sigmoid((volts - half_nodes) * slope_nodes)
        gate_flat = inf_value + (gate_flat - inf_value) * decay_nodes
        current = jnp.sum(cond_nodes * gate_flat * (volts - reversal[:, None]), 0)
        potential = potential - time_step * (
            diffusion / heart_mass + current.reshape(potential.shape)
        )
    new_gating = gate_flat.reshape(gating.shape)

    rim_width = REACH + 1
    extended = rim_plane(potential[0], rim_width)
    distinct_second = lax.axis_size("hy") * (second_len - 1) + 1
    target_first = epi_target // distinct_second
    target_second = epi_target % distinct_second
    place_first = ext_index(target_first, index_first * (first_len - 1), first_len, rim_width)
    place_second = ext_index(target_second, index_second * (second_len - 1), second_len, rim_width)
    shift_first = place_first - rim_width - jnp.arange(first_len)[:, None]
    shift_second = place_second - rim_width - jnp.arange(second_len)[None, :]
    picked_values = jnp.zeros((first_len, second_len), jnp.float32)
    for step_first in range(-rim_width, rim_width + 1):
        rows = extended[rim_width + step_first : rim_width + step_first + first_len]
        along = jnp.zeros((first_len, second_len), jnp.float32)
        for step_second in range(-rim_width, rim_width + 1):
            window = rows[:, rim_width + step_second : rim_width + step_second + second_len]
            along = jnp.where(shift_second == step_second, window, along)
        picked_values = jnp.where(shift_first == step_first, along, picked_values)
    plane = jnp.where(index_torso == 0, picked_values, 0.0)
    rhs = jnp.concatenate(
        [plane[None], jnp.zeros((torso_len - 1, first_len, second_len), jnp.float32)], 0
    )

    mass_shift = torso_shift * torso_mass
    weighted_mass = torso_weight * mass_shift
    zero_lanes = 0.0 * torso_weight[0, 0]

    def exchange(residual, extra):
        local = local_products(residual, torso_cond, mats, merged=True)
        terms = [
            torso_weight * residual * residual,
            residual * local + weighted_mass * residual * residual,
        ] + extra(local)
        partial = jnp.sum(jnp.sum(jnp.stack(terms), axis=(1, 2)), axis=1)
        summed, sums = face_sums(local, partial)
        return summed + mass_shift * residual, sums[:, None] + zero_lanes[None, :]

    image, sums = exchange(rhs, lambda local: [])
    norm_now = sums[0]
    curvature = sums[1]
    step_size = norm_now / curvature
    solution = step_size * rhs
    direction = rhs
    residual = rhs - step_size * image

    def later_turn(turn_index, state_tuple):
        solution, residual, direction, image, norm_now, curvature = state_tuple
        s_image, sums = exchange(
            residual,
            lambda local: [
                torso_weight * residual * image,
                direction * local + weighted_mass * direction * residual,
            ],
        )
        norm_next = sums[0]
        ratio = norm_next / norm_now
        curvature = sums[1] + ratio * (sums[2] + sums[3]) + ratio * ratio * curvature
        direction = residual + ratio * direction
        image = s_image + ratio * image
        step_size = norm_next / curvature
        solution = solution + step_size * direction
        residual = residual - step_size * image
        return (solution, residual, direction, image, norm_next, curvature)

    state = (solution, residual, direction, image, norm_now, curvature)
    solution = lax.fori_loop(1, ITERS, later_turn, state)[0]
    return (potential, new_gating, solution)


def solution(mesh):
    placed = (
        P("torso", "hx", "hy"),
        P(None, "torso", "hx", "hy"),
        P("torso", "hx", "hy"),
        P("torso", "hx", "hy"),
        P(),
        P(),
        P(),
        P(),
        P(),
        P(),
        P("torso", "hx", "hy"),
        P("torso", "hx", "hy"),
        P("hx", "hy"),
    )
    return jax.shard_map(
        per_device,
        mesh=mesh,
        in_specs=placed,
        out_specs=(P("torso", "hx", "hy"), P(None, "torso", "hx", "hy"), P("torso", "hx", "hy")),
        check_vma=False,
    )
```
